32 devices in a mesh: space: 4 (over y, x), chan: 8 (over z, core).
Axes of the slice: x: 2, y: 2, z: 4, core: 2. Of those that a mesh axis runs over, the one named last changes fastest.
Arguments:
- inputs: bfloat16 [256, 16, 1024], P('chan', 'space'), may hold values from -6 to 6
- weight: bfloat16 [27, 256, 256], P(None, None, 'chan'), may hold values from -0.078125 to 0.078125
- bias_term: float32 [256], P('chan'), may hold values from -1 to 1
- output_grad: bfloat16 [256, 16, 1024], P('chan', 'space'), may hold values from -6 to 6
Outputs:
- outputs: bfloat16 [256, 16, 1024], P('chan', 'space')
- input_grad: bfloat16 [256, 16, 1024], P('chan', 'space')
- weight_grad: float32 [27, 256, 256], P(None, None, 'chan')
- bias_grad: float32 [256], P('chan')
The draws below stay inside these ranges and needn't reach their ends.
All inputs are finite; a program needn't handle non-finite values.
Results may differ from the reference program's by a relative error of at most 0.001.
Values may be sent and summed in bfloat16 or wider, within the bound.
No kernel may reach another device: no remote copies, remote signals or barrier semaphores. Data moves between devices by JAX's collectives and lax.ppermute only.
A program may use at most 128 MiB of HBM per device.

```python
import math
import jax
import jax.numpy as jnp
from jax import lax

CIN = 256
COUT = 256
TAPS = 27
H = 16
W = 64
NZ = 16
CELLS = 16384


def level_of(rng, shape, shards, smallest, high):
    loudness = 1.0
    for dim, parts in shards:
        draws = jax.random.uniform(jax.random.fold_in(jax.random.fold_in(rng, 6), dim), (parts,), jnp.float32, smallest / len(shards), high / len(shards))
        loudness = loudness * jnp.repeat(jnp.exp(draws), shape[dim] // parts).reshape((-1,) + (1,) * (len(shape) - 1 - dim))
    return loudness


def noise(key, extent, width, most, split=(), kind=jnp.bfloat16):
    gain = level_of(key, extent, split, -0.22, 0.18) if split else 1.0
    values = jax.random.normal(key, extent, jnp.float32) * width * gain
    return jnp.minimum(jnp.maximum(values, -most), most).astype(kind)


def setup_inputs(seed: int = 0) -> dict:
    key_list = jax.random.split(jax.random.key(seed), 5)
    inputs = noise(key_list[0], (CIN, NZ, H * W), 1.0, 6.0, ((0, 8), (1, 4)))
    weight = noise(key_list[1], (TAPS, CIN, COUT), (TAPS * CIN) ** -0.5, 0.078125, ((2, 8),))
    bias_term = jnp.clip(jax.random.uniform(key_list[2], (COUT,), jnp.float32, -1.0, 1.0) * level_of(key_list[2], (COUT,), ((0, 8),), -0.4, 0.0), -1.0, 1.0)
    output_grad = noise(key_list[3], (COUT, NZ, H * W), 1.0, 6.0, ((0, 8), (1, 4)))
    return {"inputs": inputs, "weight": weight, "bias_term": bias_term, "output_grad": output_grad}


tap_offsets = tuple(((depth_step, row_step, column_step) for depth_step in (-1, 0, 1) for row_step in (-1, 0, 1) for column_step in (-1, 0, 1)))

def shift_cells(field, row_step, column_step):
    length_flat = field.shape[-1]
    pad_width = W + 1
    widths = [(0, 0)] * (field.ndim - 1) + [(pad_width, pad_width)]
    padded = jnp.pad(field, widths)
    first_index = pad_width + row_step * W + column_step
    shifted = lax.slice_in_dim(padded, first_index, first_index + length_flat, axis=field.ndim - 1)
    column = jnp.arange(length_flat, dtype=jnp.int32) % W
    inside = (column + column_step >= 0) & (column + column_step < W)
    return jnp.where(inside, shifted, jnp.zeros_like(shifted))

def reference(inputs, weight, bias_term, output_grad):
    grad_scale = 1.0 / math.sqrt(CELLS)
    flat_cells = NZ * H * W
    in_padded = jnp.pad(inputs, ((0, 0), (1, 1), (0, 0)))
    grad_padded = jnp.pad(output_grad, ((0, 0), (1, 1), (0, 0)))
    grad_flat = output_grad.reshape(COUT, flat_cells)
    forward = jnp.zeros((COUT, flat_cells), jnp.float32)
    backward = jnp.zeros((CIN, flat_cells), jnp.float32)
    gradients = []
    for tap_index, (depth_step, row_step, column_step) in enumerate(tap_offsets):
        source = shift_cells(in_padded[:, 1 + depth_step:1 + depth_step + NZ, :], row_step, column_step).reshape(CIN, flat_cells)
        forward = forward + jnp.dot(weight[tap_index].T, source, preferred_element_type=jnp.float32)
        grad_source = shift_cells(grad_padded[:, 1 - depth_step:1 - depth_step + NZ, :], -row_step, -column_step).reshape(COUT, flat_cells)
        backward = backward + jnp.dot(weight[tap_index], grad_source, preferred_element_type=jnp.float32)
        gradients.append(lax.dot_general(source, grad_flat, (((1,), (1,)), ((), ())), preferred_element_type=jnp.float32))
    outputs = (forward + bias_term.astype(jnp.float32)[:, None]).astype(jnp.bfloat16).reshape(COUT, NZ, H * W)
    input_grad = backward.astype(jnp.bfloat16).reshape(CIN, NZ, H * W)
    weight_grad = jnp.stack(gradients) * grad_scale
    bias_grad = lax.optimization_barrier(jnp.sum(output_grad.astype(jnp.float32), axis=(1, 2))) * grad_scale
    return (outputs, input_grad, weight_grad, bias_grad)
```

```python
import math

import jax
import jax.numpy as jnp
from jax import lax
from jax.sharding import PartitionSpec as P

W = 64


def padded_2(array, sides, width):
    for axis, dim in sides:
        devices, length = (lax.axis_size(axis), array.shape[dim])
        up = [(i, (i + 1) % devices) for i in range(devices - 1)]
        down = [(j, i) for i, j in up]
        last = lax.slice_in_dim(array, length - width, length, axis=dim)
        first = lax.slice_in_dim(array, 0, width, axis=dim)
        before = lax.ppermute(last, axis, up)
        after = lax.ppermute(first, axis, down)
        array = jnp.concatenate([before, array, after], axis=dim)
    return array


def outer_planes(field):
    return jnp.concatenate([field[:, :1], field[:, -1:]], axis=1)


def attach_rims(field, rims):
    return jnp.concatenate([rims[:, :1], field, rims[:, 3:]], axis=1)


def volume(field):
    return field.reshape(1, field.shape[0], field.shape[1], field.shape[2] // W, W)


def body(inputs, weight, bias_term, output_grad):
    taps_total = weight.shape[0]
    channels_in = weight.shape[1]
    block_out = weight.shape[2]
    block_in = inputs.shape[0]
    depth_cells = inputs.shape[1]
    plane_cells = inputs.shape[2]
    rows = plane_cells // W
    grad_scale = 1.0 / math.sqrt(lax.axis_size("space") * depth_cells * plane_cells)
    own_rims = padded_2(outer_planes(inputs), (("space", 1),), 1)
    rimmed = attach_rims(inputs, own_rims)
    gathered = lax.all_gather(rimmed, "chan", axis=0, tiled=True)
    kernel = weight.reshape(3, 3, 3, channels_in, block_out)
    in_vol = volume(gathered)
    forward = lax.conv_general_dilated(
        in_vol,
        kernel,
        window_strides=(1, 1, 1),
        padding=((0, 0), (1, 1), (1, 1)),
        dimension_numbers=("NCDHW", "DHWIO", "NCDHW"),
        preferred_element_type=jnp.float32,
    )
    forward = forward.reshape(block_out, depth_cells, plane_cells)
    outputs = (forward + bias_term[:, None, None]).astype(jnp.bfloat16)

    grad_vol = volume(output_grad)
    filter_grad = lax.conv_general_dilated(
        in_vol.reshape(channels_in, 1, depth_cells + 2, rows, W),
        grad_vol.reshape(1, block_out, depth_cells, rows, W),
        window_strides=(1, 1, 1),
        padding=((0, 0), (1, 1), (1, 1)),
        dimension_numbers=("NCDHW", "IODHW", "NCDHW"),
        preferred_element_type=jnp.float32,
    )
    weight_part = jnp.transpose(filter_grad, (2, 3, 4, 0, 1)).reshape(taps_total * channels_in * block_out)
    bias_part = jnp.sum(output_grad.astype(jnp.float32), axis=(1, 2))
    reduced = lax.psum(jnp.concatenate([weight_part, bias_part]) * grad_scale, "space")
    weight_grad = reduced[: taps_total * channels_in * block_out].reshape(taps_total, channels_in, block_out)
    bias_grad = reduced[taps_total * channels_in * block_out :]

    grad_rimmed = padded_2(output_grad, (("space", 1),), 1)
    flipped = kernel[::-1, ::-1, ::-1]
    spread = lax.conv_general_dilated(
        volume(grad_rimmed),
        flipped,
        window_strides=(1, 1, 1),
        padding=((0, 0), (1, 1), (1, 1)),
        dimension_numbers=("NCDHW", "DHWOI", "NCDHW"),
        preferred_element_type=jnp.float32,
    )
    summed = lax.psum_scatter(
        spread.reshape(channels_in, depth_cells * plane_cells),
        "chan",
        scatter_dimension=0,
        tiled=True,
    )
    input_grad = summed.astype(jnp.bfloat16).reshape(block_in, depth_cells, plane_cells)
    return (outputs, input_grad, weight_grad, bias_grad)


def solution(mesh):
    placed = (P("chan", "space", None), P(None, None, "chan"), P("chan"), P("chan", "space", None))
    return jax.shard_map(
        body,
        mesh=mesh,
        in_specs=placed,
        out_specs=(
            P("chan", "space", None),
            P("chan", "space", None),
            P(None, None, "chan"),
            P("chan"),
        ),
        check_vma=False,
    )
```

```python
import math

import jax
import jax.numpy as jnp
from jax import lax
from jax.sharding import PartitionSpec as P

W = 64


tap_offsets = tuple(
    (
        (depth_step, row_step, column_step)
        for depth_step in (-1, 0, 1)
        for row_step in (-1, 0, 1)
        for column_step in (-1, 0, 1)
    )
)


def padded_2(array, sides, width):
    for axis, dim in sides:
        devices, length = (lax.axis_size(axis), array.shape[dim])
        up = [(i, (i + 1) % devices) for i in range(devices - 1)]
        down = [(j, i) for i, j in up]
        last = lax.slice_in_dim(array, length - width, length, axis=dim)
        first = lax.slice_in_dim(array, 0, width, axis=dim)
        before = lax.ppermute(last, axis, up)
        after = lax.ppermute(first, axis, down)
        array = jnp.concatenate([before, array, after], axis=dim)
    return array


def shift_cells(field, row_step, column_step):
    length_flat = field.shape[-1]
    pad_width = W + 1
    widths = [(0, 0)] * (field.ndim - 1) + [(pad_width, pad_width)]
    padded = jnp.pad(field, widths)
    first_index = pad_width + row_step * W + column_step
    shifted = lax.slice_in_dim(padded, first_index, first_index + length_flat, axis=field.ndim - 1)
    column = jnp.arange(length_flat, dtype=jnp.int32) % W
    inside = (column + column_step >= 0) & (column + column_step < W)
    return jnp.where(inside, shifted, jnp.zeros_like(shifted))


def outer_planes(field):
    return jnp.concatenate([field[:, :1], field[:, -1:]], axis=1)


def attach_rims(field, rims):
    return jnp.concatenate([rims[:, :1], field, rims[:, 3:]], axis=1)


def all_reduce_pairs(flat, axis):
    devices = lax.axis_size(axis)
    steps = devices.bit_length() - 1
    assert 1 << steps == devices
    length = flat.shape[0]
    padded_length = -(-length // devices) * devices
    current = jnp.pad(flat, (0, padded_length - length))
    index = lax.axis_index(axis)
    for step in range(steps):
        half = current.shape[0] // 2
        bit = (index >> step) & 1
        keep = lax.dynamic_slice_in_dim(current, bit * half, half)
        send = lax.dynamic_slice_in_dim(current, (1 - bit) * half, half)
        pairs = [(i, i ^ (1 << step)) for i in range(devices)]
        current = keep + lax.ppermute(send, axis, pairs)
    for step in reversed(range(steps)):
        half = current.shape[0]
        bit = (index >> step) & 1
        pairs = [(i, i ^ (1 << step)) for i in range(devices)]
        other = lax.ppermute(current, axis, pairs)
        both = jnp.zeros((2 * half,), current.dtype)
        both = lax.dynamic_update_slice_in_dim(both, current, bit * half, 0)
        current = lax.dynamic_update_slice_in_dim(both, other, (1 - bit) * half, 0)
    return current[:length]


def body(inputs, weight, bias_term, output_grad):
    taps_total = weight.shape[0]
    channels_in = weight.shape[1]
    block_out = weight.shape[2]
    block_in = inputs.shape[0]
    depth_cells = inputs.shape[1]
    plane_cells = inputs.shape[2]
    grad_scale = 1.0 / math.sqrt(lax.axis_size("space") * depth_cells * plane_cells)
    own_rims = padded_2(outer_planes(inputs), (("space", 1),), 1)
    rimmed = attach_rims(inputs, own_rims)
    gathered = lax.all_gather(rimmed, "chan", axis=0, tiled=True)
    gathered_flat = gathered.reshape(channels_in, (depth_cells + 2) * plane_cells)
    forward_weight = jnp.transpose(weight, (0, 2, 1)).reshape(taps_total * block_out, channels_in)
    stacked = jnp.dot(forward_weight, gathered_flat, preferred_element_type=jnp.float32)
    stacked = stacked.reshape(taps_total, block_out, depth_cells + 2, plane_cells)
    forward = jnp.zeros((block_out, depth_cells, plane_cells), jnp.float32)
    for tap_index, (depth_step, row_step, column_step) in enumerate(tap_offsets):
        forward = forward + shift_cells(
            stacked[tap_index, :, 1 + depth_step : 1 + depth_step + depth_cells],
            row_step,
            column_step,
        )
    outputs = (forward + bias_term[:, None, None]).astype(jnp.bfloat16)
    grad_rimmed = padded_2(output_grad, (("space", 1),), 1)
    grad_wide = jnp.pad(output_grad, ((0, 0), (2, 2), (0, 0)))
    placed = jnp.stack(
        [
            shift_cells(
                grad_wide[:, 1 - depth_step : 1 - depth_step + depth_cells + 2],
                -row_step,
                -column_step,
            )
            for depth_step, row_step, column_step in tap_offsets
        ]
    )
    placed = placed.reshape(taps_total * block_out, (depth_cells + 2) * plane_cells)
    weight_part = lax.dot_general(
        gathered_flat, placed, (((1,), (1,)), ((), ())), preferred_element_type=jnp.float32
    )
    weight_part = (
        jnp.transpose(weight_part.reshape(channels_in, taps_total, block_out), (1, 0, 2))
        * grad_scale
    )
    bias_part = jnp.sum(output_grad.astype(jnp.float32), axis=(1, 2)) * grad_scale
    weight_size = weight_part.size
    reduced = all_reduce_pairs(jnp.concatenate([weight_part.reshape(weight_size), bias_part]), "space")
    weight_grad = reduced[:weight_size].reshape(weight_part.shape)
    bias_grad = reduced[weight_size : weight_size + bias_part.shape[0]]
    spread = jnp.stack(
        [
            shift_cells(
                grad_rimmed[:, 1 - depth_step : 1 - depth_step + depth_cells],
                -row_step,
                -column_step,
            )
            for depth_step, row_step, column_step in tap_offsets
        ]
    )
    spread = spread.reshape(taps_total * block_out, depth_cells * plane_cells)
    backward_weight = jnp.transpose(weight, (1, 0, 2)).reshape(channels_in, taps_total * block_out)
    summed = lax.psum_scatter(
        jnp.dot(backward_weight, spread, preferred_element_type=jnp.float32),
        "chan",
        scatter_dimension=0,
        tiled=True,
    )
    input_grad = summed.astype(jnp.bfloat16).reshape(block_in, depth_cells, plane_cells)
    return (outputs, input_grad, weight_grad, bias_grad)


def solution(mesh):
    placed = (P("chan", "space", None), P(None, None, "chan"), P("chan"), P("chan", "space", None))
    return jax.shard_map(
        body,
        mesh=mesh,
        in_specs=placed,
        out_specs=(
            P("chan", "space", None),
            P("chan", "space", None),
            P(None, None, "chan"),
            P("chan"),
        ),
        check_vma=False,
    )
```

```python
import math

import jax
import jax.numpy as jnp
from jax import lax
from jax.sharding import PartitionSpec as P

W = 64


tap_offsets = tuple(
    (
        (depth_step, row_step, column_step)
        for depth_step in (-1, 0, 1)
        for row_step in (-1, 0, 1)
        for column_step in (-1, 0, 1)
    )
)


def padded_2(array, sides, width):
    for axis, dim in sides:
        devices, length = (lax.axis_size(axis), array.shape[dim])
        up = [(i, (i + 1) % devices) for i in range(devices - 1)]
        down = [(j, i) for i, j in up]
        last = lax.slice_in_dim(array, length - width, length, axis=dim)
        first = lax.slice_in_dim(array, 0, width, axis=dim)
        before = lax.ppermute(last, axis, up)
        after = lax.ppermute(first, axis, down)
        array = jnp.concatenate([before, array, after], axis=dim)
    return array


def shift_cells(field, row_step, column_step):
    length_flat = field.shape[-1]
    pad_width = W + 1
    widths = [(0, 0)] * (field.ndim - 1) + [(pad_width, pad_width)]
    padded = jnp.pad(field, widths)
    first_index = pad_width + row_step * W + column_step
    shifted = lax.slice_in_dim(padded, first_index, first_index + length_flat, axis=field.ndim - 1)
    column = jnp.arange(length_flat, dtype=jnp.int32) % W
    inside = (column + column_step >= 0) & (column + column_step < W)
    return jnp.where(inside, shifted, jnp.zeros_like(shifted))


def outer_planes(field):
    return jnp.concatenate([field[:, :1], field[:, -1:]], axis=1)


def attach_rims(field, rims):
    return jnp.concatenate([rims[:, :1], field, rims[:, 3:]], axis=1)


def all_reduce_rows(block, axis):
    devices = lax.axis_size(axis)
    steps = devices.bit_length() - 1
    assert 1 << steps == devices
    current = block
    index = lax.axis_index(axis)
    for step in range(steps):
        half = current.shape[0] // 2
        bit = (index >> step) & 1
        keep = lax.dynamic_slice_in_dim(current, bit * half, half)
        send = lax.dynamic_slice_in_dim(current, (1 - bit) * half, half)
        pairs = [(i, i ^ (1 << step)) for i in range(devices)]
        current = keep + lax.ppermute(send, axis, pairs)
    for step in reversed(range(steps)):
        half = current.shape[0]
        bit = (index >> step) & 1
        pairs = [(i, i ^ (1 << step)) for i in range(devices)]
        other = lax.ppermute(current, axis, pairs)
        both = jnp.zeros((2 * half,) + current.shape[1:], current.dtype)
        both = lax.dynamic_update_slice_in_dim(both, current, bit * half, 0)
        current = lax.dynamic_update_slice_in_dim(both, other, (1 - bit) * half, 0)
    return current


def shift_volume(field, row_step, column_step, rows):
    length_flat = field.shape[-1]
    pad_width = W + 1
    widths = [(0, 0)] * (field.ndim - 1) + [(pad_width, pad_width)]
    padded = jnp.pad(field, widths)
    first_index = pad_width + row_step * W + column_step
    shifted = lax.slice_in_dim(padded, first_index, first_index + length_flat, axis=field.ndim - 1)
    cell = jnp.arange(length_flat, dtype=jnp.int32)
    column = cell % W
    row = (cell // W) % rows
    inside = (column + column_step >= 0) & (column + column_step < W)
    inside = inside & (row + row_step >= 0) & (row + row_step < rows)
    return jnp.where(inside, shifted, jnp.zeros_like(shifted))


plane_offsets = tuple((row_step, column_step) for row_step in (-1, 0, 1) for column_step in (-1, 0, 1))


def body(inputs, weight, bias_term, output_grad):
    taps_total = weight.shape[0]
    channels_in = weight.shape[1]
    block_out = weight.shape[2]
    block_in = inputs.shape[0]
    depth_cells = inputs.shape[1]
    plane_cells = inputs.shape[2]
    rows = plane_cells // W
    slab_cells = depth_cells * plane_cells
    grad_scale = 1.0 / math.sqrt(lax.axis_size("space") * depth_cells * plane_cells)
    own_rims = padded_2(outer_planes(inputs), (("space", 1),), 1)
    rimmed = attach_rims(inputs, own_rims)
    gathered = lax.all_gather(rimmed, "chan", axis=0, tiled=True)
    windows = jnp.stack(
        [gathered[:, 1 + depth_step : 1 + depth_step + depth_cells] for depth_step in (-1, 0, 1)]
    ).reshape(3, channels_in, slab_cells)

    weight_grid = weight.reshape(3, 9, channels_in, block_out)
    forward_weight = jnp.transpose(weight_grid, (1, 3, 0, 2)).reshape(9 * block_out, 3 * channels_in)
    in_plane = jnp.dot(
        forward_weight, windows.reshape(3 * channels_in, slab_cells), preferred_element_type=jnp.float32
    ).reshape(9, block_out, slab_cells)
    forward = jnp.zeros((block_out, slab_cells), jnp.float32)
    for shift_index, (row_step, column_step) in enumerate(plane_offsets):
        forward = forward + shift_volume(in_plane[shift_index], row_step, column_step, rows)
    outputs = (forward + bias_term[:, None]).astype(jnp.bfloat16).reshape(block_out, depth_cells, plane_cells)

    grad_rimmed = padded_2(output_grad, (("space", 1),), 1)
    grad_shifted = jnp.stack(
        [shift_cells(grad_rimmed, -row_step, -column_step) for row_step, column_step in plane_offsets]
    )
    placed = grad_shifted[:, :, 1 : 1 + depth_cells].reshape(9 * block_out, slab_cells)
    weight_part = lax.dot_general(
        placed, windows, (((1,), (2,)), ((), ())), preferred_element_type=jnp.float32
    )
    weight_part = jnp.transpose(weight_part, (1, 0, 2)).reshape(taps_total * block_out, channels_in)
    bias_part = jnp.sum(output_grad.astype(jnp.float32), axis=(1, 2))
    space_devices = lax.axis_size("space")
    unit = 8 * space_devices
    total_rows = -(-(taps_total * block_out + 1) // unit) * unit
    bias_rows = jnp.zeros((total_rows - taps_total * block_out, channels_in), jnp.float32)
    bias_rows = bias_rows.at[0, :block_out].set(bias_part)
    reduced = all_reduce_rows(
        jnp.concatenate([weight_part, bias_rows]) * grad_scale, "space"
    )
    weight_grad = jnp.transpose(
        reduced[: taps_total * block_out].reshape(taps_total, block_out, channels_in), (0, 2, 1)
    )
    bias_grad = reduced[taps_total * block_out, :block_out]

    spread = jnp.stack(
        [grad_shifted[:, :, 1 - depth_step : 1 - depth_step + depth_cells] for depth_step in (-1, 0, 1)]
    ).reshape(taps_total * block_out, slab_cells)
    backward_weight = jnp.transpose(weight, (1, 0, 2)).reshape(channels_in, taps_total * block_out)
    summed = lax.psum_scatter(
        jnp.dot(backward_weight, spread, preferred_element_type=jnp.float32),
        "chan",
        scatter_dimension=0,
        tiled=True,
    )
    input_grad = summed.astype(jnp.bfloat16).reshape(block_in, depth_cells, plane_cells)
    return (outputs, input_grad, weight_grad, bias_grad)


def solution(mesh):
    placed = (P("chan", "space", None), P(None, None, "chan"), P("chan"), P("chan", "space", None))
    return jax.shard_map(
        body,
        mesh=mesh,
        in_specs=placed,
        out_specs=(
            P("chan", "space", None),
            P("chan", "space", None),
            P(None, None, "chan"),
            P("chan"),
        ),
        check_vma=False,
    )
```

```python
import math

import jax
import jax.numpy as jnp
from jax import lax
from jax.sharding import PartitionSpec as P

W = 64


tap_offsets = tuple(
    (
        (depth_step, row_step, column_step)
        for depth_step in (-1, 0, 1)
        for row_step in (-1, 0, 1)
        for column_step in (-1, 0, 1)
    )
)


def padded_2(array, sides, width):
    for axis, dim in sides:
        devices, length = (lax.axis_size(axis), array.shape[dim])
        up = [(i, (i + 1) % devices) for i in range(devices - 1)]
        down = [(j, i) for i, j in up]
        last = lax.slice_in_dim(array, length - width, length, axis=dim)
        first = lax.slice_in_dim(array, 0, width, axis=dim)
        before = lax.ppermute(last, axis, up)
        after = lax.ppermute(first, axis, down)
        array = jnp.concatenate([before, array, after], axis=dim)
    return array


def shift_cells(field, row_step, column_step):
    length_flat = field.shape[-1]
    pad_width = W + 1
    widths = [(0, 0)] * (field.ndim - 1) + [(pad_width, pad_width)]
    padded = jnp.pad(field, widths)
    first_index = pad_width + row_step * W + column_step
    shifted = lax.slice_in_dim(padded, first_index, first_index + length_flat, axis=field.ndim - 1)
    column = jnp.arange(length_flat, dtype=jnp.int32) % W
    inside = (column + column_step >= 0) & (column + column_step < W)
    return jnp.where(inside, shifted, jnp.zeros_like(shifted))


def outer_planes(field):
    return jnp.concatenate([field[:, :1], field[:, -1:]], axis=1)


def attach_rims(field, rims):
    return jnp.concatenate([rims[:, :1], field, rims[:, 3:]], axis=1)


def all_reduce_rows(block, axis):
    devices = lax.axis_size(axis)
    steps = devices.bit_length() - 1
    assert 1 << steps == devices
    current = block
    index = lax.axis_index(axis)
    for step in range(steps):
        half = current.shape[0] // 2
        bit = (index >> step) & 1
        keep = lax.dynamic_slice_in_dim(current, bit * half, half)
        send = lax.dynamic_slice_in_dim(current, (1 - bit) * half, half)
        pairs = [(i, i ^ (1 << step)) for i in range(devices)]
        current = keep + lax.ppermute(send, axis, pairs)
    for step in reversed(range(steps)):
        half = current.shape[0]
        bit = (index >> step) & 1
        pairs = [(i, i ^ (1 << step)) for i in range(devices)]
        other = lax.ppermute(current, axis, pairs)
        both = jnp.zeros((2 * half,) + current.shape[1:], current.dtype)
        both = lax.dynamic_update_slice_in_dim(both, current, bit * half, 0)
        current = lax.dynamic_update_slice_in_dim(both, other, (1 - bit) * half, 0)
    return current


def shift_volume(field, row_step, column_step, rows):
    length_flat = field.shape[-1]
    pad_width = W + 1
    widths = [(0, 0)] * (field.ndim - 1) + [(pad_width, pad_width)]
    padded = jnp.pad(field, widths)
    first_index = pad_width + row_step * W + column_step
    shifted = lax.slice_in_dim(padded, first_index, first_index + length_flat, axis=field.ndim - 1)
    cell = jnp.arange(length_flat, dtype=jnp.int32)
    column = cell % W
    row = (cell // W) % rows
    inside = (column + column_step >= 0) & (column + column_step < W)
    inside = inside & (row + row_step >= 0) & (row + row_step < rows)
    return jnp.where(inside, shifted, jnp.zeros_like(shifted))


plane_offsets = tuple((row_step, column_step) for row_step in (-1, 0, 1) for column_step in (-1, 0, 1))


def body(inputs, weight, bias_term, output_grad):
    taps_total = weight.shape[0]
    channels_in = weight.shape[1]
    block_out = weight.shape[2]
    block_in = inputs.shape[0]
    depth_cells = inputs.shape[1]
    plane_cells = inputs.shape[2]
    grad_scale = 1.0 / math.sqrt(lax.axis_size("space") * depth_cells * plane_cells)
    inputs_planes = jnp.transpose(inputs, (1, 0, 2))
    grad_planes = jnp.transpose(output_grad, (1, 0, 2))
    rimmed = padded_2(inputs_planes, (("space", 0),), 1)
    gathered = lax.all_gather(rimmed, "chan", axis=1, tiled=True)

    weight_grid = weight.reshape(3, 9, channels_in, block_out)
    forward_weight = jnp.transpose(weight_grid, (0, 1, 3, 2)).reshape(3, 9 * block_out, channels_in)
    in_plane = None
    for depth_index in range(3):
        part = jnp.einsum(
            "ki,zin->zkn",
            forward_weight[depth_index],
            gathered[depth_index : depth_index + depth_cells],
            preferred_element_type=jnp.float32,
        )
        in_plane = part if in_plane is None else in_plane + part
    in_plane = in_plane.reshape(depth_cells, 9, block_out, plane_cells)
    forward = None
    for shift_index, (row_step, column_step) in enumerate(plane_offsets):
        term = shift_cells(in_plane[:, shift_index], row_step, column_step)
        forward = term if forward is None else forward + term
    outputs = jnp.transpose(
        (forward + bias_term[None, :, None]).astype(jnp.bfloat16), (1, 0, 2)
    )

    grad_rimmed = padded_2(grad_planes, (("space", 0),), 1)
    grad_shifted = jnp.stack(
        [shift_cells(grad_rimmed, -row_step, -column_step) for row_step, column_step in plane_offsets],
        axis=1,
    ).reshape(depth_cells + 2, 9 * block_out, plane_cells)
    placed = grad_shifted[1 : 1 + depth_cells]
    weight_part = jnp.stack(
        [
            jnp.einsum(
                "zkn,zin->ki",
                placed,
                gathered[depth_index : depth_index + depth_cells],
                preferred_element_type=jnp.float32,
            )
            for depth_index in range(3)
        ]
    ).reshape(taps_total * block_out, channels_in)
    bias_part = jnp.sum(output_grad.astype(jnp.float32), axis=(1, 2))
    space_devices = lax.axis_size("space")
    unit = 8 * space_devices
    total_rows = -(-(taps_total * block_out + 1) // unit) * unit
    bias_rows = jnp.zeros((total_rows - taps_total * block_out, channels_in), jnp.float32)
    bias_rows = bias_rows.at[0, :block_out].set(bias_part)
    reduced = all_reduce_rows(
        jnp.concatenate([weight_part, bias_rows]) * grad_scale, "space"
    )
    weight_grad = jnp.transpose(
        reduced[: taps_total * block_out].reshape(taps_total, block_out, channels_in), (0, 2, 1)
    )
    bias_grad = reduced[taps_total * block_out, :block_out]

    chan_devices = lax.axis_size("chan")
    backward_weight = jnp.transpose(weight_grid, (0, 2, 1, 3)).reshape(
        3, chan_devices, channels_in // chan_devices, 9 * block_out
    )
    spread = None
    for depth_index in range(3):
        part = jnp.einsum(
            "bjk,zkn->bjzn",
            backward_weight[depth_index],
            grad_shifted[2 - depth_index : 2 - depth_index + depth_cells],
            preferred_element_type=jnp.float32,
        )
        spread = part if spread is None else spread + part
    summed = lax.psum_scatter(
        spread.reshape(channels_in, depth_cells * plane_cells), "chan", scatter_dimension=0, tiled=True
    )
    input_grad = summed.astype(jnp.bfloat16).reshape(block_in, depth_cells, plane_cells)
    return (outputs, input_grad, weight_grad, bias_grad)


def solution(mesh):
    placed = (P("chan", "space", None), P(None, None, "chan"), P("chan"), P("chan", "space", None))
    return jax.shard_map(
        body,
        mesh=mesh,
        in_specs=placed,
        out_specs=(
            P("chan", "space", None),
            P("chan", "space", None),
            P(None, None, "chan"),
            P("chan"),
        ),
        check_vma=False,
    )
```

```python
import math

import jax
import jax.numpy as jnp
from jax import lax
from jax.sharding import PartitionSpec as P

W = 64


tap_offsets = tuple(
    (
        (depth_step, row_step, column_step)
        for depth_step in (-1, 0, 1)
        for row_step in (-1, 0, 1)
        for column_step in (-1, 0, 1)
    )
)


def padded_2(array, sides, width):
    for axis, dim in sides:
        devices, length = (lax.axis_size(axis), array.shape[dim])
        up = [(i, (i + 1) % devices) for i in range(devices - 1)]
        down = [(j, i) for i, j in up]
        last = lax.slice_in_dim(array, length - width, length, axis=dim)
        first = lax.slice_in_dim(array, 0, width, axis=dim)
        before = lax.ppermute(last, axis, up)
        after = lax.ppermute(first, axis, down)
        array = jnp.concatenate([before, array, after], axis=dim)
    return array


def shift_cells(field, row_step, column_step):
    length_flat = field.shape[-1]
    pad_width = W + 1
    widths = [(0, 0)] * (field.ndim - 1) + [(pad_width, pad_width)]
    padded = jnp.pad(field, widths)
    first_index = pad_width + row_step * W + column_step
    shifted = lax.slice_in_dim(padded, first_index, first_index + length_flat, axis=field.ndim - 1)
    column = jnp.arange(length_flat, dtype=jnp.int32) % W
    inside = (column + column_step >= 0) & (column + column_step < W)
    return jnp.where(inside, shifted, jnp.zeros_like(shifted))


def outer_planes(field):
    return jnp.concatenate([field[:, :1], field[:, -1:]], axis=1)


def attach_rims(field, rims):
    return jnp.concatenate([rims[:, :1], field, rims[:, 3:]], axis=1)


def all_reduce_rows(block, axis):
    devices = lax.axis_size(axis)
    steps = devices.bit_length() - 1
    assert 1 << steps == devices
    current = block
    index = lax.axis_index(axis)
    for step in range(steps):
        half = current.shape[0] // 2
        bit = (index >> step) & 1
        keep = lax.dynamic_slice_in_dim(current, bit * half, half)
        send = lax.dynamic_slice_in_dim(current, (1 - bit) * half, half)
        pairs = [(i, i ^ (1 << step)) for i in range(devices)]
        current = keep + lax.ppermute(send, axis, pairs)
    for step in reversed(range(steps)):
        half = current.shape[0]
        bit = (index >> step) & 1
        pairs = [(i, i ^ (1 << step)) for i in range(devices)]
        other = lax.ppermute(current, axis, pairs)
        both = jnp.zeros((2 * half,) + current.shape[1:], current.dtype)
        both = lax.dynamic_update_slice_in_dim(both, current, bit * half, 0)
        current = lax.dynamic_update_slice_in_dim(both, other, (1 - bit) * half, 0)
    return current


def shift_volume(field, row_step, column_step, rows):
    length_flat = field.shape[-1]
    pad_width = W + 1
    widths = [(0, 0)] * (field.ndim - 1) + [(pad_width, pad_width)]
    padded = jnp.pad(field, widths)
    first_index = pad_width + row_step * W + column_step
    shifted = lax.slice_in_dim(padded, first_index, first_index + length_flat, axis=field.ndim - 1)
    cell = jnp.arange(length_flat, dtype=jnp.int32)
    column = cell % W
    row = (cell // W) % rows
    inside = (column + column_step >= 0) & (column + column_step < W)
    inside = inside & (row + row_step >= 0) & (row + row_step < rows)
    return jnp.where(inside, shifted, jnp.zeros_like(shifted))


plane_offsets = tuple((row_step, column_step) for row_step in (-1, 0, 1) for column_step in (-1, 0, 1))


def body(inputs, weight, bias_term, output_grad):
    taps_total = weight.shape[0]
    channels_in = weight.shape[1]
    block_out = weight.shape[2]
    block_in = inputs.shape[0]
    depth_cells = inputs.shape[1]
    plane_cells = inputs.shape[2]
    grad_scale = 1.0 / math.sqrt(lax.axis_size("space") * depth_cells * plane_cells)
    inputs_planes = jnp.transpose(inputs, (1, 0, 2))
    grad_planes = jnp.transpose(output_grad, (1, 0, 2))
    gathered = lax.all_gather(inputs_planes, "chan", axis=1, tiled=True)

    weight_grid = weight.reshape(3, 9, channels_in, block_out)
    forward_weight = jnp.transpose(weight_grid, (0, 1, 3, 2)).reshape(3, 9 * block_out, channels_in)
    in_plane = None
    for depth_index in range(3):
        part = jnp.einsum(
            "ki,zin->zkn",
            forward_weight[depth_index],
            gathered,
            preferred_element_type=jnp.float32,
        )
        part = jnp.pad(part, ((2 - depth_index, depth_index), (0, 0), (0, 0)))
        in_plane = part if in_plane is None else in_plane + part
    in_plane = in_plane.reshape(depth_cells + 2, 9, block_out, plane_cells)
    forward = None
    for shift_index, (row_step, column_step) in enumerate(plane_offsets):
        term = shift_cells(in_plane[:, shift_index], row_step, column_step)
        forward = term if forward is None else forward + term
    space_devices = lax.axis_size("space")
    up = [(i, i + 1) for i in range(space_devices - 1)]
    down = [(i + 1, i) for i in range(space_devices - 1)]
    from_below = lax.ppermute(forward[depth_cells + 1 :], "space", up)
    from_above = lax.ppermute(forward[:1], "space", down)
    forward = forward[1 : depth_cells + 1] + jnp.concatenate(
        [from_below, jnp.zeros((depth_cells - 2, block_out, plane_cells), jnp.float32), from_above]
    )
    outputs = jnp.transpose(
        (forward + bias_term[None, :, None]).astype(jnp.bfloat16), (1, 0, 2)
    )

    grad_rimmed = padded_2(grad_planes, (("space", 0),), 1)
    grad_shifted = jnp.stack(
        [shift_cells(grad_rimmed, -row_step, -column_step) for row_step, column_step in plane_offsets],
        axis=1,
    ).reshape(depth_cells + 2, 9 * block_out, plane_cells)
    weight_part = jnp.stack(
        [
            jnp.einsum(
                "zkn,zin->ki",
                grad_shifted[2 - depth_index : 2 - depth_index + depth_cells],
                gathered,
                preferred_element_type=jnp.float32,
            )
            for depth_index in range(3)
        ]
    ).reshape(taps_total * block_out, channels_in)
    bias_part = jnp.sum(output_grad.astype(jnp.float32), axis=(1, 2))
    unit = 8 * space_devices
    total_rows = -(-(taps_total * block_out + 1) // unit) * unit
    bias_rows = jnp.zeros((total_rows - taps_total * block_out, channels_in), jnp.float32)
    bias_rows = bias_rows.at[0, :block_out].set(bias_part)
    reduced = all_reduce_rows(
        jnp.concatenate([weight_part, bias_rows]) * grad_scale, "space"
    )
    weight_grad = jnp.transpose(
        reduced[: taps_total * block_out].reshape(taps_total, block_out, channels_in), (0, 2, 1)
    )
    bias_grad = reduced[taps_total * block_out, :block_out]

    chan_devices = lax.axis_size("chan")
    backward_weight = jnp.transpose(weight_grid, (0, 2, 1, 3)).reshape(
        3, chan_devices, channels_in // chan_devices, 9 * block_out
    )
    spread = None
    for depth_index in range(3):
        part = jnp.einsum(
            "bjk,zkn->bjzn",
            backward_weight[depth_index],
            grad_shifted[2 - depth_index : 2 - depth_index + depth_cells],
            preferred_element_type=jnp.float32,
        )
        spread = part if spread is None else spread + part
    summed = lax.psum_scatter(
        spread.reshape(channels_in, depth_cells * plane_cells), "chan", scatter_dimension=0, tiled=True
    )
    input_grad = summed.astype(jnp.bfloat16).reshape(block_in, depth_cells, plane_cells)
    return (outputs, input_grad, weight_grad, bias_grad)


def solution(mesh):
    placed = (P("chan", "space", None), P(None, None, "chan"), P("chan"), P("chan", "space", None))
    return jax.shard_map(
        body,
        mesh=mesh,
        in_specs=placed,
        out_specs=(
            P("chan", "space", None),
            P("chan", "space", None),
            P(None, None, "chan"),
            P("chan"),
        ),
        check_vma=False,
    )
```

```python
import math

import jax
import jax.numpy as jnp
from jax import lax
from jax.sharding import PartitionSpec as P

W = 64


tap_offsets = tuple(
    (
        (depth_step, row_step, column_step)
        for depth_step in (-1, 0, 1)
        for row_step in (-1, 0, 1)
        for column_step in (-1, 0, 1)
    )
)


def padded_2(array, sides, width):
    for axis, dim in sides:
        devices, length = (lax.axis_size(axis), array.shape[dim])
        up = [(i, (i + 1) % devices) for i in range(devices - 1)]
        down = [(j, i) for i, j in up]
        last = lax.slice_in_dim(array, length - width, length, axis=dim)
        first = lax.slice_in_dim(array, 0, width, axis=dim)
        before = lax.ppermute(last, axis, up)
        after = lax.ppermute(first, axis, down)
        array = jnp.concatenate([before, array, after], axis=dim)
    return array


def shift_cells(field, row_step, column_step):
    length_flat = field.shape[-1]
    pad_width = W + 1
    widths = [(0, 0)] * (field.ndim - 1) + [(pad_width, pad_width)]
    padded = jnp.pad(field, widths)
    first_index = pad_width + row_step * W + column_step
    shifted = lax.slice_in_dim(padded, first_index, first_index + length_flat, axis=field.ndim - 1)
    column = jnp.arange(length_flat, dtype=jnp.int32) % W
    inside = (column + column_step >= 0) & (column + column_step < W)
    return jnp.where(inside, shifted, jnp.zeros_like(shifted))


def outer_planes(field):
    return jnp.concatenate([field[:, :1], field[:, -1:]], axis=1)


def attach_rims(field, rims):
    return jnp.concatenate([rims[:, :1], field, rims[:, 3:]], axis=1)


def all_reduce_rows(block, axis):
    devices = lax.axis_size(axis)
    steps = devices.bit_length() - 1
    assert 1 << steps == devices
    current = block
    index = lax.axis_index(axis)
    for step in range(steps):
        half = current.shape[0] // 2
        bit = (index >> step) & 1
        keep = lax.dynamic_slice_in_dim(current, bit * half, half)
        send = lax.dynamic_slice_in_dim(current, (1 - bit) * half, half)
        pairs = [(i, i ^ (1 << step)) for i in range(devices)]
        current = keep + lax.ppermute(send, axis, pairs)
    for step in reversed(range(steps)):
        half = current.shape[0]
        bit = (index >> step) & 1
        pairs = [(i, i ^ (1 << step)) for i in range(devices)]
        other = lax.ppermute(current, axis, pairs)
        both = jnp.zeros((2 * half,) + current.shape[1:], current.dtype)
        both = lax.dynamic_update_slice_in_dim(both, current, bit * half, 0)
        current = lax.dynamic_update_slice_in_dim(both, other, (1 - bit) * half, 0)
    return current


def shift_volume(field, row_step, column_step, rows):
    length_flat = field.shape[-1]
    pad_width = W + 1
    widths = [(0, 0)] * (field.ndim - 1) + [(pad_width, pad_width)]
    padded = jnp.pad(field, widths)
    first_index = pad_width + row_step * W + column_step
    shifted = lax.slice_in_dim(padded, first_index, first_index + length_flat, axis=field.ndim - 1)
    cell = jnp.arange(length_flat, dtype=jnp.int32)
    column = cell % W
    row = (cell // W) % rows
    inside = (column + column_step >= 0) & (column + column_step < W)
    inside = inside & (row + row_step >= 0) & (row + row_step < rows)
    return jnp.where(inside, shifted, jnp.zeros_like(shifted))


plane_offsets = tuple((row_step, column_step) for row_step in (-1, 0, 1) for column_step in (-1, 0, 1))


def reduce_scatter_blocks(blocks, axis):
    devices = lax.axis_size(axis)
    steps = devices.bit_length() - 1
    assert 1 << steps == devices
    current = blocks.reshape((2,) * steps + blocks.shape[1:])
    index = lax.axis_index(axis)
    for step in range(steps):
        bit = (index >> step) & 1
        position = steps - 1 - step
        keep = lax.dynamic_index_in_dim(current, bit, axis=position, keepdims=False)
        send = lax.dynamic_index_in_dim(current, 1 - bit, axis=position, keepdims=False)
        pairs = [(i, i ^ (1 << step)) for i in range(devices)]
        current = keep + lax.ppermute(send, axis, pairs)
    return current


def body(inputs, weight, bias_term, output_grad):
    taps_total = weight.shape[0]
    channels_in = weight.shape[1]
    block_out = weight.shape[2]
    block_in = inputs.shape[0]
    depth_cells = inputs.shape[1]
    plane_cells = inputs.shape[2]
    grad_scale = 1.0 / math.sqrt(lax.axis_size("space") * depth_cells * plane_cells)
    inputs_planes = jnp.transpose(inputs, (1, 0, 2))
    grad_planes = jnp.transpose(output_grad, (1, 0, 2))
    gathered = lax.all_gather(inputs_planes, "chan", axis=1, tiled=True)

    weight_grid = weight.reshape(3, 9, channels_in, block_out)
    forward_weight = jnp.transpose(weight_grid, (0, 1, 3, 2)).reshape(3, 9 * block_out, channels_in)
    in_plane = None
    for depth_index in range(3):
        part = jnp.einsum(
            "ki,zin->zkn",
            forward_weight[depth_index],
            gathered,
            preferred_element_type=jnp.float32,
        )
        part = jnp.pad(part, ((2 - depth_index, depth_index), (0, 0), (0, 0)))
        in_plane = part if in_plane is None else in_plane + part
    in_plane = in_plane.reshape(depth_cells + 2, 9, block_out, plane_cells)
    forward = None
    for shift_index, (row_step, column_step) in enumerate(plane_offsets):
        term = shift_cells(in_plane[:, shift_index], row_step, column_step)
        forward = term if forward is None else forward + term
    space_devices = lax.axis_size("space")
    up = [(i, i + 1) for i in range(space_devices - 1)]
    down = [(i + 1, i) for i in range(space_devices - 1)]
    from_below = lax.ppermute(forward[depth_cells + 1 :], "space", up)
    from_above = lax.ppermute(forward[:1], "space", down)
    forward = forward[1 : depth_cells + 1] + jnp.concatenate(
        [from_below, jnp.zeros((depth_cells - 2, block_out, plane_cells), jnp.float32), from_above]
    )
    outputs = jnp.transpose(
        (forward + bias_term[None, :, None]).astype(jnp.bfloat16), (1, 0, 2)
    )

    grad_rimmed = padded_2(grad_planes, (("space", 0),), 1)
    grad_shifted = jnp.stack(
        [shift_cells(grad_rimmed, -row_step, -column_step) for row_step, column_step in plane_offsets],
        axis=1,
    ).reshape(depth_cells + 2, 9 * block_out, plane_cells)
    weight_part = jnp.stack(
        [
            jnp.einsum(
                "zkn,zin->ki",
                grad_shifted[2 - depth_index : 2 - depth_index + depth_cells],
                gathered,
                preferred_element_type=jnp.float32,
            )
            for depth_index in range(3)
        ]
    ).reshape(taps_total * block_out, channels_in)
    bias_part = jnp.sum(output_grad.astype(jnp.float32), axis=(1, 2))
    unit = 8 * space_devices
    total_rows = -(-(taps_total * block_out + 1) // unit) * unit
    bias_rows = jnp.zeros((total_rows - taps_total * block_out, channels_in), jnp.float32)
    bias_rows = bias_rows.at[0, :block_out].set(bias_part)
    reduced = all_reduce_rows(
        jnp.concatenate([weight_part, bias_rows]) * grad_scale, "space"
    )
    weight_grad = jnp.transpose(
        reduced[: taps_total * block_out].reshape(taps_total, block_out, channels_in), (0, 2, 1)
    )
    bias_grad = reduced[taps_total * block_out, :block_out]

    chan_devices = lax.axis_size("chan")
    backward_weight = jnp.transpose(weight_grid, (0, 2, 1, 3)).reshape(
        3, chan_devices, channels_in // chan_devices, 9 * block_out
    )
    spread = None
    for depth_index in range(3):
        part = jnp.einsum(
            "bjk,zkn->bjzn",
            backward_weight[depth_index],
            grad_shifted[2 - depth_index : 2 - depth_index + depth_cells],
            preferred_element_type=jnp.float32,
        )
        spread = part if spread is None else spread + part
    summed = reduce_scatter_blocks(
        spread.reshape(chan_devices, channels_in // chan_devices, depth_cells * plane_cells), "chan"
    )
    input_grad = summed.astype(jnp.bfloat16).reshape(block_in, depth_cells, plane_cells)
    return (outputs, input_grad, weight_grad, bias_grad)


def solution(mesh):
    placed = (P("chan", "space", None), P(None, None, "chan"), P("chan"), P("chan", "space", None))
    return jax.shard_map(
        body,
        mesh=mesh,
        in_specs=placed,
        out_specs=(
            P("chan", "space", None),
            P("chan", "space", None),
            P(None, None, "chan"),
            P("chan"),
        ),
        check_vma=False,
    )
```

```python
import math

import jax
import jax.numpy as jnp
from jax import lax
from jax.sharding import Mesh, PartitionSpec as P

W = 64


tap_offsets = tuple(
    (
        (depth_step, row_step, column_step)
        for depth_step in (-1, 0, 1)
        for row_step in (-1, 0, 1)
        for column_step in (-1, 0, 1)
    )
)


def padded_2(array, sides, width):
    for axis, dim in sides:
        devices, length = (lax.axis_size(axis), array.shape[dim])
        up = [(i, (i + 1) % devices) for i in range(devices - 1)]
        down = [(j, i) for i, j in up]
        last = lax.slice_in_dim(array, length - width, length, axis=dim)
        first = lax.slice_in_dim(array, 0, width, axis=dim)
        before = lax.ppermute(last, axis, up)
        after = lax.ppermute(first, axis, down)
        array = jnp.concatenate([before, array, after], axis=dim)
    return array


def shift_cells(field, row_step, column_step):
    length_flat = field.shape[-1]
    pad_width = W + 1
    widths = [(0, 0)] * (field.ndim - 1) + [(pad_width, pad_width)]
    padded = jnp.pad(field, widths)
    first_index = pad_width + row_step * W + column_step
    shifted = lax.slice_in_dim(padded, first_index, first_index + length_flat, axis=field.ndim - 1)
    column = jnp.arange(length_flat, dtype=jnp.int32) % W
    inside = (column + column_step >= 0) & (column + column_step < W)
    return jnp.where(inside, shifted, jnp.zeros_like(shifted))


def outer_planes(field):
    return jnp.concatenate([field[:, :1], field[:, -1:]], axis=1)


def attach_rims(field, rims):
    return jnp.concatenate([rims[:, :1], field, rims[:, 3:]], axis=1)


def all_reduce_rows(block, axis):
    devices = lax.axis_size(axis)
    steps = devices.bit_length() - 1
    assert 1 << steps == devices
    current = block
    index = lax.axis_index(axis)
    for step in range(steps):
        half = current.shape[0] // 2
        bit = (index >> step) & 1
        keep = lax.dynamic_slice_in_dim(current, bit * half, half)
        send = lax.dynamic_slice_in_dim(current, (1 - bit) * half, half)
        pairs = [(i, i ^ (1 << step)) for i in range(devices)]
        current = keep + lax.ppermute(send, axis, pairs)
    for step in reversed(range(steps)):
        half = current.shape[0]
        bit = (index >> step) & 1
        pairs = [(i, i ^ (1 << step)) for i in range(devices)]
        other = lax.ppermute(current, axis, pairs)
        both = jnp.zeros((2 * half,) + current.shape[1:], current.dtype)
        both = lax.dynamic_update_slice_in_dim(both, current, bit * half, 0)
        current = lax.dynamic_update_slice_in_dim(both, other, (1 - bit) * half, 0)
    return current


def shift_volume(field, row_step, column_step, rows):
    length_flat = field.shape[-1]
    pad_width = W + 1
    widths = [(0, 0)] * (field.ndim - 1) + [(pad_width, pad_width)]
    padded = jnp.pad(field, widths)
    first_index = pad_width + row_step * W + column_step
    shifted = lax.slice_in_dim(padded, first_index, first_index + length_flat, axis=field.ndim - 1)
    cell = jnp.arange(length_flat, dtype=jnp.int32)
    column = cell % W
    row = (cell // W) % rows
    inside = (column + column_step >= 0) & (column + column_step < W)
    inside = inside & (row + row_step >= 0) & (row + row_step < rows)
    return jnp.where(inside, shifted, jnp.zeros_like(shifted))


plane_offsets = tuple((row_step, column_step) for row_step in (-1, 0, 1) for column_step in (-1, 0, 1))


def other_core(value):
    return lax.ppermute(value, "core", [(0, 1), (1, 0)])


def gather_channels(planes):
    chip_blocks = lax.all_gather(planes, "chips", axis=1, tiled=False)
    partner = other_core(chip_blocks)
    first = lax.axis_index("core") == 0
    low = jnp.where(first, chip_blocks, partner)
    high = jnp.where(first, partner, chip_blocks)
    both = jnp.stack([low, high], axis=2)
    return both.reshape(planes.shape[0], -1, planes.shape[2])


def scatter_channels(blocks):
    by_core = blocks.reshape(-1, 2, blocks.shape[1], blocks.shape[2])
    core = lax.axis_index("core")
    keep = lax.dynamic_index_in_dim(by_core, core, axis=1, keepdims=False)
    send = lax.dynamic_index_in_dim(by_core, 1 - core, axis=1, keepdims=False)
    partial = keep + other_core(send)
    return lax.psum_scatter(
        partial.reshape(-1, blocks.shape[2]), "chips", scatter_dimension=0, tiled=True
    )


def body(inputs, weight, bias_term, output_grad):
    taps_total = weight.shape[0]
    channels_in = weight.shape[1]
    block_out = weight.shape[2]
    block_in = inputs.shape[0]
    depth_cells = inputs.shape[1]
    plane_cells = inputs.shape[2]
    grad_scale = 1.0 / math.sqrt(lax.axis_size("space") * depth_cells * plane_cells)
    inputs_planes = jnp.transpose(inputs, (1, 0, 2))
    grad_planes = jnp.transpose(output_grad, (1, 0, 2))
    gathered = gather_channels(inputs_planes)

    weight_grid = weight.reshape(3, 9, channels_in, block_out)
    forward_weight = jnp.transpose(weight_grid, (0, 1, 3, 2)).reshape(3, 9 * block_out, channels_in)
    in_plane = None
    for depth_index in range(3):
        part = jnp.einsum(
            "ki,zin->zkn",
            forward_weight[depth_index],
            gathered,
            preferred_element_type=jnp.float32,
        )
        part = jnp.pad(part, ((2 - depth_index, depth_index), (0, 0), (0, 0)))
        in_plane = part if in_plane is None else in_plane + part
    in_plane = in_plane.reshape(depth_cells + 2, 9, block_out, plane_cells)
    forward = None
    for shift_index, (row_step, column_step) in enumerate(plane_offsets):
        term = shift_cells(in_plane[:, shift_index], row_step, column_step)
        forward = term if forward is None else forward + term
    space_devices = lax.axis_size("space")
    up = [(i, i + 1) for i in range(space_devices - 1)]
    down = [(i + 1, i) for i in range(space_devices - 1)]
    from_below = lax.ppermute(forward[depth_cells + 1 :], "space", up)
    from_above = lax.ppermute(forward[:1], "space", down)
    forward = forward[1 : depth_cells + 1] + jnp.concatenate(
        [from_below, jnp.zeros((depth_cells - 2, block_out, plane_cells), jnp.float32), from_above]
    )
    outputs = jnp.transpose(
        (forward + bias_term[None, :, None]).astype(jnp.bfloat16), (1, 0, 2)
    )

    grad_rimmed = padded_2(grad_planes, (("space", 0),), 1)
    grad_shifted = jnp.stack(
        [shift_cells(grad_rimmed, -row_step, -column_step) for row_step, column_step in plane_offsets],
        axis=1,
    ).reshape(depth_cells + 2, 9 * block_out, plane_cells)
    weight_part = jnp.stack(
        [
            jnp.einsum(
                "zkn,zin->ki",
                grad_shifted[2 - depth_index : 2 - depth_index + depth_cells],
                gathered,
                preferred_element_type=jnp.float32,
            )
            for depth_index in range(3)
        ]
    ).reshape(taps_total * block_out, channels_in)
    bias_part = jnp.sum(output_grad.astype(jnp.float32), axis=(1, 2))
    unit = 8 * space_devices
    total_rows = -(-(taps_total * block_out + 1) // unit) * unit
    bias_rows = jnp.zeros((total_rows - taps_total * block_out, channels_in), jnp.float32)
    bias_rows = bias_rows.at[0, :block_out].set(bias_part)
    reduced = all_reduce_rows(
        jnp.concatenate([weight_part, bias_rows]) * grad_scale, "space"
    )
    weight_grad = jnp.transpose(
        reduced[: taps_total * block_out].reshape(taps_total, block_out, channels_in), (0, 2, 1)
    )
    bias_grad = reduced[taps_total * block_out, :block_out]

    chan_devices = lax.axis_size("chips") * lax.axis_size("core")
    backward_weight = jnp.transpose(weight_grid, (0, 2, 1, 3)).reshape(
        3, chan_devices, channels_in // chan_devices, 9 * block_out
    )
    spread = None
    for depth_index in range(3):
        part = jnp.einsum(
            "bjk,zkn->bjzn",
            backward_weight[depth_index],
            grad_shifted[2 - depth_index : 2 - depth_index + depth_cells],
            preferred_element_type=jnp.float32,
        )
        spread = part if spread is None else spread + part
    summed = scatter_channels(spread.reshape(chan_devices, channels_in // chan_devices, depth_cells * plane_cells))
    input_grad = summed.astype(jnp.bfloat16).reshape(block_in, depth_cells, plane_cells)
    return (outputs, input_grad, weight_grad, bias_grad)


def solution(mesh):
    space_devices, chan_devices = mesh.shape["space"], mesh.shape["chan"]
    split = Mesh(mesh.devices.reshape(space_devices, chan_devices // 2, 2), ("space", "chips", "core"))
    chan = ("chips", "core")
    placed = (P(chan, "space", None), P(None, None, chan), P(chan), P(chan, "space", None))
    return jax.shard_map(
        body,
        mesh=split,
        in_specs=placed,
        out_specs=(
            P(chan, "space", None),
            P(chan, "space", None),
            P(None, None, chan),
            P(chan),
        ),
        check_vma=False,
    )
```

```python
import math

import jax
import jax.numpy as jnp
from jax import lax
from jax.sharding import PartitionSpec as P

W = 64


tap_offsets = tuple(
    (
        (depth_step, row_step, column_step)
        for depth_step in (-1, 0, 1)
        for row_step in (-1, 0, 1)
        for column_step in (-1, 0, 1)
    )
)


def padded_2(array, sides, width):
    for axis, dim in sides:
        devices, length = (lax.axis_size(axis), array.shape[dim])
        up = [(i, (i + 1) % devices) for i in range(devices - 1)]
        down = [(j, i) for i, j in up]
        last = lax.slice_in_dim(array, length - width, length, axis=dim)
        first = lax.slice_in_dim(array, 0, width, axis=dim)
        before = lax.ppermute(last, axis, up)
        after = lax.ppermute(first, axis, down)
        array = jnp.concatenate([before, array, after], axis=dim)
    return array


def shift_cells(field, row_step, column_step):
    length_flat = field.shape[-1]
    pad_width = W + 1
    widths = [(0, 0)] * (field.ndim - 1) + [(pad_width, pad_width)]
    padded = jnp.pad(field, widths)
    first_index = pad_width + row_step * W + column_step
    shifted = lax.slice_in_dim(padded, first_index, first_index + length_flat, axis=field.ndim - 1)
    column = jnp.arange(length_flat, dtype=jnp.int32) % W
    inside = (column + column_step >= 0) & (column + column_step < W)
    return jnp.where(inside, shifted, jnp.zeros_like(shifted))


def outer_planes(field):
    return jnp.concatenate([field[:, :1], field[:, -1:]], axis=1)


def attach_rims(field, rims):
    return jnp.concatenate([rims[:, :1], field, rims[:, 3:]], axis=1)


def all_reduce_rows(block, axis):
    devices = lax.axis_size(axis)
    steps = devices.bit_length() - 1
    assert 1 << steps == devices
    current = block
    index = lax.axis_index(axis)
    for step in range(steps):
        half = current.shape[0] // 2
        bit = (index >> step) & 1
        keep = lax.dynamic_slice_in_dim(current, bit * half, half)
        send = lax.dynamic_slice_in_dim(current, (1 - bit) * half, half)
        pairs = [(i, i ^ (1 << step)) for i in range(devices)]
        current = keep + lax.ppermute(send, axis, pairs)
    for step in reversed(range(steps)):
        half = current.shape[0]
        bit = (index >> step) & 1
        pairs = [(i, i ^ (1 << step)) for i in range(devices)]
        other = lax.ppermute(current, axis, pairs)
        both = jnp.zeros((2 * half,) + current.shape[1:], current.dtype)
        both = lax.dynamic_update_slice_in_dim(both, current, bit * half, 0)
        current = lax.dynamic_update_slice_in_dim(both, other, (1 - bit) * half, 0)
    return current


def shift_volume(field, row_step, column_step, rows):
    length_flat = field.shape[-1]
    pad_width = W + 1
    widths = [(0, 0)] * (field.ndim - 1) + [(pad_width, pad_width)]
    padded = jnp.pad(field, widths)
    first_index = pad_width + row_step * W + column_step
    shifted = lax.slice_in_dim(padded, first_index, first_index + length_flat, axis=field.ndim - 1)
    cell = jnp.arange(length_flat, dtype=jnp.int32)
    column = cell % W
    row = (cell // W) % rows
    inside = (column + column_step >= 0) & (column + column_step < W)
    inside = inside & (row + row_step >= 0) & (row + row_step < rows)
    return jnp.where(inside, shifted, jnp.zeros_like(shifted))


plane_offsets = tuple((row_step, column_step) for row_step in (-1, 0, 1) for column_step in (-1, 0, 1))


def all_reduce_direct(block, axis):
    devices = lax.axis_size(axis)
    index = lax.axis_index(axis)
    chunks = block.reshape((devices, block.shape[0] // devices) + block.shape[1:])
    reduced = lax.dynamic_index_in_dim(chunks, index, 0, keepdims=False)
    for distance in range(1, devices):
        pairs = [(i, i ^ distance) for i in range(devices)]
        send = lax.dynamic_index_in_dim(chunks, index ^ distance, 0, keepdims=False)
        reduced = reduced + lax.ppermute(send, axis, pairs)
    pieces = [reduced] + [
        lax.ppermute(reduced, axis, [(i, i ^ distance) for i in range(devices)])
        for distance in range(1, devices)
    ]
    stacked = jnp.stack(pieces)
    return jnp.concatenate(
        [lax.dynamic_index_in_dim(stacked, index ^ chunk, 0, keepdims=False) for chunk in range(devices)]
    )


def body(inputs, weight, bias_term, output_grad):
    taps_total = weight.shape[0]
    channels_in = weight.shape[1]
    block_out = weight.shape[2]
    block_in = inputs.shape[0]
    depth_cells = inputs.shape[1]
    plane_cells = inputs.shape[2]
    grad_scale = 1.0 / math.sqrt(lax.axis_size("space") * depth_cells * plane_cells)
    inputs_planes = jnp.transpose(inputs, (1, 0, 2))
    grad_planes = jnp.transpose(output_grad, (1, 0, 2))
    gathered = lax.all_gather(inputs_planes, "chan", axis=1, tiled=True)

    weight_grid = weight.reshape(3, 9, channels_in, block_out)
    forward_weight = jnp.transpose(weight_grid, (0, 1, 3, 2)).reshape(3, 9 * block_out, channels_in)
    in_plane = None
    for depth_index in range(3):
        part = jnp.einsum(
            "ki,zin->zkn",
            forward_weight[depth_index],
            gathered,
            preferred_element_type=jnp.float32,
        )
        part = jnp.pad(part, ((2 - depth_index, depth_index), (0, 0), (0, 0)))
        in_plane = part if in_plane is None else in_plane + part
    in_plane = in_plane.reshape(depth_cells + 2, 9, block_out, plane_cells)
    forward = None
    for shift_index, (row_step, column_step) in enumerate(plane_offsets):
        term = shift_cells(in_plane[:, shift_index], row_step, column_step)
        forward = term if forward is None else forward + term
    space_devices = lax.axis_size("space")
    up = [(i, i + 1) for i in range(space_devices - 1)]
    down = [(i + 1, i) for i in range(space_devices - 1)]
    from_below = lax.ppermute(forward[depth_cells + 1 :], "space", up)
    from_above = lax.ppermute(forward[:1], "space", down)
    forward = forward[1 : depth_cells + 1] + jnp.concatenate(
        [from_below, jnp.zeros((depth_cells - 2, block_out, plane_cells), jnp.float32), from_above]
    )
    outputs = jnp.transpose(
        (forward + bias_term[None, :, None]).astype(jnp.bfloat16), (1, 0, 2)
    )

    grad_rimmed = padded_2(grad_planes, (("space", 0),), 1)
    grad_shifted = jnp.stack(
        [shift_cells(grad_rimmed, -row_step, -column_step) for row_step, column_step in plane_offsets],
        axis=1,
    ).reshape(depth_cells + 2, 9 * block_out, plane_cells)
    weight_part = jnp.stack(
        [
            jnp.einsum(
                "zkn,zin->ki",
                grad_shifted[2 - depth_index : 2 - depth_index + depth_cells],
                gathered,
                preferred_element_type=jnp.float32,
            )
            for depth_index in range(3)
        ]
    ).reshape(taps_total * block_out, channels_in)
    bias_part = jnp.sum(output_grad.astype(jnp.float32), axis=(1, 2))
    unit = 8 * space_devices
    total_rows = -(-(taps_total * block_out + 1) // unit) * unit
    bias_rows = jnp.zeros((total_rows - taps_total * block_out, channels_in), jnp.float32)
    bias_rows = bias_rows.at[0, :block_out].set(bias_part)
    space_reduce = all_reduce_direct if space_devices <= 4 else all_reduce_rows
    reduced = space_reduce(jnp.concatenate([weight_part, bias_rows]) * grad_scale, "space")
    weight_grad = jnp.transpose(
        reduced[: taps_total * block_out].reshape(taps_total, block_out, channels_in), (0, 2, 1)
    )
    bias_grad = reduced[taps_total * block_out, :block_out]

    chan_devices = lax.axis_size("chan")
    backward_weight = jnp.transpose(weight_grid, (0, 2, 1, 3)).reshape(
        3, chan_devices, channels_in // chan_devices, 9 * block_out
    )
    spread = None
    for depth_index in range(3):
        part = jnp.einsum(
            "bjk,zkn->bjzn",
            backward_weight[depth_index],
            grad_shifted[2 - depth_index : 2 - depth_index + depth_cells],
            preferred_element_type=jnp.float32,
        )
        spread = part if spread is None else spread + part
    summed = lax.psum_scatter(
        spread.reshape(channels_in, depth_cells * plane_cells), "chan", scatter_dimension=0, tiled=True
    )
    input_grad = summed.astype(jnp.bfloat16).reshape(block_in, depth_cells, plane_cells)
    return (outputs, input_grad, weight_grad, bias_grad)


def solution(mesh):
    placed = (P("chan", "space", None), P(None, None, "chan"), P("chan"), P("chan", "space", None))
    return jax.shard_map(
        body,
        mesh=mesh,
        in_specs=placed,
        out_specs=(
            P("chan", "space", None),
            P("chan", "space", None),
            P(None, None, "chan"),
            P("chan"),
        ),
        check_vma=False,
    )
```

```python
import math

import jax
import jax.numpy as jnp
from jax import lax
from jax.sharding import PartitionSpec as P

W = 64


tap_offsets = tuple(
    (
        (depth_step, row_step, column_step)
        for depth_step in (-1, 0, 1)
        for row_step in (-1, 0, 1)
        for column_step in (-1, 0, 1)
    )
)


def padded_2(array, sides, width):
    for axis, dim in sides:
        devices, length = (lax.axis_size(axis), array.shape[dim])
        up = [(i, (i + 1) % devices) for i in range(devices - 1)]
        down = [(j, i) for i, j in up]
        last = lax.slice_in_dim(array, length - width, length, axis=dim)
        first = lax.slice_in_dim(array, 0, width, axis=dim)
        before = lax.ppermute(last, axis, up)
        after = lax.ppermute(first, axis, down)
        array = jnp.concatenate([before, array, after], axis=dim)
    return array


def shift_cells(field, row_step, column_step):
    length_flat = field.shape[-1]
    pad_width = W + 1
    widths = [(0, 0)] * (field.ndim - 1) + [(pad_width, pad_width)]
    padded = jnp.pad(field, widths)
    first_index = pad_width + row_step * W + column_step
    shifted = lax.slice_in_dim(padded, first_index, first_index + length_flat, axis=field.ndim - 1)
    column = jnp.arange(length_flat, dtype=jnp.int32) % W
    inside = (column + column_step >= 0) & (column + column_step < W)
    return jnp.where(inside, shifted, jnp.zeros_like(shifted))


def outer_planes(field):
    return jnp.concatenate([field[:, :1], field[:, -1:]], axis=1)


def attach_rims(field, rims):
    return jnp.concatenate([rims[:, :1], field, rims[:, 3:]], axis=1)


def all_reduce_rows(block, axis):
    devices = lax.axis_size(axis)
    steps = devices.bit_length() - 1
    assert 1 << steps == devices
    current = block
    index = lax.axis_index(axis)
    for step in range(steps):
        half = current.shape[0] // 2
        bit = (index >> step) & 1
        keep = lax.dynamic_slice_in_dim(current, bit * half, half)
        send = lax.dynamic_slice_in_dim(current, (1 - bit) * half, half)
        pairs = [(i, i ^ (1 << step)) for i in range(devices)]
        current = keep + lax.ppermute(send, axis, pairs)
    for step in reversed(range(steps)):
        half = current.shape[0]
        bit = (index >> step) & 1
        pairs = [(i, i ^ (1 << step)) for i in range(devices)]
        other = lax.ppermute(current, axis, pairs)
        both = jnp.zeros((2 * half,) + current.shape[1:], current.dtype)
        both = lax.dynamic_update_slice_in_dim(both, current, bit * half, 0)
        current = lax.dynamic_update_slice_in_dim(both, other, (1 - bit) * half, 0)
    return current


def shift_volume(field, row_step, column_step, rows):
    length_flat = field.shape[-1]
    pad_width = W + 1
    widths = [(0, 0)] * (field.ndim - 1) + [(pad_width, pad_width)]
    padded = jnp.pad(field, widths)
    first_index = pad_width + row_step * W + column_step
    shifted = lax.slice_in_dim(padded, first_index, first_index + length_flat, axis=field.ndim - 1)
    cell = jnp.arange(length_flat, dtype=jnp.int32)
    column = cell % W
    row = (cell // W) % rows
    inside = (column + column_step >= 0) & (column + column_step < W)
    inside = inside & (row + row_step >= 0) & (row + row_step < rows)
    return jnp.where(inside, shifted, jnp.zeros_like(shifted))


plane_offsets = tuple((row_step, column_step) for row_step in (-1, 0, 1) for column_step in (-1, 0, 1))


def all_reduce_direct(block, axis):
    devices = lax.axis_size(axis)
    index = lax.axis_index(axis)
    chunks = block.reshape((devices, block.shape[0] // devices) + block.shape[1:])
    reduced = lax.dynamic_index_in_dim(chunks, index, 0, keepdims=False)
    for distance in range(1, devices):
        pairs = [(i, i ^ distance) for i in range(devices)]
        send = lax.dynamic_index_in_dim(chunks, index ^ distance, 0, keepdims=False)
        reduced = reduced + lax.ppermute(send, axis, pairs)
    pieces = [reduced] + [
        lax.ppermute(reduced, axis, [(i, i ^ distance) for i in range(devices)])
        for distance in range(1, devices)
    ]
    stacked = jnp.stack(pieces)
    return jnp.concatenate(
        [lax.dynamic_index_in_dim(stacked, index ^ chunk, 0, keepdims=False) for chunk in range(devices)]
    )


def shift_sum(stacked, steps_sign):
    total = None
    for shift_index, (row_step, column_step) in enumerate(plane_offsets):
        term = shift_cells(stacked[:, shift_index], steps_sign * row_step, steps_sign * column_step)
        total = term if total is None else total + term
    return total


def depth_products(weights, planes, toward_output):
    total = None
    for depth_index in range(3):
        part = jnp.einsum("ki,zin->zkn", weights[depth_index], planes, preferred_element_type=jnp.float32)
        front = 2 - depth_index if toward_output else depth_index
        part = jnp.pad(part, ((front, 2 - front), (0, 0), (0, 0)))
        total = part if total is None else total + part
    return total


def settle_rims(field):
    depth = field.shape[0] - 2
    space_devices = lax.axis_size("space")
    up = [(i, i + 1) for i in range(space_devices - 1)]
    down = [(i + 1, i) for i in range(space_devices - 1)]
    from_below = lax.ppermute(field[depth + 1 :], "space", up)
    from_above = lax.ppermute(field[:1], "space", down)
    return field[1 : depth + 1] + jnp.concatenate(
        [from_below, jnp.zeros((depth - 2,) + field.shape[1:], field.dtype), from_above]
    )


def body(inputs, weight, bias_term, output_grad):
    taps_total = weight.shape[0]
    channels_in = weight.shape[1]
    block_out = weight.shape[2]
    block_in = inputs.shape[0]
    depth_cells = inputs.shape[1]
    plane_cells = inputs.shape[2]
    grad_scale = 1.0 / math.sqrt(lax.axis_size("space") * depth_cells * plane_cells)
    inputs_planes = jnp.transpose(inputs, (1, 0, 2))
    grad_planes = jnp.transpose(output_grad, (1, 0, 2))
    both = lax.all_gather(jnp.concatenate([inputs_planes, grad_planes]), "chan", axis=1, tiled=True)
    gathered = both[:depth_cells]
    grad_gathered = both[depth_cells:]
    weight_rows = lax.all_to_all(weight, "chan", 1, 2, tiled=True)

    weight_grid = weight.reshape(3, 9, channels_in, block_out)
    forward_weight = jnp.transpose(weight_grid, (0, 1, 3, 2)).reshape(3, 9 * block_out, channels_in)
    forward = shift_sum(
        depth_products(forward_weight, gathered, True).reshape(depth_cells + 2, 9, block_out, plane_cells), 1
    )
    forward = settle_rims(forward)
    outputs = jnp.transpose(
        (forward + bias_term[None, :, None]).astype(jnp.bfloat16), (1, 0, 2)
    )

    grad_rimmed = padded_2(grad_planes, (("space", 0),), 1)
    grad_shifted = jnp.stack(
        [shift_cells(grad_rimmed, -row_step, -column_step) for row_step, column_step in plane_offsets],
        axis=1,
    ).reshape(depth_cells + 2, 9 * block_out, plane_cells)
    weight_part = jnp.stack(
        [
            jnp.einsum(
                "zkn,zin->ki",
                grad_shifted[2 - depth_index : 2 - depth_index + depth_cells],
                gathered,
                preferred_element_type=jnp.float32,
            )
            for depth_index in range(3)
        ]
    ).reshape(taps_total * block_out, channels_in)
    bias_part = jnp.sum(output_grad.astype(jnp.float32), axis=(1, 2))
    space_devices = lax.axis_size("space")
    unit = 8 * space_devices
    total_rows = -(-(taps_total * block_out + 1) // unit) * unit
    bias_rows = jnp.zeros((total_rows - taps_total * block_out, channels_in), jnp.float32)
    bias_rows = bias_rows.at[0, :block_out].set(bias_part)
    space_reduce = all_reduce_direct if space_devices <= 4 else all_reduce_rows
    reduced = space_reduce(jnp.concatenate([weight_part, bias_rows]) * grad_scale, "space")
    weight_grad = jnp.transpose(
        reduced[: taps_total * block_out].reshape(taps_total, block_out, channels_in), (0, 2, 1)
    )
    bias_grad = reduced[taps_total * block_out, :block_out]

    channels_out = weight_rows.shape[2]
    backward_weight = weight_rows.reshape(3, 9 * block_in, channels_out)
    spread = shift_sum(
        depth_products(backward_weight, grad_gathered, False).reshape(depth_cells + 2, 9, block_in, plane_cells), -1
    )
    spread = settle_rims(spread)
    input_grad = jnp.transpose(spread.astype(jnp.bfloat16), (1, 0, 2))
    return (outputs, input_grad, weight_grad, bias_grad)


def solution(mesh):
    placed = (P("chan", "space", None), P(None, None, "chan"), P("chan"), P("chan", "space", None))
    return jax.shard_map(
        body,
        mesh=mesh,
        in_specs=placed,
        out_specs=(
            P("chan", "space", None),
            P("chan", "space", None),
            P(None, None, "chan"),
            P("chan"),
        ),
        check_vma=False,
    )
```

```python
import math

import jax
import jax.numpy as jnp
from jax import lax
from jax.sharding import PartitionSpec as P

W = 64


tap_offsets = tuple(
    (
        (depth_step, row_step, column_step)
        for depth_step in (-1, 0, 1)
        for row_step in (-1, 0, 1)
        for column_step in (-1, 0, 1)
    )
)


def padded_2(array, sides, width):
    for axis, dim in sides:
        devices, length = (lax.axis_size(axis), array.shape[dim])
        up = [(i, (i + 1) % devices) for i in range(devices - 1)]
        down = [(j, i) for i, j in up]
        last = lax.slice_in_dim(array, length - width, length, axis=dim)
        first = lax.slice_in_dim(array, 0, width, axis=dim)
        before = lax.ppermute(last, axis, up)
        after = lax.ppermute(first, axis, down)
        array = jnp.concatenate([before, array, after], axis=dim)
    return array


def shift_cells(field, row_step, column_step):
    length_flat = field.shape[-1]
    pad_width = W + 1
    widths = [(0, 0)] * (field.ndim - 1) + [(pad_width, pad_width)]
    padded = jnp.pad(field, widths)
    first_index = pad_width + row_step * W + column_step
    shifted = lax.slice_in_dim(padded, first_index, first_index + length_flat, axis=field.ndim - 1)
    column = jnp.arange(length_flat, dtype=jnp.int32) % W
    inside = (column + column_step >= 0) & (column + column_step < W)
    return jnp.where(inside, shifted, jnp.zeros_like(shifted))


def outer_planes(field):
    return jnp.concatenate([field[:, :1], field[:, -1:]], axis=1)


def attach_rims(field, rims):
    return jnp.concatenate([rims[:, :1], field, rims[:, 3:]], axis=1)


def all_reduce_rows(block, axis):
    devices = lax.axis_size(axis)
    steps = devices.bit_length() - 1
    assert 1 << steps == devices
    current = block
    index = lax.axis_index(axis)
    for step in range(steps):
        half = current.shape[0] // 2
        bit = (index >> step) & 1
        keep = lax.dynamic_slice_in_dim(current, bit * half, half)
        send = lax.dynamic_slice_in_dim(current, (1 - bit) * half, half)
        pairs = [(i, i ^ (1 << step)) for i in range(devices)]
        current = keep + lax.ppermute(send, axis, pairs)
    for step in reversed(range(steps)):
        half = current.shape[0]
        bit = (index >> step) & 1
        pairs = [(i, i ^ (1 << step)) for i in range(devices)]
        other = lax.ppermute(current, axis, pairs)
        both = jnp.zeros((2 * half,) + current.shape[1:], current.dtype)
        both = lax.dynamic_update_slice_in_dim(both, current, bit * half, 0)
        current = lax.dynamic_update_slice_in_dim(both, other, (1 - bit) * half, 0)
    return current


def shift_volume(field, row_step, column_step, rows):
    length_flat = field.shape[-1]
    pad_width = W + 1
    widths = [(0, 0)] * (field.ndim - 1) + [(pad_width, pad_width)]
    padded = jnp.pad(field, widths)
    first_index = pad_width + row_step * W + column_step
    shifted = lax.slice_in_dim(padded, first_index, first_index + length_flat, axis=field.ndim - 1)
    cell = jnp.arange(length_flat, dtype=jnp.int32)
    column = cell % W
    row = (cell // W) % rows
    inside = (column + column_step >= 0) & (column + column_step < W)
    inside = inside & (row + row_step >= 0) & (row + row_step < rows)
    return jnp.where(inside, shifted, jnp.zeros_like(shifted))


plane_offsets = tuple((row_step, column_step) for row_step in (-1, 0, 1) for column_step in (-1, 0, 1))


def all_reduce_direct(block, axis):
    devices = lax.axis_size(axis)
    index = lax.axis_index(axis)
    chunks = block.reshape((devices, block.shape[0] // devices) + block.shape[1:])
    reduced = lax.dynamic_index_in_dim(chunks, index, 0, keepdims=False)
    for distance in range(1, devices):
        pairs = [(i, i ^ distance) for i in range(devices)]
        send = lax.dynamic_index_in_dim(chunks, index ^ distance, 0, keepdims=False)
        reduced = reduced + lax.ppermute(send, axis, pairs)
    pieces = [reduced] + [
        lax.ppermute(reduced, axis, [(i, i ^ distance) for i in range(devices)])
        for distance in range(1, devices)
    ]
    stacked = jnp.stack(pieces)
    return jnp.concatenate(
        [lax.dynamic_index_in_dim(stacked, index ^ chunk, 0, keepdims=False) for chunk in range(devices)]
    )


def shift_sum(stacked, steps_sign):
    total = None
    for shift_index, (row_step, column_step) in enumerate(plane_offsets):
        term = shift_cells(stacked[:, shift_index], steps_sign * row_step, steps_sign * column_step)
        total = term if total is None else total + term
    return total


def depth_products(weights, planes, toward_output):
    total = None
    for depth_index in range(3):
        part = jnp.einsum("ki,zin->zkn", weights[depth_index], planes, preferred_element_type=jnp.float32)
        front = 2 - depth_index if toward_output else depth_index
        part = jnp.pad(part, ((front, 2 - front), (0, 0), (0, 0)))
        total = part if total is None else total + part
    return total


def settle_rims(field):
    depth = field.shape[0] - 2
    space_devices = lax.axis_size("space")
    up = [(i, i + 1) for i in range(space_devices - 1)]
    down = [(i + 1, i) for i in range(space_devices - 1)]
    from_below = lax.ppermute(field[depth + 1 :], "space", up)
    from_above = lax.ppermute(field[:1], "space", down)
    return field[1 : depth + 1] + jnp.concatenate(
        [from_below, jnp.zeros((depth - 2,) + field.shape[1:], field.dtype), from_above]
    )


def body(inputs, weight, bias_term, output_grad):
    taps_total = weight.shape[0]
    channels_in = weight.shape[1]
    block_out = weight.shape[2]
    block_in = inputs.shape[0]
    depth_cells = inputs.shape[1]
    plane_cells = inputs.shape[2]
    grad_scale = 1.0 / math.sqrt(lax.axis_size("space") * depth_cells * plane_cells)
    inputs_planes = jnp.transpose(inputs, (1, 0, 2))
    grad_planes = jnp.transpose(output_grad, (1, 0, 2))
    gathered = lax.all_gather(inputs_planes, "chan", axis=1, tiled=True)
    grad_gathered = lax.all_gather(grad_planes, "chan", axis=1, tiled=True)
    weight_rows = lax.all_to_all(weight, "chan", 1, 2, tiled=True)

    weight_grid = weight.reshape(3, 9, channels_in, block_out)
    forward_weight = jnp.transpose(weight_grid, (0, 1, 3, 2)).reshape(3, 9 * block_out, channels_in)
    forward = shift_sum(
        depth_products(forward_weight, gathered, True).reshape(depth_cells + 2, 9, block_out, plane_cells), 1
    )
    forward = settle_rims(forward)
    outputs = jnp.transpose(
        (forward + bias_term[None, :, None]).astype(jnp.bfloat16), (1, 0, 2)
    )

    grad_rimmed = padded_2(grad_planes, (("space", 0),), 1)
    grad_shifted = jnp.stack(
        [shift_cells(grad_rimmed, -row_step, -column_step) for row_step, column_step in plane_offsets],
        axis=1,
    ).reshape(depth_cells + 2, 9 * block_out, plane_cells)
    weight_part = jnp.stack(
        [
            jnp.einsum(
                "zkn,zin->ki",
                grad_shifted[2 - depth_index : 2 - depth_index + depth_cells],
                gathered,
                preferred_element_type=jnp.float32,
            )
            for depth_index in range(3)
        ]
    ).reshape(taps_total * block_out, channels_in)
    bias_part = jnp.sum(output_grad.astype(jnp.float32), axis=(1, 2))
    space_devices = lax.axis_size("space")
    unit = 8 * space_devices
    total_rows = -(-(taps_total * block_out + 1) // unit) * unit
    bias_rows = jnp.zeros((total_rows - taps_total * block_out, channels_in), jnp.float32)
    bias_rows = bias_rows.at[0, :block_out].set(bias_part)
    space_reduce = all_reduce_direct if space_devices <= 4 else all_reduce_rows
    reduced = space_reduce(jnp.concatenate([weight_part, bias_rows]) * grad_scale, "space")
    weight_grad = jnp.transpose(
        reduced[: taps_total * block_out].reshape(taps_total, block_out, channels_in), (0, 2, 1)
    )
    bias_grad = reduced[taps_total * block_out, :block_out]

    channels_out = weight_rows.shape[2]
    backward_weight = weight_rows.reshape(3, 9 * block_in, channels_out)
    spread = shift_sum(
        depth_products(backward_weight, grad_gathered, False).reshape(depth_cells + 2, 9, block_in, plane_cells), -1
    )
    spread = settle_rims(spread)
    input_grad = jnp.transpose(spread.astype(jnp.bfloat16), (1, 0, 2))
    return (outputs, input_grad, weight_grad, bias_grad)


def solution(mesh):
    placed = (P("chan", "space", None), P(None, None, "chan"), P("chan"), P("chan", "space", None))
    return jax.shard_map(
        body,
        mesh=mesh,
        in_specs=placed,
        out_specs=(
            P("chan", "space", None),
            P("chan", "space", None),
            P(None, None, "chan"),
            P("chan"),
        ),
        check_vma=False,
    )
```

```python
import math

import jax
import jax.numpy as jnp
from jax import lax
from jax.sharding import Mesh, PartitionSpec as P

W = 64


tap_offsets = tuple(
    (
        (depth_step, row_step, column_step)
        for depth_step in (-1, 0, 1)
        for row_step in (-1, 0, 1)
        for column_step in (-1, 0, 1)
    )
)


def padded_2(array, sides, width):
    for axis, dim in sides:
        devices, length = (lax.axis_size(axis), array.shape[dim])
        up = [(i, (i + 1) % devices) for i in range(devices - 1)]
        down = [(j, i) for i, j in up]
        last = lax.slice_in_dim(array, length - width, length, axis=dim)
        first = lax.slice_in_dim(array, 0, width, axis=dim)
        before = lax.ppermute(last, axis, up)
        after = lax.ppermute(first, axis, down)
        array = jnp.concatenate([before, array, after], axis=dim)
    return array


def shift_cells(field, row_step, column_step):
    length_flat = field.shape[-1]
    pad_width = W + 1
    widths = [(0, 0)] * (field.ndim - 1) + [(pad_width, pad_width)]
    padded = jnp.pad(field, widths)
    first_index = pad_width + row_step * W + column_step
    shifted = lax.slice_in_dim(padded, first_index, first_index + length_flat, axis=field.ndim - 1)
    column = jnp.arange(length_flat, dtype=jnp.int32) % W
    inside = (column + column_step >= 0) & (column + column_step < W)
    return jnp.where(inside, shifted, jnp.zeros_like(shifted))


def outer_planes(field):
    return jnp.concatenate([field[:, :1], field[:, -1:]], axis=1)


def attach_rims(field, rims):
    return jnp.concatenate([rims[:, :1], field, rims[:, 3:]], axis=1)


def all_reduce_rows(block, axis):
    devices = lax.axis_size(axis)
    steps = devices.bit_length() - 1
    assert 1 << steps == devices
    current = block
    index = lax.axis_index(axis)
    for step in range(steps):
        half = current.shape[0] // 2
        bit = (index >> step) & 1
        keep = lax.dynamic_slice_in_dim(current, bit * half, half)
        send = lax.dynamic_slice_in_dim(current, (1 - bit) * half, half)
        pairs = [(i, i ^ (1 << step)) for i in range(devices)]
        current = keep + lax.ppermute(send, axis, pairs)
    for step in reversed(range(steps)):
        half = current.shape[0]
        bit = (index >> step) & 1
        pairs = [(i, i ^ (1 << step)) for i in range(devices)]
        other = lax.ppermute(current, axis, pairs)
        both = jnp.zeros((2 * half,) + current.shape[1:], current.dtype)
        both = lax.dynamic_update_slice_in_dim(both, current, bit * half, 0)
        current = lax.dynamic_update_slice_in_dim(both, other, (1 - bit) * half, 0)
    return current


def shift_volume(field, row_step, column_step, rows):
    length_flat = field.shape[-1]
    pad_width = W + 1
    widths = [(0, 0)] * (field.ndim - 1) + [(pad_width, pad_width)]
    padded = jnp.pad(field, widths)
    first_index = pad_width + row_step * W + column_step
    shifted = lax.slice_in_dim(padded, first_index, first_index + length_flat, axis=field.ndim - 1)
    cell = jnp.arange(length_flat, dtype=jnp.int32)
    column = cell % W
    row = (cell // W) % rows
    inside = (column + column_step >= 0) & (column + column_step < W)
    inside = inside & (row + row_step >= 0) & (row + row_step < rows)
    return jnp.where(inside, shifted, jnp.zeros_like(shifted))


plane_offsets = tuple((row_step, column_step) for row_step in (-1, 0, 1) for column_step in (-1, 0, 1))


def all_reduce_direct(block, axis):
    devices = lax.axis_size(axis)
    index = lax.axis_index(axis)
    chunks = block.reshape((devices, block.shape[0] // devices) + block.shape[1:])
    reduced = lax.dynamic_index_in_dim(chunks, index, 0, keepdims=False)
    for distance in range(1, devices):
        pairs = [(i, i ^ distance) for i in range(devices)]
        send = lax.dynamic_index_in_dim(chunks, index ^ distance, 0, keepdims=False)
        reduced = reduced + lax.ppermute(send, axis, pairs)
    pieces = [reduced] + [
        lax.ppermute(reduced, axis, [(i, i ^ distance) for i in range(devices)])
        for distance in range(1, devices)
    ]
    stacked = jnp.stack(pieces)
    return jnp.concatenate(
        [lax.dynamic_index_in_dim(stacked, index ^ chunk, 0, keepdims=False) for chunk in range(devices)]
    )


def scatter_channels(blocks):
    by_core = blocks.reshape(-1, 2, blocks.shape[1], blocks.shape[2])
    core = lax.axis_index("core")
    keep = lax.dynamic_index_in_dim(by_core, core, axis=1, keepdims=False)
    send = lax.dynamic_index_in_dim(by_core, 1 - core, axis=1, keepdims=False)
    partial = keep + lax.ppermute(send, "core", [(0, 1), (1, 0)])
    return lax.psum_scatter(
        partial.reshape(-1, blocks.shape[2]), "chips", scatter_dimension=0, tiled=True
    )


def body(inputs, weight, bias_term, output_grad):
    taps_total = weight.shape[0]
    channels_in = weight.shape[1]
    block_out = weight.shape[2]
    block_in = inputs.shape[0]
    depth_cells = inputs.shape[1]
    plane_cells = inputs.shape[2]
    grad_scale = 1.0 / math.sqrt(lax.axis_size("space") * depth_cells * plane_cells)
    inputs_planes = jnp.transpose(inputs, (1, 0, 2))
    grad_planes = jnp.transpose(output_grad, (1, 0, 2))
    gathered = lax.all_gather(inputs_planes, ("chips", "core"), axis=1, tiled=True)

    weight_grid = weight.reshape(3, 9, channels_in, block_out)
    forward_weight = jnp.transpose(weight_grid, (0, 1, 3, 2)).reshape(3, 9 * block_out, channels_in)
    in_plane = None
    for depth_index in range(3):
        part = jnp.einsum(
            "ki,zin->zkn",
            forward_weight[depth_index],
            gathered,
            preferred_element_type=jnp.float32,
        )
        part = jnp.pad(part, ((2 - depth_index, depth_index), (0, 0), (0, 0)))
        in_plane = part if in_plane is None else in_plane + part
    in_plane = in_plane.reshape(depth_cells + 2, 9, block_out, plane_cells)
    forward = None
    for shift_index, (row_step, column_step) in enumerate(plane_offsets):
        term = shift_cells(in_plane[:, shift_index], row_step, column_step)
        forward = term if forward is None else forward + term
    space_devices = lax.axis_size("space")
    up = [(i, i + 1) for i in range(space_devices - 1)]
    down = [(i + 1, i) for i in range(space_devices - 1)]
    from_below = lax.ppermute(forward[depth_cells + 1 :], "space", up)
    from_above = lax.ppermute(forward[:1], "space", down)
    forward = forward[1 : depth_cells + 1] + jnp.concatenate(
        [from_below, jnp.zeros((depth_cells - 2, block_out, plane_cells), jnp.float32), from_above]
    )
    outputs = jnp.transpose(
        (forward + bias_term[None, :, None]).astype(jnp.bfloat16), (1, 0, 2)
    )

    grad_rimmed = padded_2(grad_planes, (("space", 0),), 1)
    grad_shifted = jnp.stack(
        [shift_cells(grad_rimmed, -row_step, -column_step) for row_step, column_step in plane_offsets],
        axis=1,
    ).reshape(depth_cells + 2, 9 * block_out, plane_cells)
    weight_part = jnp.stack(
        [
            jnp.einsum(
                "zkn,zin->ki",
                grad_shifted[2 - depth_index : 2 - depth_index + depth_cells],
                gathered,
                preferred_element_type=jnp.float32,
            )
            for depth_index in range(3)
        ]
    ).reshape(taps_total * block_out, channels_in)
    bias_part = jnp.sum(output_grad.astype(jnp.float32), axis=(1, 2))
    unit = 8 * space_devices
    total_rows = -(-(taps_total * block_out + 1) // unit) * unit
    bias_rows = jnp.zeros((total_rows - taps_total * block_out, channels_in), jnp.float32)
    bias_rows = bias_rows.at[0, :block_out].set(bias_part)
    space_reduce = all_reduce_direct if space_devices <= 4 else all_reduce_rows
    reduced = space_reduce(jnp.concatenate([weight_part, bias_rows]) * grad_scale, "space")
    weight_grad = jnp.transpose(
        reduced[: taps_total * block_out].reshape(taps_total, block_out, channels_in), (0, 2, 1)
    )
    bias_grad = reduced[taps_total * block_out, :block_out]

    chan_devices = lax.axis_size("chips") * lax.axis_size("core")
    backward_weight = jnp.transpose(weight_grid, (0, 2, 1, 3)).reshape(
        3, chan_devices, channels_in // chan_devices, 9 * block_out
    )
    spread = None
    for depth_index in range(3):
        part = jnp.einsum(
            "bjk,zkn->bjzn",
            backward_weight[depth_index],
            grad_shifted[2 - depth_index : 2 - depth_index + depth_cells],
            preferred_element_type=jnp.float32,
        )
        spread = part if spread is None else spread + part
    summed = scatter_channels(spread.reshape(chan_devices, channels_in // chan_devices, depth_cells * plane_cells))
    input_grad = summed.astype(jnp.bfloat16).reshape(block_in, depth_cells, plane_cells)
    return (outputs, input_grad, weight_grad, bias_grad)


def solution(mesh):
    space_devices, chan_devices = mesh.shape["space"], mesh.shape["chan"]
    split = Mesh(mesh.devices.reshape(space_devices, chan_devices // 2, 2), ("space", "chips", "core"))
    chan = ("chips", "core")
    placed = (P(chan, "space", None), P(None, None, chan), P(chan), P(chan, "space", None))
    return jax.shard_map(
        body,
        mesh=split,
        in_specs=placed,
        out_specs=(
            P(chan, "space", None),
            P(chan, "space", None),
            P(None, None, chan),
            P(chan),
        ),
        check_vma=False,
    )
```

```python
import math

import jax
import jax.numpy as jnp
from jax import lax
from jax.sharding import Mesh, PartitionSpec as P

W = 64


tap_offsets = tuple(
    (
        (depth_step, row_step, column_step)
        for depth_step in (-1, 0, 1)
        for row_step in (-1, 0, 1)
        for column_step in (-1, 0, 1)
    )
)


def padded_2(array, sides, width):
    for axis, dim in sides:
        devices, length = (lax.axis_size(axis), array.shape[dim])
        up = [(i, (i + 1) % devices) for i in range(devices - 1)]
        down = [(j, i) for i, j in up]
        last = lax.slice_in_dim(array, length - width, length, axis=dim)
        first = lax.slice_in_dim(array, 0, width, axis=dim)
        before = lax.ppermute(last, axis, up)
        after = lax.ppermute(first, axis, down)
        array = jnp.concatenate([before, array, after], axis=dim)
    return array


def shift_cells(field, row_step, column_step):
    length_flat = field.shape[-1]
    pad_width = W + 1
    widths = [(0, 0)] * (field.ndim - 1) + [(pad_width, pad_width)]
    padded = jnp.pad(field, widths)
    first_index = pad_width + row_step * W + column_step
    shifted = lax.slice_in_dim(padded, first_index, first_index + length_flat, axis=field.ndim - 1)
    column = jnp.arange(length_flat, dtype=jnp.int32) % W
    inside = (column + column_step >= 0) & (column + column_step < W)
    return jnp.where(inside, shifted, jnp.zeros_like(shifted))


def outer_planes(field):
    return jnp.concatenate([field[:, :1], field[:, -1:]], axis=1)


def attach_rims(field, rims):
    return jnp.concatenate([rims[:, :1], field, rims[:, 3:]], axis=1)


def all_reduce_rows(block, axis):
    devices = lax.axis_size(axis)
    steps = devices.bit_length() - 1
    assert 1 << steps == devices
    current = block
    index = lax.axis_index(axis)
    for step in range(steps):
        half = current.shape[0] // 2
        bit = (index >> step) & 1
        keep = lax.dynamic_slice_in_dim(current, bit * half, half)
        send = lax.dynamic_slice_in_dim(current, (1 - bit) * half, half)
        pairs = [(i, i ^ (1 << step)) for i in range(devices)]
        current = keep + lax.ppermute(send, axis, pairs)
    for step in reversed(range(steps)):
        half = current.shape[0]
        bit = (index >> step) & 1
        pairs = [(i, i ^ (1 << step)) for i in range(devices)]
        other = lax.ppermute(current, axis, pairs)
        both = jnp.zeros((2 * half,) + current.shape[1:], current.dtype)
        both = lax.dynamic_update_slice_in_dim(both, current, bit * half, 0)
        current = lax.dynamic_update_slice_in_dim(both, other, (1 - bit) * half, 0)
    return current


def shift_volume(field, row_step, column_step, rows):
    length_flat = field.shape[-1]
    pad_width = W + 1
    widths = [(0, 0)] * (field.ndim - 1) + [(pad_width, pad_width)]
    padded = jnp.pad(field, widths)
    first_index = pad_width + row_step * W + column_step
    shifted = lax.slice_in_dim(padded, first_index, first_index + length_flat, axis=field.ndim - 1)
    cell = jnp.arange(length_flat, dtype=jnp.int32)
    column = cell % W
    row = (cell // W) % rows
    inside = (column + column_step >= 0) & (column + column_step < W)
    inside = inside & (row + row_step >= 0) & (row + row_step < rows)
    return jnp.where(inside, shifted, jnp.zeros_like(shifted))


plane_offsets = tuple((row_step, column_step) for row_step in (-1, 0, 1) for column_step in (-1, 0, 1))


def all_reduce_direct(block, axis):
    devices = lax.axis_size(axis)
    index = lax.axis_index(axis)
    chunks = block.reshape((devices, block.shape[0] // devices) + block.shape[1:])
    reduced = lax.dynamic_index_in_dim(chunks, index, 0, keepdims=False)
    for distance in range(1, devices):
        pairs = [(i, i ^ distance) for i in range(devices)]
        send = lax.dynamic_index_in_dim(chunks, index ^ distance, 0, keepdims=False)
        reduced = reduced + lax.ppermute(send, axis, pairs)
    pieces = [reduced] + [
        lax.ppermute(reduced, axis, [(i, i ^ distance) for i in range(devices)])
        for distance in range(1, devices)
    ]
    stacked = jnp.stack(pieces)
    return jnp.concatenate(
        [lax.dynamic_index_in_dim(stacked, index ^ chunk, 0, keepdims=False) for chunk in range(devices)]
    )


def scatter_channels(blocks):
    by_core = blocks.reshape((-1, 2) + blocks.shape[1:])
    core = lax.axis_index("core")
    keep = lax.dynamic_index_in_dim(by_core, core, axis=1, keepdims=False)
    send = lax.dynamic_index_in_dim(by_core, 1 - core, axis=1, keepdims=False)
    partial = keep + lax.ppermute(send, "core", [(0, 1), (1, 0)])
    return lax.psum_scatter(
        partial.reshape(-1, blocks.shape[-1]), "chips", scatter_dimension=0, tiled=True
    )


def body(inputs, weight, bias_term, output_grad):
    taps_total = weight.shape[0]
    channels_in = weight.shape[1]
    block_out = weight.shape[2]
    block_in = inputs.shape[0]
    depth_cells = inputs.shape[1]
    plane_cells = inputs.shape[2]
    grad_scale = 1.0 / math.sqrt(lax.axis_size("space") * depth_cells * plane_cells)
    inputs_planes = jnp.transpose(inputs, (1, 0, 2))
    grad_planes = jnp.transpose(output_grad, (1, 0, 2))
    gathered = lax.all_gather(inputs_planes, ("chips", "core"), axis=1, tiled=True)

    weight_grid = weight.reshape(3, 9, channels_in, block_out)
    forward_weight = jnp.transpose(weight_grid, (0, 1, 3, 2)).reshape(3, 9 * block_out, channels_in)
    in_plane = None
    for depth_index in range(3):
        part = jnp.einsum(
            "ki,zin->zkn",
            forward_weight[depth_index],
            gathered,
            preferred_element_type=jnp.float32,
        )
        part = jnp.pad(part, ((2 - depth_index, depth_index), (0, 0), (0, 0)))
        in_plane = part if in_plane is None else in_plane + part
    in_plane = in_plane.reshape(depth_cells + 2, 9, block_out, plane_cells)
    forward = None
    for shift_index, (row_step, column_step) in enumerate(plane_offsets):
        term = shift_cells(in_plane[:, shift_index], row_step, column_step)
        forward = term if forward is None else forward + term
    space_devices = lax.axis_size("space")
    up = [(i, i + 1) for i in range(space_devices - 1)]
    down = [(i + 1, i) for i in range(space_devices - 1)]
    from_below = lax.ppermute(forward[depth_cells + 1 :], "space", up)
    from_above = lax.ppermute(forward[:1], "space", down)
    forward = forward[1 : depth_cells + 1] + jnp.concatenate(
        [from_below, jnp.zeros((depth_cells - 2, block_out, plane_cells), jnp.float32), from_above]
    )
    outputs = jnp.transpose(
        (forward + bias_term[None, :, None]).astype(jnp.bfloat16), (1, 0, 2)
    )

    grad_rimmed = padded_2(grad_planes, (("space", 0),), 1)
    grad_shifted = jnp.stack(
        [shift_cells(grad_rimmed, -row_step, -column_step) for row_step, column_step in plane_offsets],
        axis=1,
    ).reshape(depth_cells + 2, 9 * block_out, plane_cells)
    weight_part = jnp.stack(
        [
            jnp.einsum(
                "zkn,zin->ki",
                grad_shifted[2 - depth_index : 2 - depth_index + depth_cells],
                gathered,
                preferred_element_type=jnp.float32,
            )
            for depth_index in range(3)
        ]
    ).reshape(taps_total * block_out, channels_in)
    bias_part = jnp.sum(output_grad.astype(jnp.float32), axis=(1, 2))
    unit = 8 * space_devices
    total_rows = -(-(taps_total * block_out + 1) // unit) * unit
    bias_rows = jnp.zeros((total_rows - taps_total * block_out, channels_in), jnp.float32)
    bias_rows = bias_rows.at[0, :block_out].set(bias_part)
    space_reduce = all_reduce_direct if space_devices <= 4 else all_reduce_rows
    reduced = space_reduce(jnp.concatenate([weight_part, bias_rows]) * grad_scale, "space")
    weight_grad = jnp.transpose(
        reduced[: taps_total * block_out].reshape(taps_total, block_out, channels_in), (0, 2, 1)
    )
    bias_grad = reduced[taps_total * block_out, :block_out]

    chan_devices = lax.axis_size("chips") * lax.axis_size("core")
    backward_weight = jnp.transpose(weight_grid, (0, 2, 1, 3)).reshape(
        3, chan_devices, channels_in // chan_devices, 9 * block_out
    )
    spread = None
    for depth_index in range(3):
        part = jnp.einsum(
            "bjk,zkn->bzjn",
            backward_weight[depth_index],
            grad_shifted[2 - depth_index : 2 - depth_index + depth_cells],
            preferred_element_type=jnp.float32,
        )
        spread = part if spread is None else spread + part
    summed = scatter_channels(spread).reshape(depth_cells, block_in, plane_cells)
    input_grad = jnp.transpose(summed.astype(jnp.bfloat16), (1, 0, 2))
    return (outputs, input_grad, weight_grad, bias_grad)


def solution(mesh):
    space_devices, chan_devices = mesh.shape["space"], mesh.shape["chan"]
    split = Mesh(mesh.devices.reshape(space_devices, chan_devices // 2, 2), ("space", "chips", "core"))
    chan = ("chips", "core")
    placed = (P(chan, "space", None), P(None, None, chan), P(chan), P(chan, "space", None))
    return jax.shard_map(
        body,
        mesh=split,
        in_specs=placed,
        out_specs=(
            P(chan, "space", None),
            P(chan, "space", None),
            P(None, None, chan),
            P(chan),
        ),
        check_vma=False,
    )
```

```python
import math

import jax
import jax.numpy as jnp
from jax import lax
from jax.sharding import PartitionSpec as P

W = 64


tap_offsets = tuple(
    (
        (depth_step, row_step, column_step)
        for depth_step in (-1, 0, 1)
        for row_step in (-1, 0, 1)
        for column_step in (-1, 0, 1)
    )
)


def padded_2(array, sides, width):
    for axis, dim in sides:
        devices, length = (lax.axis_size(axis), array.shape[dim])
        up = [(i, (i + 1) % devices) for i in range(devices - 1)]
        down = [(j, i) for i, j in up]
        last = lax.slice_in_dim(array, length - width, length, axis=dim)
        first = lax.slice_in_dim(array, 0, width, axis=dim)
        before = lax.ppermute(last, axis, up)
        after = lax.ppermute(first, axis, down)
        array = jnp.concatenate([before, array, after], axis=dim)
    return array


def shift_cells(field, row_step, column_step):
    length_flat = field.shape[-1]
    pad_width = W + 1
    widths = [(0, 0)] * (field.ndim - 1) + [(pad_width, pad_width)]
    padded = jnp.pad(field, widths)
    first_index = pad_width + row_step * W + column_step
    shifted = lax.slice_in_dim(padded, first_index, first_index + length_flat, axis=field.ndim - 1)
    column = jnp.arange(length_flat, dtype=jnp.int32) % W
    inside = (column + column_step >= 0) & (column + column_step < W)
    return jnp.where(inside, shifted, jnp.zeros_like(shifted))


def outer_planes(field):
    return jnp.concatenate([field[:, :1], field[:, -1:]], axis=1)


def attach_rims(field, rims):
    return jnp.concatenate([rims[:, :1], field, rims[:, 3:]], axis=1)


def all_reduce_rows(block, axis):
    devices = lax.axis_size(axis)
    steps = devices.bit_length() - 1
    assert 1 << steps == devices
    current = block
    index = lax.axis_index(axis)
    for step in range(steps):
        half = current.shape[0] // 2
        bit = (index >> step) & 1
        keep = lax.dynamic_slice_in_dim(current, bit * half, half)
        send = lax.dynamic_slice_in_dim(current, (1 - bit) * half, half)
        pairs = [(i, i ^ (1 << step)) for i in range(devices)]
        current = keep + lax.ppermute(send, axis, pairs)
    for step in reversed(range(steps)):
        half = current.shape[0]
        bit = (index >> step) & 1
        pairs = [(i, i ^ (1 << step)) for i in range(devices)]
        other = lax.ppermute(current, axis, pairs)
        both = jnp.zeros((2 * half,) + current.shape[1:], current.dtype)
        both = lax.dynamic_update_slice_in_dim(both, current, bit * half, 0)
        current = lax.dynamic_update_slice_in_dim(both, other, (1 - bit) * half, 0)
    return current


def shift_volume(field, row_step, column_step, rows):
    length_flat = field.shape[-1]
    pad_width = W + 1
    widths = [(0, 0)] * (field.ndim - 1) + [(pad_width, pad_width)]
    padded = jnp.pad(field, widths)
    first_index = pad_width + row_step * W + column_step
    shifted = lax.slice_in_dim(padded, first_index, first_index + length_flat, axis=field.ndim - 1)
    cell = jnp.arange(length_flat, dtype=jnp.int32)
    column = cell % W
    row = (cell // W) % rows
    inside = (column + column_step >= 0) & (column + column_step < W)
    inside = inside & (row + row_step >= 0) & (row + row_step < rows)
    return jnp.where(inside, shifted, jnp.zeros_like(shifted))


plane_offsets = tuple((row_step, column_step) for row_step in (-1, 0, 1) for column_step in (-1, 0, 1))


def all_reduce_direct(block, axis):
    devices = lax.axis_size(axis)
    index = lax.axis_index(axis)
    chunks = block.reshape((devices, block.shape[0] // devices) + block.shape[1:])
    reduced = lax.dynamic_index_in_dim(chunks, index, 0, keepdims=False)
    for distance in range(1, devices):
        pairs = [(i, i ^ distance) for i in range(devices)]
        send = lax.dynamic_index_in_dim(chunks, index ^ distance, 0, keepdims=False)
        reduced = reduced + lax.ppermute(send, axis, pairs)
    pieces = [reduced] + [
        lax.ppermute(reduced, axis, [(i, i ^ distance) for i in range(devices)])
        for distance in range(1, devices)
    ]
    stacked = jnp.stack(pieces)
    return jnp.concatenate(
        [lax.dynamic_index_in_dim(stacked, index ^ chunk, 0, keepdims=False) for chunk in range(devices)]
    )


def shift_sum(stacked, steps_sign):
    total = None
    for shift_index, (row_step, column_step) in enumerate(plane_offsets):
        term = shift_cells(stacked[:, shift_index], steps_sign * row_step, steps_sign * column_step)
        total = term if total is None else total + term
    return total


def depth_products(weights, planes, toward_output):
    total = None
    for depth_index in range(3):
        part = jnp.einsum("ki,zin->zkn", weights[depth_index], planes, preferred_element_type=jnp.float32)
        front = 2 - depth_index if toward_output else depth_index
        part = jnp.pad(part, ((front, 2 - front), (0, 0), (0, 0)))
        total = part if total is None else total + part
    return total


def settle_rims(field):
    depth = field.shape[0] - 2
    space_devices = lax.axis_size("space")
    up = [(i, i + 1) for i in range(space_devices - 1)]
    down = [(i + 1, i) for i in range(space_devices - 1)]
    from_below = lax.ppermute(field[depth + 1 :], "space", up)
    from_above = lax.ppermute(field[:1], "space", down)
    return field[1 : depth + 1] + jnp.concatenate(
        [from_below, jnp.zeros((depth - 2,) + field.shape[1:], field.dtype), from_above]
    )


def exchange_rows(weight, axis):
    devices = lax.axis_size(axis)
    if devices > 8:
        return lax.all_to_all(weight, axis, 1, 2, tiled=True)
    index = lax.axis_index(axis)
    rows = weight.reshape(weight.shape[0], devices, weight.shape[1] // devices, weight.shape[2])
    pieces = [lax.dynamic_index_in_dim(rows, index, 1, keepdims=False)]
    for distance in range(1, devices):
        send = lax.dynamic_index_in_dim(rows, index ^ distance, 1, keepdims=False)
        pieces.append(lax.ppermute(send, axis, [(i, i ^ distance) for i in range(devices)]))
    stacked = jnp.stack(pieces)
    return jnp.concatenate(
        [lax.dynamic_index_in_dim(stacked, index ^ block, 0, keepdims=False) for block in range(devices)],
        axis=2,
    )


def body(inputs, weight, bias_term, output_grad):
    taps_total = weight.shape[0]
    channels_in = weight.shape[1]
    block_out = weight.shape[2]
    block_in = inputs.shape[0]
    depth_cells = inputs.shape[1]
    plane_cells = inputs.shape[2]
    grad_scale = 1.0 / math.sqrt(lax.axis_size("space") * depth_cells * plane_cells)
    inputs_planes = jnp.transpose(inputs, (1, 0, 2))
    grad_planes = jnp.transpose(output_grad, (1, 0, 2))
    gathered = lax.all_gather(inputs_planes, "chan", axis=1, tiled=True)
    grad_gathered = lax.all_gather(grad_planes, "chan", axis=1, tiled=True)
    weight_rows = exchange_rows(weight, "chan")

    weight_grid = weight.reshape(3, 9, channels_in, block_out)
    forward_weight = jnp.transpose(weight_grid, (0, 1, 3, 2)).reshape(3, 9 * block_out, channels_in)
    forward = shift_sum(
        depth_products(forward_weight, gathered, True).reshape(depth_cells + 2, 9, block_out, plane_cells), 1
    )
    forward = settle_rims(forward)
    outputs = jnp.transpose(
        (forward + bias_term[None, :, None]).astype(jnp.bfloat16), (1, 0, 2)
    )

    grad_rimmed = padded_2(grad_planes, (("space", 0),), 1)
    grad_shifted = jnp.stack(
        [shift_cells(grad_rimmed, -row_step, -column_step) for row_step, column_step in plane_offsets],
        axis=1,
    ).reshape(depth_cells + 2, 9 * block_out, plane_cells)
    weight_part = jnp.stack(
        [
            jnp.einsum(
                "zkn,zin->ki",
                grad_shifted[2 - depth_index : 2 - depth_index + depth_cells],
                gathered,
                preferred_element_type=jnp.float32,
            )
            for depth_index in range(3)
        ]
    ).reshape(taps_total * block_out, channels_in)
    bias_part = jnp.sum(output_grad.astype(jnp.float32), axis=(1, 2))
    space_devices = lax.axis_size("space")
    unit = 8 * space_devices
    total_rows = -(-(taps_total * block_out + 1) // unit) * unit
    bias_rows = jnp.zeros((total_rows - taps_total * block_out, channels_in), jnp.float32)
    bias_rows = bias_rows.at[0, :block_out].set(bias_part)
    space_reduce = all_reduce_direct if space_devices <= 4 else all_reduce_rows
    reduced = space_reduce(jnp.concatenate([weight_part, bias_rows]) * grad_scale, "space")
    weight_grad = jnp.transpose(
        reduced[: taps_total * block_out].reshape(taps_total, block_out, channels_in), (0, 2, 1)
    )
    bias_grad = reduced[taps_total * block_out, :block_out]

    channels_out = weight_rows.shape[2]
    backward_weight = weight_rows.reshape(3, 9 * block_in, channels_out)
    spread = shift_sum(
        depth_products(backward_weight, grad_gathered, False).reshape(depth_cells + 2, 9, block_in, plane_cells), -1
    )
    spread = settle_rims(spread)
    input_grad = jnp.transpose(spread.astype(jnp.bfloat16), (1, 0, 2))
    return (outputs, input_grad, weight_grad, bias_grad)


def solution(mesh):
    placed = (P("chan", "space", None), P(None, None, "chan"), P("chan"), P("chan", "space", None))
    return jax.shard_map(
        body,
        mesh=mesh,
        in_specs=placed,
        out_specs=(
            P("chan", "space", None),
            P("chan", "space", None),
            P(None, None, "chan"),
            P("chan"),
        ),
        check_vma=False,
    )
```

```python
import math

import jax
import jax.numpy as jnp
from jax import lax
from jax.sharding import Mesh, PartitionSpec as P

W = 64


tap_offsets = tuple(
    (
        (depth_step, row_step, column_step)
        for depth_step in (-1, 0, 1)
        for row_step in (-1, 0, 1)
        for column_step in (-1, 0, 1)
    )
)


def padded_2(array, sides, width):
    for axis, dim in sides:
        devices, length = (lax.axis_size(axis), array.shape[dim])
        up = [(i, (i + 1) % devices) for i in range(devices - 1)]
        down = [(j, i) for i, j in up]
        last = lax.slice_in_dim(array, length - width, length, axis=dim)
        first = lax.slice_in_dim(array, 0, width, axis=dim)
        before = lax.ppermute(last, axis, up)
        after = lax.ppermute(first, axis, down)
        array = jnp.concatenate([before, array, after], axis=dim)
    return array


def shift_cells(field, row_step, column_step):
    length_flat = field.shape[-1]
    pad_width = W + 1
    widths = [(0, 0)] * (field.ndim - 1) + [(pad_width, pad_width)]
    padded = jnp.pad(field, widths)
    first_index = pad_width + row_step * W + column_step
    shifted = lax.slice_in_dim(padded, first_index, first_index + length_flat, axis=field.ndim - 1)
    column = jnp.arange(length_flat, dtype=jnp.int32) % W
    inside = (column + column_step >= 0) & (column + column_step < W)
    return jnp.where(inside, shifted, jnp.zeros_like(shifted))


def outer_planes(field):
    return jnp.concatenate([field[:, :1], field[:, -1:]], axis=1)


def attach_rims(field, rims):
    return jnp.concatenate([rims[:, :1], field, rims[:, 3:]], axis=1)


def all_reduce_rows(block, axis):
    devices = lax.axis_size(axis)
    steps = devices.bit_length() - 1
    assert 1 << steps == devices
    current = block
    index = lax.axis_index(axis)
    for step in range(steps):
        half = current.shape[0] // 2
        bit = (index >> step) & 1
        keep = lax.dynamic_slice_in_dim(current, bit * half, half)
        send = lax.dynamic_slice_in_dim(current, (1 - bit) * half, half)
        pairs = [(i, i ^ (1 << step)) for i in range(devices)]
        current = keep + lax.ppermute(send, axis, pairs)
    for step in reversed(range(steps)):
        half = current.shape[0]
        bit = (index >> step) & 1
        pairs = [(i, i ^ (1 << step)) for i in range(devices)]
        other = lax.ppermute(current, axis, pairs)
        both = jnp.zeros((2 * half,) + current.shape[1:], current.dtype)
        both = lax.dynamic_update_slice_in_dim(both, current, bit * half, 0)
        current = lax.dynamic_update_slice_in_dim(both, other, (1 - bit) * half, 0)
    return current


def shift_volume(field, row_step, column_step, rows):
    length_flat = field.shape[-1]
    pad_width = W + 1
    widths = [(0, 0)] * (field.ndim - 1) + [(pad_width, pad_width)]
    padded = jnp.pad(field, widths)
    first_index = pad_width + row_step * W + column_step
    shifted = lax.slice_in_dim(padded, first_index, first_index + length_flat, axis=field.ndim - 1)
    cell = jnp.arange(length_flat, dtype=jnp.int32)
    column = cell % W
    row = (cell // W) % rows
    inside = (column + column_step >= 0) & (column + column_step < W)
    inside = inside & (row + row_step >= 0) & (row + row_step < rows)
    return jnp.where(inside, shifted, jnp.zeros_like(shifted))


plane_offsets = tuple((row_step, column_step) for row_step in (-1, 0, 1) for column_step in (-1, 0, 1))


def all_reduce_direct(block, axis):
    devices = lax.axis_size(axis)
    index = lax.axis_index(axis)
    chunks = block.reshape((devices, block.shape[0] // devices) + block.shape[1:])
    reduced = lax.dynamic_index_in_dim(chunks, index, 0, keepdims=False)
    for distance in range(1, devices):
        pairs = [(i, i ^ distance) for i in range(devices)]
        send = lax.dynamic_index_in_dim(chunks, index ^ distance, 0, keepdims=False)
        reduced = reduced + lax.ppermute(send, axis, pairs)
    pieces = [reduced] + [
        lax.ppermute(reduced, axis, [(i, i ^ distance) for i in range(devices)])
        for distance in range(1, devices)
    ]
    stacked = jnp.stack(pieces)
    return jnp.concatenate(
        [lax.dynamic_index_in_dim(stacked, index ^ chunk, 0, keepdims=False) for chunk in range(devices)]
    )


def gather_channels(planes):
    chip_blocks = lax.all_gather(planes, "chips", axis=1, tiled=False)
    partner = lax.ppermute(chip_blocks, "core", [(0, 1), (1, 0)])
    first = lax.axis_index("core") == 0
    low = jnp.where(first, chip_blocks, partner)
    high = jnp.where(first, partner, chip_blocks)
    return jnp.stack([low, high], axis=2).reshape(planes.shape[0], -1, planes.shape[2])


def scatter_channels(blocks):
    by_core = blocks.reshape((-1, 2) + blocks.shape[1:])
    core = lax.axis_index("core")
    keep = lax.dynamic_index_in_dim(by_core, core, axis=1, keepdims=False)
    send = lax.dynamic_index_in_dim(by_core, 1 - core, axis=1, keepdims=False)
    partial = keep + lax.ppermute(send, "core", [(0, 1), (1, 0)])
    return lax.psum_scatter(
        partial.reshape(-1, blocks.shape[-1]), "chips", scatter_dimension=0, tiled=True
    )


def body(inputs, weight, bias_term, output_grad):
    taps_total = weight.shape[0]
    channels_in = weight.shape[1]
    block_out = weight.shape[2]
    block_in = inputs.shape[0]
    depth_cells = inputs.shape[1]
    plane_cells = inputs.shape[2]
    grad_scale = 1.0 / math.sqrt(lax.axis_size("space") * depth_cells * plane_cells)
    inputs_planes = jnp.transpose(inputs, (1, 0, 2))
    grad_planes = jnp.transpose(output_grad, (1, 0, 2))
    gathered = gather_channels(inputs_planes)

    weight_grid = weight.reshape(3, 9, channels_in, block_out)
    forward_weight = jnp.transpose(weight_grid, (0, 1, 3, 2)).reshape(3, 9 * block_out, channels_in)
    in_plane = None
    for depth_index in range(3):
        part = jnp.einsum(
            "ki,zin->zkn",
            forward_weight[depth_index],
            gathered,
            preferred_element_type=jnp.float32,
        )
        part = jnp.pad(part, ((2 - depth_index, depth_index), (0, 0), (0, 0)))
        in_plane = part if in_plane is None else in_plane + part
    in_plane = in_plane.reshape(depth_cells + 2, 9, block_out, plane_cells)
    forward = None
    for shift_index, (row_step, column_step) in enumerate(plane_offsets):
        term = shift_cells(in_plane[:, shift_index], row_step, column_step)
        forward = term if forward is None else forward + term
    space_devices = lax.axis_size("space")
    up = [(i, i + 1) for i in range(space_devices - 1)]
    down = [(i + 1, i) for i in range(space_devices - 1)]
    from_below = lax.ppermute(forward[depth_cells + 1 :], "space", up)
    from_above = lax.ppermute(forward[:1], "space", down)
    forward = forward[1 : depth_cells + 1] + jnp.concatenate(
        [from_below, jnp.zeros((depth_cells - 2, block_out, plane_cells), jnp.float32), from_above]
    )
    outputs = jnp.transpose(
        (forward + bias_term[None, :, None]).astype(jnp.bfloat16), (1, 0, 2)
    )

    grad_rimmed = padded_2(grad_planes, (("space", 0),), 1)
    grad_shifted = jnp.stack(
        [shift_cells(grad_rimmed, -row_step, -column_step) for row_step, column_step in plane_offsets],
        axis=1,
    ).reshape(depth_cells + 2, 9 * block_out, plane_cells)
    weight_part = jnp.stack(
        [
            jnp.einsum(
                "zkn,zin->ki",
                grad_shifted[2 - depth_index : 2 - depth_index + depth_cells],
                gathered,
                preferred_element_type=jnp.float32,
            )
            for depth_index in range(3)
        ]
    ).reshape(taps_total * block_out, channels_in)
    bias_part = jnp.sum(output_grad.astype(jnp.float32), axis=(1, 2))
    unit = 8 * space_devices
    total_rows = -(-(taps_total * block_out + 1) // unit) * unit
    bias_rows = jnp.zeros((total_rows - taps_total * block_out, channels_in), jnp.float32)
    bias_rows = bias_rows.at[0, :block_out].set(bias_part)
    space_reduce = all_reduce_direct if space_devices <= 4 else all_reduce_rows
    reduced = space_reduce(jnp.concatenate([weight_part, bias_rows]) * grad_scale, "space")
    weight_grad = jnp.transpose(
        reduced[: taps_total * block_out].reshape(taps_total, block_out, channels_in), (0, 2, 1)
    )
    bias_grad = reduced[taps_total * block_out, :block_out]

    chan_devices = lax.axis_size("chips") * lax.axis_size("core")
    backward_weight = jnp.transpose(weight_grid, (0, 2, 1, 3)).reshape(
        3, chan_devices, channels_in // chan_devices, 9 * block_out
    )
    spread = None
    for depth_index in range(3):
        part = jnp.einsum(
            "bjk,zkn->bzjn",
            backward_weight[depth_index],
            grad_shifted[2 - depth_index : 2 - depth_index + depth_cells],
            preferred_element_type=jnp.float32,
        )
        spread = part if spread is None else spread + part
    summed = scatter_channels(spread).reshape(depth_cells, block_in, plane_cells)
    input_grad = jnp.transpose(summed.astype(jnp.bfloat16), (1, 0, 2))
    return (outputs, input_grad, weight_grad, bias_grad)


def solution(mesh):
    space_devices, chan_devices = mesh.shape["space"], mesh.shape["chan"]
    split = Mesh(mesh.devices.reshape(space_devices, chan_devices // 2, 2), ("space", "chips", "core"))
    chan = ("chips", "core")
    placed = (P(chan, "space", None), P(None, None, chan), P(chan), P(chan, "space", None))
    return jax.shard_map(
        body,
        mesh=split,
        in_specs=placed,
        out_specs=(
            P(chan, "space", None),
            P(chan, "space", None),
            P(None, None, chan),
            P(chan),
        ),
        check_vma=False,
    )
```

```python
import math

import jax
import jax.numpy as jnp
from jax import lax
from jax.sharding import Mesh, PartitionSpec as P

W = 64


tap_offsets = tuple(
    (
        (depth_step, row_step, column_step)
        for depth_step in (-1, 0, 1)
        for row_step in (-1, 0, 1)
        for column_step in (-1, 0, 1)
    )
)


def padded_2(array, sides, width):
    for axis, dim in sides:
        devices, length = (lax.axis_size(axis), array.shape[dim])
        up = [(i, (i + 1) % devices) for i in range(devices - 1)]
        down = [(j, i) for i, j in up]
        last = lax.slice_in_dim(array, length - width, length, axis=dim)
        first = lax.slice_in_dim(array, 0, width, axis=dim)
        before = lax.ppermute(last, axis, up)
        after = lax.ppermute(first, axis, down)
        array = jnp.concatenate([before, array, after], axis=dim)
    return array


def shift_cells(field, row_step, column_step):
    length_flat = field.shape[-1]
    pad_width = W + 1
    widths = [(0, 0)] * (field.ndim - 1) + [(pad_width, pad_width)]
    padded = jnp.pad(field, widths)
    first_index = pad_width + row_step * W + column_step
    shifted = lax.slice_in_dim(padded, first_index, first_index + length_flat, axis=field.ndim - 1)
    column = jnp.arange(length_flat, dtype=jnp.int32) % W
    inside = (column + column_step >= 0) & (column + column_step < W)
    return jnp.where(inside, shifted, jnp.zeros_like(shifted))


def outer_planes(field):
    return jnp.concatenate([field[:, :1], field[:, -1:]], axis=1)


def attach_rims(field, rims):
    return jnp.concatenate([rims[:, :1], field, rims[:, 3:]], axis=1)


def all_reduce_rows(block, axis):
    devices = lax.axis_size(axis)
    steps = devices.bit_length() - 1
    assert 1 << steps == devices
    current = block
    index = lax.axis_index(axis)
    for step in range(steps):
        half = current.shape[0] // 2
        bit = (index >> step) & 1
        keep = lax.dynamic_slice_in_dim(current, bit * half, half)
        send = lax.dynamic_slice_in_dim(current, (1 - bit) * half, half)
        pairs = [(i, i ^ (1 << step)) for i in range(devices)]
        current = keep + lax.ppermute(send, axis, pairs)
    for step in reversed(range(steps)):
        half = current.shape[0]
        bit = (index >> step) & 1
        pairs = [(i, i ^ (1 << step)) for i in range(devices)]
        other = lax.ppermute(current, axis, pairs)
        both = jnp.zeros((2 * half,) + current.shape[1:], current.dtype)
        both = lax.dynamic_update_slice_in_dim(both, current, bit * half, 0)
        current = lax.dynamic_update_slice_in_dim(both, other, (1 - bit) * half, 0)
    return current


def shift_volume(field, row_step, column_step, rows):
    length_flat = field.shape[-1]
    pad_width = W + 1
    widths = [(0, 0)] * (field.ndim - 1) + [(pad_width, pad_width)]
    padded = jnp.pad(field, widths)
    first_index = pad_width + row_step * W + column_step
    shifted = lax.slice_in_dim(padded, first_index, first_index + length_flat, axis=field.ndim - 1)
    cell = jnp.arange(length_flat, dtype=jnp.int32)
    column = cell % W
    row = (cell // W) % rows
    inside = (column + column_step >= 0) & (column + column_step < W)
    inside = inside & (row + row_step >= 0) & (row + row_step < rows)
    return jnp.where(inside, shifted, jnp.zeros_like(shifted))


plane_offsets = tuple((row_step, column_step) for row_step in (-1, 0, 1) for column_step in (-1, 0, 1))


def all_reduce_direct(block, axis):
    devices = lax.axis_size(axis)
    index = lax.axis_index(axis)
    chunks = block.reshape((devices, block.shape[0] // devices) + block.shape[1:])
    reduced = lax.dynamic_index_in_dim(chunks, index, 0, keepdims=False)
    for distance in range(1, devices):
        pairs = [(i, i ^ distance) for i in range(devices)]
        send = lax.dynamic_index_in_dim(chunks, index ^ distance, 0, keepdims=False)
        reduced = reduced + lax.ppermute(send, axis, pairs)
    pieces = [reduced] + [
        lax.ppermute(reduced, axis, [(i, i ^ distance) for i in range(devices)])
        for distance in range(1, devices)
    ]
    stacked = jnp.stack(pieces)
    return jnp.concatenate(
        [lax.dynamic_index_in_dim(stacked, index ^ chunk, 0, keepdims=False) for chunk in range(devices)]
    )


def scatter_channels(blocks):
    by_core = blocks.reshape((-1, 2) + blocks.shape[1:])
    core = lax.axis_index("core")
    keep = lax.dynamic_index_in_dim(by_core, core, axis=1, keepdims=False)
    send = lax.dynamic_index_in_dim(by_core, 1 - core, axis=1, keepdims=False)
    partial = keep + lax.ppermute(send, "core", [(0, 1), (1, 0)])
    return lax.psum_scatter(
        partial.reshape(-1, blocks.shape[-1]), "chips", scatter_dimension=0, tiled=True
    )


def body(inputs, weight, bias_term, output_grad):
    taps_total = weight.shape[0]
    channels_in = weight.shape[1]
    block_out = weight.shape[2]
    block_in = inputs.shape[0]
    depth_cells = inputs.shape[1]
    plane_cells = inputs.shape[2]
    grad_scale = 1.0 / math.sqrt(lax.axis_size("space") * depth_cells * plane_cells)
    inputs_planes = jnp.transpose(inputs, (1, 0, 2))
    inputs_planes, output_grad = lax.optimization_barrier((inputs_planes, output_grad))
    grad_planes = jnp.transpose(output_grad, (1, 0, 2))
    gathered = lax.all_gather(inputs_planes, ("chips", "core"), axis=1, tiled=True)

    weight_grid = weight.reshape(3, 9, channels_in, block_out)
    forward_weight = jnp.transpose(weight_grid, (0, 1, 3, 2)).reshape(3, 9 * block_out, channels_in)
    in_plane = None
    for depth_index in range(3):
        part = jnp.einsum(
            "ki,zin->zkn",
            forward_weight[depth_index],
            gathered,
            preferred_element_type=jnp.float32,
        )
        part = jnp.pad(part, ((2 - depth_index, depth_index), (0, 0), (0, 0)))
        in_plane = part if in_plane is None else in_plane + part
    in_plane = in_plane.reshape(depth_cells + 2, 9, block_out, plane_cells)
    forward = None
    for shift_index, (row_step, column_step) in enumerate(plane_offsets):
        term = shift_cells(in_plane[:, shift_index], row_step, column_step)
        forward = term if forward is None else forward + term
    space_devices = lax.axis_size("space")
    up = [(i, i + 1) for i in range(space_devices - 1)]
    down = [(i + 1, i) for i in range(space_devices - 1)]
    from_below = lax.ppermute(forward[depth_cells + 1 :], "space", up)
    from_above = lax.ppermute(forward[:1], "space", down)
    forward = forward[1 : depth_cells + 1] + jnp.concatenate(
        [from_below, jnp.zeros((depth_cells - 2, block_out, plane_cells), jnp.float32), from_above]
    )
    outputs = jnp.transpose(
        (forward + bias_term[None, :, None]).astype(jnp.bfloat16), (1, 0, 2)
    )

    grad_rimmed = padded_2(grad_planes, (("space", 0),), 1)
    grad_shifted = jnp.stack(
        [shift_cells(grad_rimmed, -row_step, -column_step) for row_step, column_step in plane_offsets],
        axis=1,
    ).reshape(depth_cells + 2, 9 * block_out, plane_cells)
    weight_part = jnp.stack(
        [
            jnp.einsum(
                "zkn,zin->ki",
                grad_shifted[2 - depth_index : 2 - depth_index + depth_cells],
                gathered,
                preferred_element_type=jnp.float32,
            )
            for depth_index in range(3)
        ]
    ).reshape(taps_total * block_out, channels_in)
    bias_part = jnp.sum(output_grad.astype(jnp.float32), axis=(1, 2))
    unit = 8 * space_devices
    total_rows = -(-(taps_total * block_out + 1) // unit) * unit
    bias_rows = jnp.zeros((total_rows - taps_total * block_out, channels_in), jnp.float32)
    bias_rows = bias_rows.at[0, :block_out].set(bias_part)
    space_reduce = all_reduce_direct if space_devices <= 4 else all_reduce_rows
    reduced = space_reduce(jnp.concatenate([weight_part, bias_rows]) * grad_scale, "space")
    weight_grad = jnp.transpose(
        reduced[: taps_total * block_out].reshape(taps_total, block_out, channels_in), (0, 2, 1)
    )
    bias_grad = reduced[taps_total * block_out, :block_out]

    chan_devices = lax.axis_size("chips") * lax.axis_size("core")
    backward_weight = jnp.transpose(weight_grid, (0, 2, 1, 3)).reshape(
        3, chan_devices // 2, 2, channels_in // chan_devices, 9 * block_out
    )
    core = lax.axis_index("core")

    def partial_sums(core_weight, total):
        for depth_index in range(3):
            part = jnp.einsum(
                "cjk,zkn->czjn",
                core_weight[depth_index],
                grad_shifted[2 - depth_index : 2 - depth_index + depth_cells],
                preferred_element_type=jnp.float32,
            )
            total = part if total is None else total + part
        return total

    sent = partial_sums(lax.dynamic_index_in_dim(backward_weight, 1 - core, axis=2, keepdims=False), None)
    received = lax.ppermute(sent, "core", [(0, 1), (1, 0)])
    spread = partial_sums(lax.dynamic_index_in_dim(backward_weight, core, axis=2, keepdims=False), received)
    summed = lax.psum_scatter(
        spread.reshape(-1, plane_cells), "chips", scatter_dimension=0, tiled=True
    ).reshape(depth_cells, block_in, plane_cells)
    input_grad = jnp.transpose(summed.astype(jnp.bfloat16), (1, 0, 2))
    return (outputs, input_grad, weight_grad, bias_grad)


def solution(mesh):
    space_devices, chan_devices = mesh.shape["space"], mesh.shape["chan"]
    split = Mesh(mesh.devices.reshape(space_devices, chan_devices // 2, 2), ("space", "chips", "core"))
    chan = ("chips", "core")
    placed = (P(chan, "space", None), P(None, None, chan), P(chan), P(chan, "space", None))
    return jax.shard_map(
        body,
        mesh=split,
        in_specs=placed,
        out_specs=(
            P(chan, "space", None),
            P(chan, "space", None),
            P(None, None, chan),
            P(chan),
        ),
        check_vma=False,
    )
```

```python
import math

import jax
import jax.numpy as jnp
from jax import lax
from jax.sharding import Mesh, PartitionSpec as P

W = 64


tap_offsets = tuple(
    (
        (depth_step, row_step, column_step)
        for depth_step in (-1, 0, 1)
        for row_step in (-1, 0, 1)
        for column_step in (-1, 0, 1)
    )
)


def padded_2(array, sides, width):
    for axis, dim in sides:
        devices, length = (lax.axis_size(axis), array.shape[dim])
        up = [(i, (i + 1) % devices) for i in range(devices - 1)]
        down = [(j, i) for i, j in up]
        last = lax.slice_in_dim(array, length - width, length, axis=dim)
        first = lax.slice_in_dim(array, 0, width, axis=dim)
        before = lax.ppermute(last, axis, up)
        after = lax.ppermute(first, axis, down)
        array = jnp.concatenate([before, array, after], axis=dim)
    return array


def shift_cells(field, row_step, column_step):
    length_flat = field.shape[-1]
    pad_width = W + 1
    widths = [(0, 0)] * (field.ndim - 1) + [(pad_width, pad_width)]
    padded = jnp.pad(field, widths)
    first_index = pad_width + row_step * W + column_step
    shifted = lax.slice_in_dim(padded, first_index, first_index + length_flat, axis=field.ndim - 1)
    column = jnp.arange(length_flat, dtype=jnp.int32) % W
    inside = (column + column_step >= 0) & (column + column_step < W)
    return jnp.where(inside, shifted, jnp.zeros_like(shifted))


def outer_planes(field):
    return jnp.concatenate([field[:, :1], field[:, -1:]], axis=1)


def attach_rims(field, rims):
    return jnp.concatenate([rims[:, :1], field, rims[:, 3:]], axis=1)


def all_reduce_rows(block, axis):
    devices = lax.axis_size(axis)
    steps = devices.bit_length() - 1
    assert 1 << steps == devices
    current = block
    index = lax.axis_index(axis)
    for step in range(steps):
        half = current.shape[0] // 2
        bit = (index >> step) & 1
        keep = lax.dynamic_slice_in_dim(current, bit * half, half)
        send = lax.dynamic_slice_in_dim(current, (1 - bit) * half, half)
        pairs = [(i, i ^ (1 << step)) for i in range(devices)]
        current = keep + lax.ppermute(send, axis, pairs)
    for step in reversed(range(steps)):
        half = current.shape[0]
        bit = (index >> step) & 1
        pairs = [(i, i ^ (1 << step)) for i in range(devices)]
        other = lax.ppermute(current, axis, pairs)
        both = jnp.zeros((2 * half,) + current.shape[1:], current.dtype)
        both = lax.dynamic_update_slice_in_dim(both, current, bit * half, 0)
        current = lax.dynamic_update_slice_in_dim(both, other, (1 - bit) * half, 0)
    return current


def shift_volume(field, row_step, column_step, rows):
    length_flat = field.shape[-1]
    pad_width = W + 1
    widths = [(0, 0)] * (field.ndim - 1) + [(pad_width, pad_width)]
    padded = jnp.pad(field, widths)
    first_index = pad_width + row_step * W + column_step
    shifted = lax.slice_in_dim(padded, first_index, first_index + length_flat, axis=field.ndim - 1)
    cell = jnp.arange(length_flat, dtype=jnp.int32)
    column = cell % W
    row = (cell // W) % rows
    inside = (column + column_step >= 0) & (column + column_step < W)
    inside = inside & (row + row_step >= 0) & (row + row_step < rows)
    return jnp.where(inside, shifted, jnp.zeros_like(shifted))


plane_offsets = tuple((row_step, column_step) for row_step in (-1, 0, 1) for column_step in (-1, 0, 1))


def all_reduce_direct(block, axis):
    devices = lax.axis_size(axis)
    index = lax.axis_index(axis)
    chunks = block.reshape((devices, block.shape[0] // devices) + block.shape[1:])
    reduced = lax.dynamic_index_in_dim(chunks, index, 0, keepdims=False)
    for distance in range(1, devices):
        pairs = [(i, i ^ distance) for i in range(devices)]
        send = lax.dynamic_index_in_dim(chunks, index ^ distance, 0, keepdims=False)
        reduced = reduced + lax.ppermute(send, axis, pairs)
    pieces = [reduced] + [
        lax.ppermute(reduced, axis, [(i, i ^ distance) for i in range(devices)])
        for distance in range(1, devices)
    ]
    stacked = jnp.stack(pieces)
    return jnp.concatenate(
        [lax.dynamic_index_in_dim(stacked, index ^ chunk, 0, keepdims=False) for chunk in range(devices)]
    )


def scatter_channels(blocks):
    by_core = blocks.reshape((-1, 2) + blocks.shape[1:])
    core = lax.axis_index("core")
    keep = lax.dynamic_index_in_dim(by_core, core, axis=1, keepdims=False)
    send = lax.dynamic_index_in_dim(by_core, 1 - core, axis=1, keepdims=False)
    partial = keep + lax.ppermute(send, "core", [(0, 1), (1, 0)])
    return lax.psum_scatter(
        partial.reshape(-1, blocks.shape[-1]), "chips", scatter_dimension=0, tiled=True
    )


def body(inputs, weight, bias_term, output_grad):
    taps_total = weight.shape[0]
    channels_in = weight.shape[1]
    block_out = weight.shape[2]
    block_in = inputs.shape[0]
    depth_cells = inputs.shape[1]
    plane_cells = inputs.shape[2]
    grad_scale = 1.0 / math.sqrt(lax.axis_size("space") * depth_cells * plane_cells)
    inputs_planes = jnp.transpose(inputs, (1, 0, 2))
    grad_planes = jnp.transpose(output_grad, (1, 0, 2))
    gathered = lax.all_gather(inputs_planes, ("chips", "core"), axis=1, tiled=True)

    weight_grid = weight.reshape(3, 9, channels_in, block_out)
    forward_weight = jnp.transpose(weight_grid, (0, 1, 3, 2)).reshape(3, 9 * block_out, channels_in)
    in_plane = None
    for depth_index in range(3):
        part = jnp.einsum(
            "ki,zin->zkn",
            forward_weight[depth_index],
            gathered,
            preferred_element_type=jnp.float32,
        )
        part = jnp.pad(part, ((2 - depth_index, depth_index), (0, 0), (0, 0)))
        in_plane = part if in_plane is None else in_plane + part
    in_plane = in_plane.reshape(depth_cells + 2, 9, block_out, plane_cells)
    forward = None
    for shift_index, (row_step, column_step) in enumerate(plane_offsets):
        term = shift_cells(in_plane[:, shift_index], row_step, column_step)
        forward = term if forward is None else forward + term
    space_devices = lax.axis_size("space")
    up = [(i, i + 1) for i in range(space_devices - 1)]
    down = [(i + 1, i) for i in range(space_devices - 1)]
    from_below = lax.ppermute(forward[depth_cells + 1 :], "space", up)
    from_above = lax.ppermute(forward[:1], "space", down)
    forward = forward[1 : depth_cells + 1] + jnp.concatenate(
        [from_below, jnp.zeros((depth_cells - 2, block_out, plane_cells), jnp.float32), from_above]
    )
    outputs = jnp.transpose(
        (forward + bias_term[None, :, None]).astype(jnp.bfloat16), (1, 0, 2)
    )

    grad_rimmed = padded_2(grad_planes, (("space", 0),), 1)
    grad_shifted = jnp.stack(
        [shift_cells(grad_rimmed, -row_step, -column_step) for row_step, column_step in plane_offsets],
        axis=1,
    ).reshape(depth_cells + 2, 9 * block_out, plane_cells)
    weight_part = jnp.stack(
        [
            jnp.einsum(
                "zkn,zin->ki",
                grad_shifted[2 - depth_index : 2 - depth_index + depth_cells],
                gathered,
                preferred_element_type=jnp.float32,
            )
            for depth_index in range(3)
        ]
    ).reshape(taps_total * block_out, channels_in)
    bias_part = jnp.sum(output_grad.astype(jnp.float32), axis=(1, 2))
    unit = 8 * space_devices
    total_rows = -(-(taps_total * block_out + 1) // unit) * unit
    bias_rows = jnp.zeros((total_rows - taps_total * block_out, channels_in), jnp.float32)
    bias_rows = bias_rows.at[0, :block_out].set(bias_part)
    space_reduce = all_reduce_direct if space_devices <= 4 else all_reduce_rows
    reduced = space_reduce(jnp.concatenate([weight_part, bias_rows]) * grad_scale, "space")
    weight_grad = jnp.transpose(
        reduced[: taps_total * block_out].reshape(taps_total, block_out, channels_in), (0, 2, 1)
    )
    bias_grad = reduced[taps_total * block_out, :block_out]

    chan_devices = lax.axis_size("chips") * lax.axis_size("core")
    backward_weight = jnp.transpose(weight_grid, (0, 2, 1, 3)).reshape(
        3, chan_devices, channels_in // chan_devices, 9 * block_out
    )
    spread = None
    for depth_index in range(3):
        part = jnp.einsum(
            "bjk,zkn->bzjn",
            backward_weight[depth_index],
            grad_shifted[2 - depth_index : 2 - depth_index + depth_cells],
            preferred_element_type=jnp.float32,
        )
        spread = part if spread is None else spread + part
    summed = lax.psum_scatter(
        spread.reshape(-1, plane_cells), ("chips", "core"), scatter_dimension=0, tiled=True
    ).reshape(depth_cells, block_in, plane_cells)
    input_grad = jnp.transpose(summed.astype(jnp.bfloat16), (1, 0, 2))
    return (outputs, input_grad, weight_grad, bias_grad)


def solution(mesh):
    space_devices, chan_devices = mesh.shape["space"], mesh.shape["chan"]
    split = Mesh(mesh.devices.reshape(space_devices, chan_devices // 2, 2), ("space", "chips", "core"))
    chan = ("chips", "core")
    placed = (P(chan, "space", None), P(None, None, chan), P(chan), P(chan, "space", None))
    return jax.shard_map(
        body,
        mesh=split,
        in_specs=placed,
        out_specs=(
            P(chan, "space", None),
            P(chan, "space", None),
            P(None, None, chan),
            P(chan),
        ),
        check_vma=False,
    )
```

```python
import math

import jax
import jax.numpy as jnp
from jax import lax
from jax.sharding import Mesh, PartitionSpec as P

W = 64


tap_offsets = tuple(
    (
        (depth_step, row_step, column_step)
        for depth_step in (-1, 0, 1)
        for row_step in (-1, 0, 1)
        for column_step in (-1, 0, 1)
    )
)


def padded_2(array, sides, width):
    for axis, dim in sides:
        devices, length = (lax.axis_size(axis), array.shape[dim])
        up = [(i, (i + 1) % devices) for i in range(devices - 1)]
        down = [(j, i) for i, j in up]
        last = lax.slice_in_dim(array, length - width, length, axis=dim)
        first = lax.slice_in_dim(array, 0, width, axis=dim)
        before = lax.ppermute(last, axis, up)
        after = lax.ppermute(first, axis, down)
        array = jnp.concatenate([before, array, after], axis=dim)
    return array


def shift_cells(field, row_step, column_step):
    length_flat = field.shape[-1]
    pad_width = W + 1
    widths = [(0, 0)] * (field.ndim - 1) + [(pad_width, pad_width)]
    padded = jnp.pad(field, widths)
    first_index = pad_width + row_step * W + column_step
    shifted = lax.slice_in_dim(padded, first_index, first_index + length_flat, axis=field.ndim - 1)
    column = jnp.arange(length_flat, dtype=jnp.int32) % W
    inside = (column + column_step >= 0) & (column + column_step < W)
    return jnp.where(inside, shifted, jnp.zeros_like(shifted))


def outer_planes(field):
    return jnp.concatenate([field[:, :1], field[:, -1:]], axis=1)


def attach_rims(field, rims):
    return jnp.concatenate([rims[:, :1], field, rims[:, 3:]], axis=1)


def all_reduce_rows(block, axis):
    devices = lax.axis_size(axis)
    steps = devices.bit_length() - 1
    assert 1 << steps == devices
    current = block
    index = lax.axis_index(axis)
    for step in range(steps):
        half = current.shape[0] // 2
        bit = (index >> step) & 1
        keep = lax.dynamic_slice_in_dim(current, bit * half, half)
        send = lax.dynamic_slice_in_dim(current, (1 - bit) * half, half)
        pairs = [(i, i ^ (1 << step)) for i in range(devices)]
        current = keep + lax.ppermute(send, axis, pairs)
    for step in reversed(range(steps)):
        half = current.shape[0]
        bit = (index >> step) & 1
        pairs = [(i, i ^ (1 << step)) for i in range(devices)]
        other = lax.ppermute(current, axis, pairs)
        both = jnp.zeros((2 * half,) + current.shape[1:], current.dtype)
        both = lax.dynamic_update_slice_in_dim(both, current, bit * half, 0)
        current = lax.dynamic_update_slice_in_dim(both, other, (1 - bit) * half, 0)
    return current


def shift_volume(field, row_step, column_step, rows):
    length_flat = field.shape[-1]
    pad_width = W + 1
    widths = [(0, 0)] * (field.ndim - 1) + [(pad_width, pad_width)]
    padded = jnp.pad(field, widths)
    first_index = pad_width + row_step * W + column_step
    shifted = lax.slice_in_dim(padded, first_index, first_index + length_flat, axis=field.ndim - 1)
    cell = jnp.arange(length_flat, dtype=jnp.int32)
    column = cell % W
    row = (cell // W) % rows
    inside = (column + column_step >= 0) & (column + column_step < W)
    inside = inside & (row + row_step >= 0) & (row + row_step < rows)
    return jnp.where(inside, shifted, jnp.zeros_like(shifted))


plane_offsets = tuple((row_step, column_step) for row_step in (-1, 0, 1) for column_step in (-1, 0, 1))


def all_reduce_direct(block, axis):
    devices = lax.axis_size(axis)
    index = lax.axis_index(axis)
    chunks = block.reshape((devices, block.shape[0] // devices) + block.shape[1:])
    reduced = lax.dynamic_index_in_dim(chunks, index, 0, keepdims=False)
    for distance in range(1, devices):
        pairs = [(i, i ^ distance) for i in range(devices)]
        send = lax.dynamic_index_in_dim(chunks, index ^ distance, 0, keepdims=False)
        reduced = reduced + lax.ppermute(send, axis, pairs)
    pieces = [reduced] + [
        lax.ppermute(reduced, axis, [(i, i ^ distance) for i in range(devices)])
        for distance in range(1, devices)
    ]
    stacked = jnp.stack(pieces)
    return jnp.concatenate(
        [lax.dynamic_index_in_dim(stacked, index ^ chunk, 0, keepdims=False) for chunk in range(devices)]
    )


def scatter_channels(blocks):
    by_core = blocks.reshape((-1, 2) + blocks.shape[1:])
    core = lax.axis_index("core")
    keep = lax.dynamic_index_in_dim(by_core, core, axis=1, keepdims=False)
    send = lax.dynamic_index_in_dim(by_core, 1 - core, axis=1, keepdims=False)
    partial = keep + lax.ppermute(send, "core", [(0, 1), (1, 0)])
    return lax.psum_scatter(
        partial.reshape(-1, blocks.shape[-1]), "chips", scatter_dimension=0, tiled=True
    )


def body(inputs, weight, bias_term, output_grad):
    taps_total = weight.shape[0]
    channels_in = weight.shape[1]
    block_out = weight.shape[2]
    block_in = inputs.shape[0]
    depth_cells = inputs.shape[1]
    plane_cells = inputs.shape[2]
    grad_scale = 1.0 / math.sqrt(lax.axis_size("space") * depth_cells * plane_cells)
    inputs_planes = jnp.transpose(inputs, (1, 0, 2))
    grad_planes = jnp.transpose(output_grad, (1, 0, 2))
    gathered = lax.all_gather(inputs_planes, ("chips", "core"), axis=1, tiled=True)

    weight_grid = weight.reshape(3, 9, channels_in, block_out)
    forward_weight = jnp.transpose(weight_grid, (0, 1, 3, 2)).reshape(3, 9 * block_out, channels_in)
    in_plane = None
    for depth_index in range(3):
        part = jnp.einsum(
            "ki,zin->zkn",
            forward_weight[depth_index],
            gathered,
            preferred_element_type=jnp.float32,
        )
        part = jnp.pad(part, ((2 - depth_index, depth_index), (0, 0), (0, 0)))
        in_plane = part if in_plane is None else in_plane + part
    in_plane = in_plane.reshape(depth_cells + 2, 9, block_out, plane_cells)
    forward = None
    for shift_index, (row_step, column_step) in enumerate(plane_offsets):
        term = shift_cells(in_plane[:, shift_index], row_step, column_step)
        forward = term if forward is None else forward + term
    space_devices = lax.axis_size("space")
    up = [(i, i + 1) for i in range(space_devices - 1)]
    down = [(i + 1, i) for i in range(space_devices - 1)]
    from_below = lax.ppermute(forward[depth_cells + 1 :], "space", up)
    from_above = lax.ppermute(forward[:1], "space", down)
    forward = forward[1 : depth_cells + 1] + jnp.concatenate(
        [from_below, jnp.zeros((depth_cells - 2, block_out, plane_cells), jnp.float32), from_above]
    )
    outputs = jnp.transpose(
        (forward + bias_term[None, :, None]).astype(jnp.bfloat16), (1, 0, 2)
    )

    grad_rimmed = padded_2(grad_planes, (("space", 0),), 1)
    grad_shifted = jnp.stack(
        [shift_cells(grad_rimmed, -row_step, -column_step) for row_step, column_step in plane_offsets],
        axis=1,
    ).reshape(depth_cells + 2, 9 * block_out, plane_cells)
    weight_part = jnp.stack(
        [
            jnp.einsum(
                "zkn,zin->ki",
                grad_shifted[2 - depth_index : 2 - depth_index + depth_cells],
                gathered,
                preferred_element_type=jnp.float32,
            )
            for depth_index in range(3)
        ]
    ).reshape(taps_total * block_out, channels_in)
    bias_part = jnp.sum(output_grad.astype(jnp.float32), axis=(1, 2))
    unit = 8 * space_devices
    total_rows = -(-(taps_total * block_out + 1) // unit) * unit
    bias_rows = jnp.zeros((total_rows - taps_total * block_out, channels_in), jnp.float32)
    bias_rows = bias_rows.at[0, :block_out].set(bias_part)
    space_reduce = all_reduce_direct if space_devices <= 4 else all_reduce_rows
    reduced = space_reduce(jnp.concatenate([weight_part, bias_rows]) * grad_scale, "space")
    weight_grad = jnp.transpose(
        reduced[: taps_total * block_out].reshape(taps_total, block_out, channels_in), (0, 2, 1)
    )
    bias_grad = reduced[taps_total * block_out, :block_out]

    chan_devices = lax.axis_size("chips") * lax.axis_size("core")
    chips_devices = lax.axis_size("chips")
    backward_weight = jnp.transpose(
        weight_grid.reshape(3, 9, chips_devices, 2, channels_in // chan_devices, block_out), (0, 3, 2, 4, 1, 5)
    ).reshape(3, chan_devices, channels_in // chan_devices, 9 * block_out)
    spread = None
    for depth_index in range(3):
        part = jnp.einsum(
            "bjk,zkn->bzjn",
            backward_weight[depth_index],
            grad_shifted[2 - depth_index : 2 - depth_index + depth_cells],
            preferred_element_type=jnp.float32,
        )
        spread = part if spread is None else spread + part
    summed = lax.psum_scatter(
        spread.reshape(-1, plane_cells), ("core", "chips"), scatter_dimension=0, tiled=True
    ).reshape(depth_cells, block_in, plane_cells)
    input_grad = jnp.transpose(summed.astype(jnp.bfloat16), (1, 0, 2))
    return (outputs, input_grad, weight_grad, bias_grad)


def solution(mesh):
    space_devices, chan_devices = mesh.shape["space"], mesh.shape["chan"]
    split = Mesh(mesh.devices.reshape(space_devices, chan_devices // 2, 2), ("space", "chips", "core"))
    chan = ("chips", "core")
    placed = (P(chan, "space", None), P(None, None, chan), P(chan), P(chan, "space", None))
    return jax.shard_map(
        body,
        mesh=split,
        in_specs=placed,
        out_specs=(
            P(chan, "space", None),
            P(chan, "space", None),
            P(None, None, chan),
            P(chan),
        ),
        check_vma=False,
    )
```

```python
import math

import jax
import jax.numpy as jnp
from jax import lax
from jax.sharding import Mesh, PartitionSpec as P

W = 64


tap_offsets = tuple(
    (
        (depth_step, row_step, column_step)
        for depth_step in (-1, 0, 1)
        for row_step in (-1, 0, 1)
        for column_step in (-1, 0, 1)
    )
)


def padded_2(array, sides, width):
    for axis, dim in sides:
        devices, length = (lax.axis_size(axis), array.shape[dim])
        up = [(i, (i + 1) % devices) for i in range(devices - 1)]
        down = [(j, i) for i, j in up]
        last = lax.slice_in_dim(array, length - width, length, axis=dim)
        first = lax.slice_in_dim(array, 0, width, axis=dim)
        before = lax.ppermute(last, axis, up)
        after = lax.ppermute(first, axis, down)
        array = jnp.concatenate([before, array, after], axis=dim)
    return array


def shift_cells(field, row_step, column_step):
    length_flat = field.shape[-1]
    pad_width = W + 1
    widths = [(0, 0)] * (field.ndim - 1) + [(pad_width, pad_width)]
    padded = jnp.pad(field, widths)
    first_index = pad_width + row_step * W + column_step
    shifted = lax.slice_in_dim(padded, first_index, first_index + length_flat, axis=field.ndim - 1)
    column = jnp.arange(length_flat, dtype=jnp.int32) % W
    inside = (column + column_step >= 0) & (column + column_step < W)
    return jnp.where(inside, shifted, jnp.zeros_like(shifted))


def outer_planes(field):
    return jnp.concatenate([field[:, :1], field[:, -1:]], axis=1)


def attach_rims(field, rims):
    return jnp.concatenate([rims[:, :1], field, rims[:, 3:]], axis=1)


def all_reduce_rows(block, axis):
    devices = lax.axis_size(axis)
    steps = devices.bit_length() - 1
    assert 1 << steps == devices
    current = block
    index = lax.axis_index(axis)
    for step in range(steps):
        half = current.shape[0] // 2
        bit = (index >> step) & 1
        keep = lax.dynamic_slice_in_dim(current, bit * half, half)
        send = lax.dynamic_slice_in_dim(current, (1 - bit) * half, half)
        pairs = [(i, i ^ (1 << step)) for i in range(devices)]
        current = keep + lax.ppermute(send, axis, pairs)
    for step in reversed(range(steps)):
        half = current.shape[0]
        bit = (index >> step) & 1
        pairs = [(i, i ^ (1 << step)) for i in range(devices)]
        other = lax.ppermute(current, axis, pairs)
        both = jnp.zeros((2 * half,) + current.shape[1:], current.dtype)
        both = lax.dynamic_update_slice_in_dim(both, current, bit * half, 0)
        current = lax.dynamic_update_slice_in_dim(both, other, (1 - bit) * half, 0)
    return current


def shift_volume(field, row_step, column_step, rows):
    length_flat = field.shape[-1]
    pad_width = W + 1
    widths = [(0, 0)] * (field.ndim - 1) + [(pad_width, pad_width)]
    padded = jnp.pad(field, widths)
    first_index = pad_width + row_step * W + column_step
    shifted = lax.slice_in_dim(padded, first_index, first_index + length_flat, axis=field.ndim - 1)
    cell = jnp.arange(length_flat, dtype=jnp.int32)
    column = cell % W
    row = (cell // W) % rows
    inside = (column + column_step >= 0) & (column + column_step < W)
    inside = inside & (row + row_step >= 0) & (row + row_step < rows)
    return jnp.where(inside, shifted, jnp.zeros_like(shifted))


plane_offsets = tuple((row_step, column_step) for row_step in (-1, 0, 1) for column_step in (-1, 0, 1))


def all_reduce_direct(block, axis):
    devices = lax.axis_size(axis)
    index = lax.axis_index(axis)
    chunks = block.reshape((devices, block.shape[0] // devices) + block.shape[1:])
    reduced = lax.dynamic_index_in_dim(chunks, index, 0, keepdims=False)
    for distance in range(1, devices):
        pairs = [(i, i ^ distance) for i in range(devices)]
        send = lax.dynamic_index_in_dim(chunks, index ^ distance, 0, keepdims=False)
        reduced = reduced + lax.ppermute(send, axis, pairs)
    pieces = [reduced] + [
        lax.ppermute(reduced, axis, [(i, i ^ distance) for i in range(devices)])
        for distance in range(1, devices)
    ]
    stacked = jnp.stack(pieces)
    return jnp.concatenate(
        [lax.dynamic_index_in_dim(stacked, index ^ chunk, 0, keepdims=False) for chunk in range(devices)]
    )


def scatter_channels(blocks):
    by_core = blocks.reshape((-1, 2) + blocks.shape[1:])
    core = lax.axis_index("core")
    keep = lax.dynamic_index_in_dim(by_core, core, axis=1, keepdims=False)
    send = lax.dynamic_index_in_dim(by_core, 1 - core, axis=1, keepdims=False)
    partial = keep + lax.ppermute(send, "core", [(0, 1), (1, 0)])
    return lax.psum_scatter(
        partial.reshape(-1, blocks.shape[-1]), "chips", scatter_dimension=0, tiled=True
    )


def body(inputs, weight, bias_term, output_grad):
    taps_total = weight.shape[0]
    channels_in = weight.shape[1]
    block_out = weight.shape[2]
    block_in = inputs.shape[0]
    depth_cells = inputs.shape[1]
    plane_cells = inputs.shape[2]
    grad_scale = 1.0 / math.sqrt(lax.axis_size("space") * depth_cells * plane_cells)
    grad_planes = jnp.transpose(output_grad, (1, 0, 2))
    gathered = jnp.transpose(lax.all_gather(inputs, ("chips", "core"), axis=0, tiled=True), (1, 0, 2))

    weight_grid = weight.reshape(3, 9, channels_in, block_out)
    forward_weight = jnp.transpose(weight_grid, (0, 1, 3, 2)).reshape(3, 9 * block_out, channels_in)
    in_plane = None
    for depth_index in range(3):
        part = jnp.einsum(
            "ki,zin->zkn",
            forward_weight[depth_index],
            gathered,
            preferred_element_type=jnp.float32,
        )
        part = jnp.pad(part, ((2 - depth_index, depth_index), (0, 0), (0, 0)))
        in_plane = part if in_plane is None else in_plane + part
    in_plane = in_plane.reshape(depth_cells + 2, 9, block_out, plane_cells)
    forward = None
    for shift_index, (row_step, column_step) in enumerate(plane_offsets):
        term = shift_cells(in_plane[:, shift_index], row_step, column_step)
        forward = term if forward is None else forward + term
    space_devices = lax.axis_size("space")
    up = [(i, i + 1) for i in range(space_devices - 1)]
    down = [(i + 1, i) for i in range(space_devices - 1)]
    from_below = lax.ppermute(forward[depth_cells + 1 :], "space", up)
    from_above = lax.ppermute(forward[:1], "space", down)
    forward = forward[1 : depth_cells + 1] + jnp.concatenate(
        [from_below, jnp.zeros((depth_cells - 2, block_out, plane_cells), jnp.float32), from_above]
    )
    outputs = jnp.transpose(
        (forward + bias_term[None, :, None]).astype(jnp.bfloat16), (1, 0, 2)
    )

    grad_rimmed = padded_2(grad_planes, (("space", 0),), 1)
    grad_shifted = jnp.stack(
        [shift_cells(grad_rimmed, -row_step, -column_step) for row_step, column_step in plane_offsets],
        axis=1,
    ).reshape(depth_cells + 2, 9 * block_out, plane_cells)
    weight_part = jnp.stack(
        [
            jnp.einsum(
                "zkn,zin->ki",
                grad_shifted[2 - depth_index : 2 - depth_index + depth_cells],
                gathered,
                preferred_element_type=jnp.float32,
            )
            for depth_index in range(3)
        ]
    ).reshape(taps_total * block_out, channels_in)
    bias_part = jnp.sum(output_grad.astype(jnp.float32), axis=(1, 2))
    unit = 8 * space_devices
    total_rows = -(-(taps_total * block_out + 1) // unit) * unit
    bias_rows = jnp.zeros((total_rows - taps_total * block_out, channels_in), jnp.float32)
    bias_rows = bias_rows.at[0, :block_out].set(bias_part)
    space_reduce = all_reduce_direct if space_devices <= 4 else all_reduce_rows
    reduced = space_reduce(jnp.concatenate([weight_part, bias_rows]) * grad_scale, "space")
    weight_grad = jnp.transpose(
        reduced[: taps_total * block_out].reshape(taps_total, block_out, channels_in), (0, 2, 1)
    )
    bias_grad = reduced[taps_total * block_out, :block_out]

    chan_devices = lax.axis_size("chips") * lax.axis_size("core")
    backward_weight = jnp.transpose(weight_grid, (0, 2, 1, 3)).reshape(
        3, chan_devices, channels_in // chan_devices, 9 * block_out
    )
    spread = None
    for depth_index in range(3):
        part = jnp.einsum(
            "bjk,zkn->bzjn",
            backward_weight[depth_index],
            grad_shifted[2 - depth_index : 2 - depth_index + depth_cells],
            preferred_element_type=jnp.float32,
        )
        spread = part if spread is None else spread + part
    summed = scatter_channels(spread).reshape(depth_cells, block_in, plane_cells)
    input_grad = jnp.transpose(summed.astype(jnp.bfloat16), (1, 0, 2))
    return (outputs, input_grad, weight_grad, bias_grad)


def solution(mesh):
    space_devices, chan_devices = mesh.shape["space"], mesh.shape["chan"]
    split = Mesh(mesh.devices.reshape(space_devices, chan_devices // 2, 2), ("space", "chips", "core"))
    chan = ("chips", "core")
    placed = (P(chan, "space", None), P(None, None, chan), P(chan), P(chan, "space", None))
    return jax.shard_map(
        body,
        mesh=split,
        in_specs=placed,
        out_specs=(
            P(chan, "space", None),
            P(chan, "space", None),
            P(None, None, chan),
            P(chan),
        ),
        check_vma=False,
    )
```

```python
import math

import jax
import jax.numpy as jnp
from jax import lax
from jax.sharding import Mesh, PartitionSpec as P

W = 64


tap_offsets = tuple(
    (
        (depth_step, row_step, column_step)
        for depth_step in (-1, 0, 1)
        for row_step in (-1, 0, 1)
        for column_step in (-1, 0, 1)
    )
)


def padded_2(array, sides, width):
    for axis, dim in sides:
        devices, length = (lax.axis_size(axis), array.shape[dim])
        up = [(i, (i + 1) % devices) for i in range(devices - 1)]
        down = [(j, i) for i, j in up]
        last = lax.slice_in_dim(array, length - width, length, axis=dim)
        first = lax.slice_in_dim(array, 0, width, axis=dim)
        before = lax.ppermute(last, axis, up)
        after = lax.ppermute(first, axis, down)
        array = jnp.concatenate([before, array, after], axis=dim)
    return array


def shift_cells(field, row_step, column_step):
    length_flat = field.shape[-1]
    pad_width = W + 1
    widths = [(0, 0)] * (field.ndim - 1) + [(pad_width, pad_width)]
    padded = jnp.pad(field, widths)
    first_index = pad_width + row_step * W + column_step
    shifted = lax.slice_in_dim(padded, first_index, first_index + length_flat, axis=field.ndim - 1)
    column = jnp.arange(length_flat, dtype=jnp.int32) % W
    inside = (column + column_step >= 0) & (column + column_step < W)
    return jnp.where(inside, shifted, jnp.zeros_like(shifted))


def outer_planes(field):
    return jnp.concatenate([field[:, :1], field[:, -1:]], axis=1)


def attach_rims(field, rims):
    return jnp.concatenate([rims[:, :1], field, rims[:, 3:]], axis=1)


def all_reduce_rows(block, axis):
    devices = lax.axis_size(axis)
    steps = devices.bit_length() - 1
    assert 1 << steps == devices
    current = block
    index = lax.axis_index(axis)
    for step in range(steps):
        half = current.shape[0] // 2
        bit = (index >> step) & 1
        keep = lax.dynamic_slice_in_dim(current, bit * half, half)
        send = lax.dynamic_slice_in_dim(current, (1 - bit) * half, half)
        pairs = [(i, i ^ (1 << step)) for i in range(devices)]
        current = keep + lax.ppermute(send, axis, pairs)
    for step in reversed(range(steps)):
        half = current.shape[0]
        bit = (index >> step) & 1
        pairs = [(i, i ^ (1 << step)) for i in range(devices)]
        other = lax.ppermute(current, axis, pairs)
        both = jnp.zeros((2 * half,) + current.shape[1:], current.dtype)
        both = lax.dynamic_update_slice_in_dim(both, current, bit * half, 0)
        current = lax.dynamic_update_slice_in_dim(both, other, (1 - bit) * half, 0)
    return current


def shift_volume(field, row_step, column_step, rows):
    length_flat = field.shape[-1]
    pad_width = W + 1
    widths = [(0, 0)] * (field.ndim - 1) + [(pad_width, pad_width)]
    padded = jnp.pad(field, widths)
    first_index = pad_width + row_step * W + column_step
    shifted = lax.slice_in_dim(padded, first_index, first_index + length_flat, axis=field.ndim - 1)
    cell = jnp.arange(length_flat, dtype=jnp.int32)
    column = cell % W
    row = (cell // W) % rows
    inside = (column + column_step >= 0) & (column + column_step < W)
    inside = inside & (row + row_step >= 0) & (row + row_step < rows)
    return jnp.where(inside, shifted, jnp.zeros_like(shifted))


plane_offsets = tuple((row_step, column_step) for row_step in (-1, 0, 1) for column_step in (-1, 0, 1))


def all_reduce_direct(block, axis):
    devices = lax.axis_size(axis)
    index = lax.axis_index(axis)
    chunks = block.reshape((devices, block.shape[0] // devices) + block.shape[1:])
    reduced = lax.dynamic_index_in_dim(chunks, index, 0, keepdims=False)
    for distance in range(1, devices):
        pairs = [(i, i ^ distance) for i in range(devices)]
        send = lax.dynamic_index_in_dim(chunks, index ^ distance, 0, keepdims=False)
        reduced = reduced + lax.ppermute(send, axis, pairs)
    pieces = [reduced] + [
        lax.ppermute(reduced, axis, [(i, i ^ distance) for i in range(devices)])
        for distance in range(1, devices)
    ]
    stacked = jnp.stack(pieces)
    return jnp.concatenate(
        [lax.dynamic_index_in_dim(stacked, index ^ chunk, 0, keepdims=False) for chunk in range(devices)]
    )


def scatter_chips_first(blocks):
    by_chip = blocks.reshape((-1, 2) + blocks.shape[1:])
    pairs = lax.psum_scatter(
        by_chip.reshape(-1, blocks.shape[-1]), "chips", scatter_dimension=0, tiled=True
    ).reshape((2,) + blocks.shape[1:])
    core = lax.axis_index("core")
    keep = lax.dynamic_index_in_dim(pairs, core, 0, keepdims=False)
    send = lax.dynamic_index_in_dim(pairs, 1 - core, 0, keepdims=False)
    return keep + lax.ppermute(send, "core", [(0, 1), (1, 0)])


def scatter_channels(blocks):
    by_core = blocks.reshape((-1, 2) + blocks.shape[1:])
    core = lax.axis_index("core")
    keep = lax.dynamic_index_in_dim(by_core, core, axis=1, keepdims=False)
    send = lax.dynamic_index_in_dim(by_core, 1 - core, axis=1, keepdims=False)
    partial = keep + lax.ppermute(send, "core", [(0, 1), (1, 0)])
    return lax.psum_scatter(
        partial.reshape(-1, blocks.shape[-1]), "chips", scatter_dimension=0, tiled=True
    )


def body(inputs, weight, bias_term, output_grad):
    taps_total = weight.shape[0]
    channels_in = weight.shape[1]
    block_out = weight.shape[2]
    block_in = inputs.shape[0]
    depth_cells = inputs.shape[1]
    plane_cells = inputs.shape[2]
    grad_scale = 1.0 / math.sqrt(lax.axis_size("space") * depth_cells * plane_cells)
    grad_planes = jnp.transpose(output_grad, (1, 0, 2))
    gathered = jnp.transpose(lax.all_gather(inputs, ("chips", "core"), axis=0, tiled=True), (1, 0, 2))

    weight_grid = weight.reshape(3, 9, channels_in, block_out)
    forward_weight = jnp.transpose(weight_grid, (0, 1, 3, 2)).reshape(3, 9 * block_out, channels_in)
    in_plane = None
    for depth_index in range(3):
        part = jnp.einsum(
            "ki,zin->zkn",
            forward_weight[depth_index],
            gathered,
            preferred_element_type=jnp.float32,
        )
        part = jnp.pad(part, ((2 - depth_index, depth_index), (0, 0), (0, 0)))
        in_plane = part if in_plane is None else in_plane + part
    in_plane = in_plane.reshape(depth_cells + 2, 9, block_out, plane_cells)
    forward = None
    for shift_index, (row_step, column_step) in enumerate(plane_offsets):
        term = shift_cells(in_plane[:, shift_index], row_step, column_step)
        forward = term if forward is None else forward + term
    space_devices = lax.axis_size("space")
    up = [(i, i + 1) for i in range(space_devices - 1)]
    down = [(i + 1, i) for i in range(space_devices - 1)]
    from_below = lax.ppermute(forward[depth_cells + 1 :], "space", up)
    from_above = lax.ppermute(forward[:1], "space", down)
    forward = forward[1 : depth_cells + 1] + jnp.concatenate(
        [from_below, jnp.zeros((depth_cells - 2, block_out, plane_cells), jnp.float32), from_above]
    )
    outputs = jnp.transpose(
        (forward + bias_term[None, :, None]).astype(jnp.bfloat16), (1, 0, 2)
    )

    grad_rimmed = padded_2(grad_planes, (("space", 0),), 1)
    grad_shifted = jnp.stack(
        [shift_cells(grad_rimmed, -row_step, -column_step) for row_step, column_step in plane_offsets],
        axis=1,
    ).reshape(depth_cells + 2, 9 * block_out, plane_cells)
    weight_part = jnp.stack(
        [
            jnp.einsum(
                "zkn,zin->ki",
                grad_shifted[2 - depth_index : 2 - depth_index + depth_cells],
                gathered,
                preferred_element_type=jnp.float32,
            )
            for depth_index in range(3)
        ]
    ).reshape(taps_total * block_out, channels_in)
    bias_part = jnp.sum(output_grad.astype(jnp.float32), axis=(1, 2))
    unit = 8 * space_devices
    total_rows = -(-(taps_total * block_out + 1) // unit) * unit
    bias_rows = jnp.zeros((total_rows - taps_total * block_out, channels_in), jnp.float32)
    bias_rows = bias_rows.at[0, :block_out].set(bias_part)
    space_reduce = all_reduce_direct if space_devices <= 4 else all_reduce_rows
    reduced = space_reduce(jnp.concatenate([weight_part, bias_rows]) * grad_scale, "space")
    weight_grad = jnp.transpose(
        reduced[: taps_total * block_out].reshape(taps_total, block_out, channels_in), (0, 2, 1)
    )
    bias_grad = reduced[taps_total * block_out, :block_out]

    chan_devices = lax.axis_size("chips") * lax.axis_size("core")
    backward_weight = jnp.transpose(weight_grid, (0, 2, 1, 3)).reshape(
        3, chan_devices, channels_in // chan_devices, 9 * block_out
    )
    spread = None
    for depth_index in range(3):
        part = jnp.einsum(
            "bjk,zkn->bzjn",
            backward_weight[depth_index],
            grad_shifted[2 - depth_index : 2 - depth_index + depth_cells],
            preferred_element_type=jnp.float32,
        )
        spread = part if spread is None else spread + part
    summed = scatter_chips_first(spread).reshape(depth_cells, block_in, plane_cells)
    input_grad = jnp.transpose(summed.astype(jnp.bfloat16), (1, 0, 2))
    return (outputs, input_grad, weight_grad, bias_grad)


def solution(mesh):
    space_devices, chan_devices = mesh.shape["space"], mesh.shape["chan"]
    split = Mesh(mesh.devices.reshape(space_devices, chan_devices // 2, 2), ("space", "chips", "core"))
    chan = ("chips", "core")
    placed = (P(chan, "space", None), P(None, None, chan), P(chan), P(chan, "space", None))
    return jax.shard_map(
        body,
        mesh=split,
        in_specs=placed,
        out_specs=(
            P(chan, "space", None),
            P(chan, "space", None),
            P(None, None, chan),
            P(chan),
        ),
        check_vma=False,
    )
```

```python
import math

import jax
import jax.numpy as jnp
from jax import lax
from jax.sharding import Mesh, PartitionSpec as P

W = 64


tap_offsets = tuple(
    (
        (depth_step, row_step, column_step)
        for depth_step in (-1, 0, 1)
        for row_step in (-1, 0, 1)
        for column_step in (-1, 0, 1)
    )
)


def padded_2(array, sides, width):
    for axis, dim in sides:
        devices, length = (lax.axis_size(axis), array.shape[dim])
        up = [(i, (i + 1) % devices) for i in range(devices - 1)]
        down = [(j, i) for i, j in up]
        last = lax.slice_in_dim(array, length - width, length, axis=dim)
        first = lax.slice_in_dim(array, 0, width, axis=dim)
        before = lax.ppermute(last, axis, up)
        after = lax.ppermute(first, axis, down)
        array = jnp.concatenate([before, array, after], axis=dim)
    return array


def shift_cells(field, row_step, column_step):
    length_flat = field.shape[-1]
    pad_width = W + 1
    widths = [(0, 0)] * (field.ndim - 1) + [(pad_width, pad_width)]
    padded = jnp.pad(field, widths)
    first_index = pad_width + row_step * W + column_step
    shifted = lax.slice_in_dim(padded, first_index, first_index + length_flat, axis=field.ndim - 1)
    column = jnp.arange(length_flat, dtype=jnp.int32) % W
    inside = (column + column_step >= 0) & (column + column_step < W)
    return jnp.where(inside, shifted, jnp.zeros_like(shifted))


def outer_planes(field):
    return jnp.concatenate([field[:, :1], field[:, -1:]], axis=1)


def attach_rims(field, rims):
    return jnp.concatenate([rims[:, :1], field, rims[:, 3:]], axis=1)


def all_reduce_rows(block, axis):
    devices = lax.axis_size(axis)
    steps = devices.bit_length() - 1
    assert 1 << steps == devices
    current = block
    index = lax.axis_index(axis)
    for step in range(steps):
        half = current.shape[0] // 2
        bit = (index >> step) & 1
        keep = lax.dynamic_slice_in_dim(current, bit * half, half)
        send = lax.dynamic_slice_in_dim(current, (1 - bit) * half, half)
        pairs = [(i, i ^ (1 << step)) for i in range(devices)]
        current = keep + lax.ppermute(send, axis, pairs)
    for step in reversed(range(steps)):
        half = current.shape[0]
        bit = (index >> step) & 1
        pairs = [(i, i ^ (1 << step)) for i in range(devices)]
        other = lax.ppermute(current, axis, pairs)
        both = jnp.zeros((2 * half,) + current.shape[1:], current.dtype)
        both = lax.dynamic_update_slice_in_dim(both, current, bit * half, 0)
        current = lax.dynamic_update_slice_in_dim(both, other, (1 - bit) * half, 0)
    return current


def shift_volume(field, row_step, column_step, rows):
    length_flat = field.shape[-1]
    pad_width = W + 1
    widths = [(0, 0)] * (field.ndim - 1) + [(pad_width, pad_width)]
    padded = jnp.pad(field, widths)
    first_index = pad_width + row_step * W + column_step
    shifted = lax.slice_in_dim(padded, first_index, first_index + length_flat, axis=field.ndim - 1)
    cell = jnp.arange(length_flat, dtype=jnp.int32)
    column = cell % W
    row = (cell // W) % rows
    inside = (column + column_step >= 0) & (column + column_step < W)
    inside = inside & (row + row_step >= 0) & (row + row_step < rows)
    return jnp.where(inside, shifted, jnp.zeros_like(shifted))


plane_offsets = tuple((row_step, column_step) for row_step in (-1, 0, 1) for column_step in (-1, 0, 1))


def all_reduce_direct(block, axis):
    devices = lax.axis_size(axis)
    index = lax.axis_index(axis)
    chunks = block.reshape((devices, block.shape[0] // devices) + block.shape[1:])
    reduced = lax.dynamic_index_in_dim(chunks, index, 0, keepdims=False)
    for distance in range(1, devices):
        pairs = [(i, i ^ distance) for i in range(devices)]
        send = lax.dynamic_index_in_dim(chunks, index ^ distance, 0, keepdims=False)
        reduced = reduced + lax.ppermute(send, axis, pairs)
    pieces = [reduced] + [
        lax.ppermute(reduced, axis, [(i, i ^ distance) for i in range(devices)])
        for distance in range(1, devices)
    ]
    stacked = jnp.stack(pieces)
    return jnp.concatenate(
        [lax.dynamic_index_in_dim(stacked, index ^ chunk, 0, keepdims=False) for chunk in range(devices)]
    )


def scatter_channels(blocks):
    by_core = blocks.reshape((-1, 2) + blocks.shape[1:])
    core = lax.axis_index("core")
    keep = lax.dynamic_index_in_dim(by_core, core, axis=1, keepdims=False)
    send = lax.dynamic_index_in_dim(by_core, 1 - core, axis=1, keepdims=False)
    partial = keep + lax.ppermute(send, "core", [(0, 1), (1, 0)])
    return lax.psum_scatter(
        partial.reshape(-1, blocks.shape[-1]), "chips", scatter_dimension=0, tiled=True
    )


def body(inputs, weight, bias_term, output_grad):
    taps_total = weight.shape[0]
    channels_in = weight.shape[1]
    block_out = weight.shape[2]
    block_in = inputs.shape[0]
    depth_cells = inputs.shape[1]
    plane_cells = inputs.shape[2]
    grad_scale = 1.0 / math.sqrt(lax.axis_size("space") * depth_cells * plane_cells)
    grad_planes = jnp.transpose(output_grad, (1, 0, 2))
    gathered = jnp.transpose(lax.all_gather(inputs, ("chips", "core"), axis=0, tiled=True), (1, 0, 2))

    weight_grid = weight.reshape(3, 9, channels_in, block_out)
    forward_weight = jnp.transpose(weight_grid, (0, 1, 3, 2)).reshape(3, 9 * block_out, channels_in)
    in_plane = None
    for depth_index in range(3):
        part = jnp.einsum(
            "ki,zin->zkn",
            forward_weight[depth_index],
            gathered,
            preferred_element_type=jnp.float32,
        )
        part = jnp.pad(part, ((2 - depth_index, depth_index), (0, 0), (0, 0)))
        in_plane = part if in_plane is None else in_plane + part
    in_plane = in_plane.reshape(depth_cells + 2, 9, block_out, plane_cells)
    forward = None
    for shift_index, (row_step, column_step) in enumerate(plane_offsets):
        term = shift_cells(in_plane[:, shift_index], row_step, column_step)
        forward = term if forward is None else forward + term
    space_devices = lax.axis_size("space")
    up = [(i, i + 1) for i in range(space_devices - 1)]
    down = [(i + 1, i) for i in range(space_devices - 1)]
    from_below = lax.ppermute(forward[depth_cells + 1 :], "space", up)
    from_above = lax.ppermute(forward[:1], "space", down)
    forward = forward[1 : depth_cells + 1] + jnp.concatenate(
        [from_below, jnp.zeros((depth_cells - 2, block_out, plane_cells), jnp.float32), from_above]
    )
    outputs = jnp.transpose(
        (forward + bias_term[None, :, None]).astype(jnp.bfloat16), (1, 0, 2)
    )

    grad_rimmed = padded_2(grad_planes, (("space", 0),), 1)
    grad_shifted = jnp.stack(
        [shift_cells(grad_rimmed, -row_step, -column_step) for row_step, column_step in plane_offsets],
        axis=1,
    ).reshape(depth_cells + 2, 9 * block_out, plane_cells)
    weight_part = jnp.stack(
        [
            jnp.einsum(
                "zkn,zin->ki",
                grad_shifted[2 - depth_index : 2 - depth_index + depth_cells],
                gathered,
                preferred_element_type=jnp.float32,
            )
            for depth_index in range(3)
        ]
    ).reshape(taps_total * block_out, channels_in)
    bias_part = jnp.sum(output_grad.astype(jnp.float32), axis=(1, 2))
    unit = 8 * space_devices
    total_rows = -(-(taps_total * block_out + 1) // unit) * unit
    bias_rows = jnp.zeros((total_rows - taps_total * block_out, channels_in), jnp.float32)
    bias_rows = bias_rows.at[0, :block_out].set(bias_part)
    space_reduce = all_reduce_direct if space_devices <= 4 else all_reduce_rows
    reduced = space_reduce(jnp.concatenate([weight_part, bias_rows]) * grad_scale, "space")
    weight_grad = jnp.transpose(
        reduced[: taps_total * block_out].reshape(taps_total, block_out, channels_in), (0, 2, 1)
    )
    bias_grad = reduced[taps_total * block_out, :block_out]

    chan_devices = lax.axis_size("chips") * lax.axis_size("core")
    backward_weight = jnp.transpose(weight_grid, (0, 2, 1, 3)).reshape(
        3, chan_devices // 2, 2, channels_in // chan_devices, 9 * block_out
    )
    core = lax.axis_index("core")

    def partial_sums(core_weight, total):
        for depth_index in range(3):
            part = jnp.einsum(
                "cjk,zkn->czjn",
                core_weight[depth_index],
                grad_shifted[2 - depth_index : 2 - depth_index + depth_cells],
                preferred_element_type=jnp.float32,
            )
            total = part if total is None else total + part
        return total

    sent = partial_sums(lax.dynamic_index_in_dim(backward_weight, 1 - core, axis=2, keepdims=False), None)
    received = lax.ppermute(sent, "core", [(0, 1), (1, 0)])
    spread = partial_sums(lax.dynamic_index_in_dim(backward_weight, core, axis=2, keepdims=False), received)
    summed = lax.psum_scatter(
        spread.reshape(-1, plane_cells), "chips", scatter_dimension=0, tiled=True
    ).reshape(depth_cells, block_in, plane_cells)
    input_grad = jnp.transpose(summed.astype(jnp.bfloat16), (1, 0, 2))
    return (outputs, input_grad, weight_grad, bias_grad)


def solution(mesh):
    space_devices, chan_devices = mesh.shape["space"], mesh.shape["chan"]
    split = Mesh(mesh.devices.reshape(space_devices, chan_devices // 2, 2), ("space", "chips", "core"))
    chan = ("chips", "core")
    placed = (P(chan, "space", None), P(None, None, chan), P(chan), P(chan, "space", None))
    return jax.shard_map(
        body,
        mesh=split,
        in_specs=placed,
        out_specs=(
            P(chan, "space", None),
            P(chan, "space", None),
            P(None, None, chan),
            P(chan),
        ),
        check_vma=False,
    )
```

```python
import math

import jax
import jax.numpy as jnp
from jax import lax
from jax.sharding import Mesh, PartitionSpec as P

W = 64


tap_offsets = tuple(
    (
        (depth_step, row_step, column_step)
        for depth_step in (-1, 0, 1)
        for row_step in (-1, 0, 1)
        for column_step in (-1, 0, 1)
    )
)


def padded_2(array, sides, width):
    for axis, dim in sides:
        devices, length = (lax.axis_size(axis), array.shape[dim])
        up = [(i, (i + 1) % devices) for i in range(devices - 1)]
        down = [(j, i) for i, j in up]
        last = lax.slice_in_dim(array, length - width, length, axis=dim)
        first = lax.slice_in_dim(array, 0, width, axis=dim)
        before = lax.ppermute(last, axis, up)
        after = lax.ppermute(first, axis, down)
        array = jnp.concatenate([before, array, after], axis=dim)
    return array


def shift_cells(field, row_step, column_step):
    length_flat = field.shape[-1]
    pad_width = W + 1
    widths = [(0, 0)] * (field.ndim - 1) + [(pad_width, pad_width)]
    padded = jnp.pad(field, widths)
    first_index = pad_width + row_step * W + column_step
    shifted = lax.slice_in_dim(padded, first_index, first_index + length_flat, axis=field.ndim - 1)
    column = jnp.arange(length_flat, dtype=jnp.int32) % W
    inside = (column + column_step >= 0) & (column + column_step < W)
    return jnp.where(inside, shifted, jnp.zeros_like(shifted))


def outer_planes(field):
    return jnp.concatenate([field[:, :1], field[:, -1:]], axis=1)


def attach_rims(field, rims):
    return jnp.concatenate([rims[:, :1], field, rims[:, 3:]], axis=1)


def all_reduce_rows(block, axis):
    devices = lax.axis_size(axis)
    steps = devices.bit_length() - 1
    assert 1 << steps == devices
    current = block
    index = lax.axis_index(axis)
    for step in range(steps):
        half = current.shape[0] // 2
        bit = (index >> step) & 1
        keep = lax.dynamic_slice_in_dim(current, bit * half, half)
        send = lax.dynamic_slice_in_dim(current, (1 - bit) * half, half)
        pairs = [(i, i ^ (1 << step)) for i in range(devices)]
        current = keep + lax.ppermute(send, axis, pairs)
    for step in reversed(range(steps)):
        half = current.shape[0]
        bit = (index >> step) & 1
        pairs = [(i, i ^ (1 << step)) for i in range(devices)]
        other = lax.ppermute(current, axis, pairs)
        both = jnp.zeros((2 * half,) + current.shape[1:], current.dtype)
        both = lax.dynamic_update_slice_in_dim(both, current, bit * half, 0)
        current = lax.dynamic_update_slice_in_dim(both, other, (1 - bit) * half, 0)
    return current


def shift_volume(field, row_step, column_step, rows):
    length_flat = field.shape[-1]
    pad_width = W + 1
    widths = [(0, 0)] * (field.ndim - 1) + [(pad_width, pad_width)]
    padded = jnp.pad(field, widths)
    first_index = pad_width + row_step * W + column_step
    shifted = lax.slice_in_dim(padded, first_index, first_index + length_flat, axis=field.ndim - 1)
    cell = jnp.arange(length_flat, dtype=jnp.int32)
    column = cell % W
    row = (cell // W) % rows
    inside = (column + column_step >= 0) & (column + column_step < W)
    inside = inside & (row + row_step >= 0) & (row + row_step < rows)
    return jnp.where(inside, shifted, jnp.zeros_like(shifted))


plane_offsets = tuple((row_step, column_step) for row_step in (-1, 0, 1) for column_step in (-1, 0, 1))


def all_reduce_direct(block, axis):
    devices = lax.axis_size(axis)
    index = lax.axis_index(axis)
    chunks = block.reshape((devices, block.shape[0] // devices) + block.shape[1:])
    reduced = lax.dynamic_index_in_dim(chunks, index, 0, keepdims=False)
    for distance in range(1, devices):
        pairs = [(i, i ^ distance) for i in range(devices)]
        send = lax.dynamic_index_in_dim(chunks, index ^ distance, 0, keepdims=False)
        reduced = reduced + lax.ppermute(send, axis, pairs)
    pieces = [reduced] + [
        lax.ppermute(reduced, axis, [(i, i ^ distance) for i in range(devices)])
        for distance in range(1, devices)
    ]
    stacked = jnp.stack(pieces)
    return jnp.concatenate(
        [lax.dynamic_index_in_dim(stacked, index ^ chunk, 0, keepdims=False) for chunk in range(devices)]
    )


def scatter_channels(blocks):
    by_core = blocks.reshape((-1, 2) + blocks.shape[1:])
    core = lax.axis_index("core")
    keep = lax.dynamic_index_in_dim(by_core, core, axis=1, keepdims=False)
    send = lax.dynamic_index_in_dim(by_core, 1 - core, axis=1, keepdims=False)
    partial = keep + lax.ppermute(send, "core", [(0, 1), (1, 0)])
    return lax.psum_scatter(
        partial.reshape(-1, blocks.shape[-1]), "chips", scatter_dimension=0, tiled=True
    )


def body(inputs, weight, bias_term, output_grad):
    taps_total = weight.shape[0]
    channels_in = weight.shape[1]
    block_out = weight.shape[2]
    block_in = inputs.shape[0]
    depth_cells = inputs.shape[1]
    plane_cells = inputs.shape[2]
    grad_scale = 1.0 / math.sqrt(lax.axis_size("space") * depth_cells * plane_cells)
    grad_planes = jnp.transpose(output_grad, (1, 0, 2))
    gathered = jnp.transpose(lax.all_gather(inputs, ("chips", "core"), axis=0, tiled=True), (1, 0, 2))

    weight_grid = weight.reshape(3, 9, channels_in, block_out)
    forward_weight = jnp.transpose(weight_grid, (0, 1, 3, 2)).reshape(3, 9 * block_out, channels_in)
    in_plane = None
    for depth_index in range(3):
        part = jnp.einsum(
            "ki,zin->zkn",
            forward_weight[depth_index],
            gathered,
            preferred_element_type=jnp.float32,
        )
        part = jnp.pad(part, ((2 - depth_index, depth_index), (0, 0), (0, 0)))
        in_plane = part if in_plane is None else in_plane + part
    in_plane = in_plane.reshape(depth_cells + 2, 9, block_out, plane_cells)
    forward = None
    for shift_index, (row_step, column_step) in enumerate(plane_offsets):
        term = shift_cells(in_plane[:, shift_index], row_step, column_step)
        forward = term if forward is None else forward + term
    space_devices = lax.axis_size("space")
    up = [(i, i + 1) for i in range(space_devices - 1)]
    down = [(i + 1, i) for i in range(space_devices - 1)]
    from_below = lax.ppermute(forward[depth_cells + 1 :], "space", up)
    from_above = lax.ppermute(forward[:1], "space", down)
    forward = forward[1 : depth_cells + 1] + jnp.concatenate(
        [from_below, jnp.zeros((depth_cells - 2, block_out, plane_cells), jnp.float32), from_above]
    )
    outputs = jnp.transpose(
        (forward + bias_term[None, :, None]).astype(jnp.bfloat16), (1, 0, 2)
    )

    grad_rimmed = padded_2(grad_planes, (("space", 0),), 1)
    grad_shifted = jnp.stack(
        [shift_cells(grad_rimmed, -row_step, -column_step) for row_step, column_step in plane_offsets],
        axis=1,
    ).reshape(depth_cells + 2, 9 * block_out, plane_cells)
    weight_part = jnp.stack(
        [
            jnp.einsum(
                "zkn,zin->ki",
                grad_shifted[2 - depth_index : 2 - depth_index + depth_cells],
                gathered,
                preferred_element_type=jnp.float32,
            )
            for depth_index in range(3)
        ]
    ).reshape(taps_total * block_out, channels_in)
    bias_part = jnp.sum(output_grad.astype(jnp.float32), axis=(1, 2))
    unit = 8 * space_devices
    total_rows = -(-(taps_total * block_out + 1) // unit) * unit
    bias_rows = jnp.zeros((total_rows - taps_total * block_out, channels_in), jnp.float32)
    bias_rows = bias_rows.at[0, :block_out].set(bias_part)
    space_reduce = all_reduce_direct if space_devices <= 4 else all_reduce_rows
    reduced = space_reduce(jnp.concatenate([weight_part, bias_rows]) * grad_scale, "space")
    weight_grad = jnp.transpose(
        reduced[: taps_total * block_out].reshape(taps_total, block_out, channels_in), (0, 2, 1)
    )
    bias_grad = reduced[taps_total * block_out, :block_out]

    chan_devices = lax.axis_size("chips") * lax.axis_size("core")
    backward_weight = weight.reshape(3, 9, chan_devices, channels_in // chan_devices, block_out)
    spread = None
    for depth_index in range(3):
        part = jnp.einsum(
            "sbjo,zson->bzjn",
            backward_weight[depth_index],
            grad_shifted[2 - depth_index : 2 - depth_index + depth_cells].reshape(
                depth_cells, 9, block_out, plane_cells
            ),
            preferred_element_type=jnp.float32,
        )
        spread = part if spread is None else spread + part
    summed = scatter_channels(spread).reshape(depth_cells, block_in, plane_cells)
    input_grad = jnp.transpose(summed.astype(jnp.bfloat16), (1, 0, 2))
    return (outputs, input_grad, weight_grad, bias_grad)


def solution(mesh):
    space_devices, chan_devices = mesh.shape["space"], mesh.shape["chan"]
    split = Mesh(mesh.devices.reshape(space_devices, chan_devices // 2, 2), ("space", "chips", "core"))
    chan = ("chips", "core")
    placed = (P(chan, "space", None), P(None, None, chan), P(chan), P(chan, "space", None))
    return jax.shard_map(
        body,
        mesh=split,
        in_specs=placed,
        out_specs=(
            P(chan, "space", None),
            P(chan, "space", None),
            P(None, None, chan),
            P(chan),
        ),
        check_vma=False,
    )
```

```python
import math

import jax
import jax.numpy as jnp
from jax import lax
from jax.sharding import Mesh, PartitionSpec as P

W = 64


tap_offsets = tuple(
    (
        (depth_step, row_step, column_step)
        for depth_step in (-1, 0, 1)
        for row_step in (-1, 0, 1)
        for column_step in (-1, 0, 1)
    )
)


def padded_2(array, sides, width):
    for axis, dim in sides:
        devices, length = (lax.axis_size(axis), array.shape[dim])
        up = [(i, (i + 1) % devices) for i in range(devices - 1)]
        down = [(j, i) for i, j in up]
        last = lax.slice_in_dim(array, length - width, length, axis=dim)
        first = lax.slice_in_dim(array, 0, width, axis=dim)
        before = lax.ppermute(last, axis, up)
        after = lax.ppermute(first, axis, down)
        array = jnp.concatenate([before, array, after], axis=dim)
    return array


def shift_cells(field, row_step, column_step):
    length_flat = field.shape[-1]
    pad_width = W + 1
    widths = [(0, 0)] * (field.ndim - 1) + [(pad_width, pad_width)]
    padded = jnp.pad(field, widths)
    first_index = pad_width + row_step * W + column_step
    shifted = lax.slice_in_dim(padded, first_index, first_index + length_flat, axis=field.ndim - 1)
    column = jnp.arange(length_flat, dtype=jnp.int32) % W
    inside = (column + column_step >= 0) & (column + column_step < W)
    return jnp.where(inside, shifted, jnp.zeros_like(shifted))


def outer_planes(field):
    return jnp.concatenate([field[:, :1], field[:, -1:]], axis=1)


def attach_rims(field, rims):
    return jnp.concatenate([rims[:, :1], field, rims[:, 3:]], axis=1)


def all_reduce_rows(block, axis):
    devices = lax.axis_size(axis)
    steps = devices.bit_length() - 1
    assert 1 << steps == devices
    current = block
    index = lax.axis_index(axis)
    for step in range(steps):
        half = current.shape[0] // 2
        bit = (index >> step) & 1
        keep = lax.dynamic_slice_in_dim(current, bit * half, half)
        send = lax.dynamic_slice_in_dim(current, (1 - bit) * half, half)
        pairs = [(i, i ^ (1 << step)) for i in range(devices)]
        current = keep + lax.ppermute(send, axis, pairs)
    for step in reversed(range(steps)):
        half = current.shape[0]
        bit = (index >> step) & 1
        pairs = [(i, i ^ (1 << step)) for i in range(devices)]
        other = lax.ppermute(current, axis, pairs)
        both = jnp.zeros((2 * half,) + current.shape[1:], current.dtype)
        both = lax.dynamic_update_slice_in_dim(both, current, bit * half, 0)
        current = lax.dynamic_update_slice_in_dim(both, other, (1 - bit) * half, 0)
    return current


def shift_volume(field, row_step, column_step, rows):
    length_flat = field.shape[-1]
    pad_width = W + 1
    widths = [(0, 0)] * (field.ndim - 1) + [(pad_width, pad_width)]
    padded = jnp.pad(field, widths)
    first_index = pad_width + row_step * W + column_step
    shifted = lax.slice_in_dim(padded, first_index, first_index + length_flat, axis=field.ndim - 1)
    cell = jnp.arange(length_flat, dtype=jnp.int32)
    column = cell % W
    row = (cell // W) % rows
    inside = (column + column_step >= 0) & (column + column_step < W)
    inside = inside & (row + row_step >= 0) & (row + row_step < rows)
    return jnp.where(inside, shifted, jnp.zeros_like(shifted))


plane_offsets = tuple((row_step, column_step) for row_step in (-1, 0, 1) for column_step in (-1, 0, 1))


def all_reduce_direct(block, axis):
    devices = lax.axis_size(axis)
    index = lax.axis_index(axis)
    chunks = block.reshape((devices, block.shape[0] // devices) + block.shape[1:])
    reduced = lax.dynamic_index_in_dim(chunks, index, 0, keepdims=False)
    for distance in range(1, devices):
        pairs = [(i, i ^ distance) for i in range(devices)]
        send = lax.dynamic_index_in_dim(chunks, index ^ distance, 0, keepdims=False)
        reduced = reduced + lax.ppermute(send, axis, pairs)
    pieces = [reduced] + [
        lax.ppermute(reduced, axis, [(i, i ^ distance) for i in range(devices)])
        for distance in range(1, devices)
    ]
    stacked = jnp.stack(pieces)
    return jnp.concatenate(
        [lax.dynamic_index_in_dim(stacked, index ^ chunk, 0, keepdims=False) for chunk in range(devices)]
    )


def scatter_channels(blocks):
    by_core = blocks.reshape((-1, 2) + blocks.shape[1:])
    core = lax.axis_index("core")
    keep = lax.dynamic_index_in_dim(by_core, core, axis=1, keepdims=False)
    send = lax.dynamic_index_in_dim(by_core, 1 - core, axis=1, keepdims=False)
    partial = keep + lax.ppermute(send, "core", [(0, 1), (1, 0)])
    return lax.psum_scatter(
        partial.reshape(-1, blocks.shape[-1]), "chips", scatter_dimension=0, tiled=True
    )


def body(inputs, weight, bias_term, output_grad):
    taps_total = weight.shape[0]
    channels_in = weight.shape[1]
    block_out = weight.shape[2]
    block_in = inputs.shape[0]
    depth_cells = inputs.shape[1]
    plane_cells = inputs.shape[2]
    grad_scale = 1.0 / math.sqrt(lax.axis_size("space") * depth_cells * plane_cells)
    grad_planes = jnp.transpose(output_grad, (1, 0, 2))
    gathered = jnp.transpose(lax.all_gather(inputs, ("chips", "core"), axis=0, tiled=True), (1, 0, 2))

    weight_grid = weight.reshape(3, 9, channels_in, block_out)
    forward_weight = jnp.transpose(weight_grid, (0, 1, 3, 2)).reshape(3, 9 * block_out, channels_in)
    in_plane = None
    for depth_index in range(3):
        part = jnp.einsum(
            "ki,zin->zkn",
            forward_weight[depth_index],
            gathered,
            preferred_element_type=jnp.float32,
        )
        part = jnp.pad(part, ((2 - depth_index, depth_index), (0, 0), (0, 0)))
        in_plane = part if in_plane is None else in_plane + part
    in_plane = in_plane.reshape(depth_cells + 2, 9, block_out, plane_cells)
    forward = None
    for shift_index, (row_step, column_step) in enumerate(plane_offsets):
        term = shift_cells(in_plane[:, shift_index], row_step, column_step)
        forward = term if forward is None else forward + term
    space_devices = lax.axis_size("space")
    up = [(i, i + 1) for i in range(space_devices - 1)]
    down = [(i + 1, i) for i in range(space_devices - 1)]
    from_below = lax.ppermute(forward[depth_cells + 1 :], "space", up)
    from_above = lax.ppermute(forward[:1], "space", down)
    forward = forward[1 : depth_cells + 1] + jnp.concatenate(
        [from_below, jnp.zeros((depth_cells - 2, block_out, plane_cells), jnp.float32), from_above]
    )
    outputs = jnp.transpose(
        (forward + bias_term[None, :, None]).astype(jnp.bfloat16), (1, 0, 2)
    )

    grad_rimmed = padded_2(grad_planes, (("space", 0),), 1)

    def shifted_planes(planes):
        return jnp.stack(
            [shift_cells(planes, -row_step, -column_step) for row_step, column_step in plane_offsets], axis=1
        ).reshape(planes.shape[0], 9 * block_out, plane_cells)

    grad_shifted = jnp.concatenate(
        [
            shifted_planes(grad_rimmed[:1]),
            shifted_planes(grad_planes),
            shifted_planes(grad_rimmed[depth_cells + 1 :]),
        ]
    )
    weight_part = jnp.stack(
        [
            jnp.einsum(
                "zkn,zin->ki",
                grad_shifted[2 - depth_index : 2 - depth_index + depth_cells],
                gathered,
                preferred_element_type=jnp.float32,
            )
            for depth_index in range(3)
        ]
    ).reshape(taps_total * block_out, channels_in)
    bias_part = jnp.sum(output_grad.astype(jnp.float32), axis=(1, 2))
    unit = 8 * space_devices
    total_rows = -(-(taps_total * block_out + 1) // unit) * unit
    bias_rows = jnp.zeros((total_rows - taps_total * block_out, channels_in), jnp.float32)
    bias_rows = bias_rows.at[0, :block_out].set(bias_part)
    space_reduce = all_reduce_direct if space_devices <= 4 else all_reduce_rows
    reduced = space_reduce(jnp.concatenate([weight_part, bias_rows]) * grad_scale, "space")
    weight_grad = jnp.transpose(
        reduced[: taps_total * block_out].reshape(taps_total, block_out, channels_in), (0, 2, 1)
    )
    bias_grad = reduced[taps_total * block_out, :block_out]

    chan_devices = lax.axis_size("chips") * lax.axis_size("core")
    backward_weight = jnp.transpose(weight_grid, (0, 2, 1, 3)).reshape(
        3, chan_devices, channels_in // chan_devices, 9 * block_out
    )
    spread = None
    for depth_index in range(3):
        part = jnp.einsum(
            "bjk,zkn->bzjn",
            backward_weight[depth_index],
            grad_shifted[2 - depth_index : 2 - depth_index + depth_cells],
            preferred_element_type=jnp.float32,
        )
        spread = part if spread is None else spread + part
    summed = scatter_channels(spread).reshape(depth_cells, block_in, plane_cells)
    input_grad = jnp.transpose(summed.astype(jnp.bfloat16), (1, 0, 2))
    return (outputs, input_grad, weight_grad, bias_grad)


def solution(mesh):
    space_devices, chan_devices = mesh.shape["space"], mesh.shape["chan"]
    split = Mesh(mesh.devices.reshape(space_devices, chan_devices // 2, 2), ("space", "chips", "core"))
    chan = ("chips", "core")
    placed = (P(chan, "space", None), P(None, None, chan), P(chan), P(chan, "space", None))
    return jax.shard_map(
        body,
        mesh=split,
        in_specs=placed,
        out_specs=(
            P(chan, "space", None),
            P(chan, "space", None),
            P(None, None, chan),
            P(chan),
        ),
        check_vma=False,
    )
```
